128 devices in a mesh: section: 4 (over x), seq: 32 (over z, y, core).
Axes of the slice: x: 4, y: 4, z: 4, core: 2. Of those that a mesh axis runs over, the one named last changes fastest.
Arguments:
- section_inputs: bfloat16 [4, 2, 16384, 256], P('section', None, 'seq'), may hold values from -6 to 6
- cotangent: bfloat16 [2, 16384, 256], P(None, 'seq'), may hold values from -6 to 6
- conv_weight: bfloat16 [4, 2, 3, 256, 512], P('section'), may hold values from -0.21875 to 0.21875
- out_weight: bfloat16 [4, 2, 256, 256], P('section'), may hold values from -0.375 to 0.375
Outputs:
- input_grads: float32 [4, 2, 16384, 256], P('section', None, 'seq')
- conv_grads: float32 [4, 2, 768, 512], P('section', None, 'seq')
- out_grads: float32 [4, 2, 256, 256], P('section', None, 'seq')
The draws below stay inside these ranges and needn't reach their ends.
All inputs are finite; a program needn't handle non-finite values.
Results may differ from the reference program's by a relative error of at most 0.019.
Values may be sent and summed in bfloat16 or wider, within the bound.
No kernel may reach another device: no remote copies, remote signals or barrier semaphores. Data moves between devices by JAX's collectives and lax.ppermute only.
A program may use at most 128 MiB of HBM per device.

```python
import math
import jax
import jax.numpy as jnp
from jax import lax

C = 256
LAYERS = 2
MICRO = 2
SECTIONS = 4
WINDOW = 16384
NEAR = 128
FAR = 1024


def shard_levels(rng, dims, split, low, top_value):
    factor_of, own = 1.0, jax.random.fold_in(rng, 6)
    for dim, shards_of in split:
        heights = jnp.exp(jax.random.uniform(jax.random.fold_in(own, dim), (shards_of,), jnp.float32, low / len(split), top_value / len(split)))
        factor_of = factor_of * jnp.repeat(heights, dims[dim] // shards_of).reshape([-1 if axis == dim else 1 for axis in range(len(dims))])
    return factor_of


def centred(rng, dims, scale, limit, cuts=(), held_as=jnp.bfloat16):
    loudness = shard_levels(rng, dims, cuts, -0.22, 0.18) if cuts else 1.0
    entries = jax.random.normal(rng, dims, jnp.float32) * scale * loudness
    return jnp.minimum(jnp.maximum(entries, -limit), limit).astype(held_as)


def setup_inputs(seed: int = 0) -> dict:
    keys = jax.random.split(jax.random.key(seed), 5)
    return {
        "section_inputs": centred(keys[0], (SECTIONS, MICRO, WINDOW, C), 1.0, 6.0, ((0, 4), (2, 32))),
        "cotangent": centred(keys[1], (MICRO, WINDOW, C), 1.0, 6.0, ((1, 32),)),
        "conv_weight": centred(keys[2], (SECTIONS, LAYERS, 3, C, 2 * C), (3 * C) ** -0.5, 0.21875, ((0, 4),)),
        "out_weight": centred(keys[3], (SECTIONS, LAYERS, C, C), C ** -0.5, 0.375, ((0, 4),)),
    }


def shifted(field, dilation):
    padding = jnp.zeros((dilation, field.shape[1]), field.dtype)
    earlier = jnp.concatenate([padding, field[:-dilation]], axis=0)
    following = jnp.concatenate([field[dilation:], padding], axis=0)
    return (earlier, following)

def layer_forward(hidden, conv_mat, out_mat, dilation):
    earlier, following = shifted(hidden, dilation)
    preact = jnp.dot(earlier, conv_mat[0], preferred_element_type=jnp.float32)
    preact = preact + jnp.dot(hidden, conv_mat[1], preferred_element_type=jnp.float32)
    preact = preact + jnp.dot(following, conv_mat[2], preferred_element_type=jnp.float32)
    chans = hidden.shape[1]
    gated = (jnp.tanh(preact[:, :chans]) * jax.nn.sigmoid(preact[:, chans:])).astype(jnp.bfloat16)
    output = (hidden.astype(jnp.float32) + jnp.dot(gated, out_mat, preferred_element_type=jnp.float32)).astype(jnp.bfloat16)
    return (output, (earlier, hidden, following, preact, gated))

def layer_backward(flowing, stored, conv_mat, out_mat, dilation):
    earlier, hidden, following, preact, gated = stored
    chans = hidden.shape[1]
    grad_half = flowing.astype(jnp.bfloat16)
    out_term = jnp.dot(gated.T, grad_half, preferred_element_type=jnp.float32)
    grad_gated = jnp.dot(grad_half, out_mat.T, preferred_element_type=jnp.float32)
    tanh_part = jnp.tanh(preact[:, :chans])
    sig_part = jax.nn.sigmoid(preact[:, chans:])
    grad_pre = jnp.concatenate([grad_gated * (1.0 - tanh_part * tanh_part) * sig_part, grad_gated * tanh_part * sig_part * (1.0 - sig_part)], axis=1).astype(jnp.bfloat16)
    conv_term = jnp.stack([jnp.dot(earlier.T, grad_pre, preferred_element_type=jnp.float32), jnp.dot(hidden.T, grad_pre, preferred_element_type=jnp.float32), jnp.dot(following.T, grad_pre, preferred_element_type=jnp.float32)])
    grad_first = jnp.dot(grad_pre, conv_mat[0].T, preferred_element_type=jnp.float32).astype(jnp.bfloat16)
    grad_third = jnp.dot(grad_pre, conv_mat[2].T, preferred_element_type=jnp.float32).astype(jnp.bfloat16)
    grad_first = lax.optimization_barrier(grad_first)
    grad_third = lax.optimization_barrier(grad_third)
    unused_low, first_following = shifted(grad_first, dilation)
    third_earlier, unused_high = shifted(grad_third, dilation)
    grad_conv = jnp.dot(grad_pre, conv_mat[1].T, preferred_element_type=jnp.float32)
    grad_conv = grad_conv + first_following.astype(jnp.float32) + third_earlier.astype(jnp.float32)
    return (flowing + grad_conv, conv_term, out_term)

def reference(section_inputs, cotangent, conv_weight, out_weight):
    dilations = [NEAR, FAR]
    grad_scale = 1.0 / math.sqrt(MICRO * WINDOW)
    carried = [cotangent[batch_index].astype(jnp.float32) for batch_index in range(MICRO)]
    input_rows = [None] * SECTIONS
    conv_rows = [None] * SECTIONS
    out_rows = [None] * SECTIONS
    for section_index in reversed(range(SECTIONS)):
        conv_total = jnp.zeros((LAYERS, 3, C, 2 * C), jnp.float32)
        out_total = jnp.zeros((LAYERS, C, C), jnp.float32)
        per_batch = []
        for batch_index in range(MICRO):
            hidden = section_inputs[section_index, batch_index]
            stored = []
            for layer in range(LAYERS):
                hidden, saved = layer_forward(hidden, conv_weight[section_index, layer], out_weight[section_index, layer], dilations[layer])
                stored.append(saved)
            flowing = carried[batch_index]
            conv_parts = [None] * LAYERS
            out_parts = [None] * LAYERS
            for layer in reversed(range(LAYERS)):
                flowing, conv_parts[layer], out_parts[layer] = layer_backward(flowing, stored[layer], conv_weight[section_index, layer], out_weight[section_index, layer], dilations[layer])
            conv_total = conv_total + jnp.stack(conv_parts)
            out_total = out_total + jnp.stack(out_parts)
            per_batch.append(flowing)
            carried[batch_index] = lax.optimization_barrier(flowing.astype(jnp.bfloat16)).astype(jnp.float32)
        input_rows[section_index] = jnp.stack(per_batch)
        conv_rows[section_index] = (conv_total * grad_scale).reshape(LAYERS, 3 * C, 2 * C)
        out_rows[section_index] = out_total * grad_scale
    return (jnp.stack(input_rows), jnp.stack(conv_rows), jnp.stack(out_rows))
```

```python
import math

import jax
import jax.numpy as jnp
from jax import lax
from jax.sharding import PartitionSpec as P

NEAR = 128
FAR = 1024


def shifted(value, axis, steps):
    count = lax.axis_size(axis)
    leading, last = (max(0, -steps), min(count, count - steps))
    return lax.ppermute(value, axis, [(source, source + steps) for source in range(leading, last)])


def halo_sides(block, width):
    rows = block.shape[1]
    from_low = shifted(block[:, rows - width :], "seq", 1)
    from_high = shifted(block[:, :width], "seq", -1)
    earlier = jnp.concatenate([from_low, block[:, : rows - width]], axis=1)
    following = jnp.concatenate([block[:, width:], from_high], axis=1)
    return earlier, following


def far_sides(block, hops):
    return shifted(block, "seq", hops), shifted(block, "seq", -hops)


def mm(a, b):
    return jnp.einsum("mpc,cd->mpd", a, b, preferred_element_type=jnp.float32)


def forward_layer(hidden, earlier, following, conv, out_mat, last):
    chans = hidden.shape[2]
    preact = mm(earlier, conv[0])
    preact = preact + mm(hidden, conv[1])
    preact = preact + mm(following, conv[2])
    tanh_part = jnp.tanh(preact[..., :chans])
    sig_part = jax.nn.sigmoid(preact[..., chans:])
    gated = (tanh_part * sig_part).astype(jnp.bfloat16)
    factor_a = (1.0 - tanh_part * tanh_part) * sig_part
    factor_b = tanh_part * sig_part * (1.0 - sig_part)
    taps = jnp.concatenate([earlier, hidden, following], axis=2)
    saved = (taps, gated, factor_a, factor_b)
    if last:
        return None, saved
    nxt = (hidden.astype(jnp.float32) + mm(gated, out_mat)).astype(jnp.bfloat16)
    return nxt, saved


def backward_layer(flowing, saved, conv, out_mat, layer, far_hops):
    taps, gated, factor_a, factor_b = saved
    chans = flowing.shape[2]
    grad_half = flowing.astype(jnp.bfloat16)
    out_term = jnp.einsum("mpc,mpd->cd", gated, grad_half, preferred_element_type=jnp.float32)
    grad_gated = jnp.einsum("mpd,cd->mpc", grad_half, out_mat, preferred_element_type=jnp.float32)
    grad_pre = jnp.concatenate([grad_gated * factor_a, grad_gated * factor_b], axis=2).astype(
        jnp.bfloat16
    )
    conv_term = jnp.einsum("mpc,mpd->cd", taps, grad_pre, preferred_element_type=jnp.float32)
    weights = conv.reshape(3 * chans, 2 * chans)
    back = jnp.einsum("mpd,cd->mpc", grad_pre, weights, preferred_element_type=jnp.float32)
    grad_first = back[..., :chans].astype(jnp.bfloat16)
    middle = back[..., chans : 2 * chans]
    grad_third = back[..., 2 * chans :].astype(jnp.bfloat16)
    if layer == 0:
        third_earlier, first_following = halo_sides_pair(grad_first, grad_third, NEAR)
    else:
        third_earlier = shifted(grad_third, "seq", far_hops)
        first_following = shifted(grad_first, "seq", -far_hops)
    grad_conv = middle + first_following.astype(jnp.float32) + third_earlier.astype(jnp.float32)
    return flowing + grad_conv, conv_term, out_term


def halo_sides_pair(grad_first, grad_third, width):
    rows = grad_first.shape[1]
    from_low = shifted(grad_third[:, rows - width :], "seq", 1)
    from_high = shifted(grad_first[:, :width], "seq", -1)
    third_earlier = jnp.concatenate([from_low, grad_third[:, : rows - width]], axis=1)
    first_following = jnp.concatenate([grad_first[:, width:], from_high], axis=1)
    return third_earlier, first_following


def halving_scatter(chunks):
    count = chunks.shape[0]
    rank = lax.axis_index("seq")
    bit = 0
    while (1 << bit) < count:
        own = (rank >> bit) & 1
        pairs = [(j, j ^ (1 << bit)) for j in range(count)]
        split = chunks.reshape(chunks.shape[0] // 2, 2, chunks.shape[1])
        keep = lax.dynamic_index_in_dim(split, own, 1, keepdims=False)
        send = lax.dynamic_index_in_dim(split, 1 - own, 1, keepdims=False)
        got = lax.ppermute(send.astype(jnp.bfloat16), "seq", pairs)
        chunks = keep + got.astype(jnp.float32)
        bit += 1
    return chunks[0]


def shards(section_inputs, cotangent, conv_weight, out_weight):
    batch_count = cotangent.shape[0]
    positions = cotangent.shape[1]
    channels = cotangent.shape[2]
    far_hops = FAR // positions
    seq_count = lax.axis_size("seq")
    section_count = lax.axis_size("section")
    section_rank = lax.axis_index("section")
    conv_mat = conv_weight[0]
    out_mat = out_weight[0]
    depth = conv_mat.shape[0]
    grad_scale = 1.0 / math.sqrt(batch_count * positions * seq_count)

    hidden = section_inputs[0]
    stored = []
    for layer in range(depth):
        if layer == 0:
            earlier, following = halo_sides(hidden, NEAR)
        else:
            earlier, following = far_sides(hidden, far_hops)
        hidden, saved = forward_layer(
            hidden, earlier, following, conv_mat[layer], out_mat[layer], layer + 1 == depth
        )
        stored.append(saved)

    top = jnp.where(section_rank == section_count - 1, 1.0, 0.0).astype(jnp.float32)
    flowing = cotangent.astype(jnp.float32) * top
    input_grads = None
    conv_acc = [None] * depth
    out_acc = [None] * depth
    for step in range(section_count):
        for layer in reversed(range(depth)):
            flowing, conv_term, out_term = backward_layer(
                flowing, stored[layer], conv_mat[layer], out_mat[layer], layer, far_hops
            )
            conv_acc[layer] = conv_term if step == 0 else conv_acc[layer] + conv_term
            out_acc[layer] = out_term if step == 0 else out_acc[layer] + out_term
        input_grads = flowing if step == 0 else input_grads + flowing
        if step + 1 < section_count:
            flowing = shifted(flowing.astype(jnp.bfloat16), "section", -1).astype(jnp.float32)

    conv_rows = 3 * channels // seq_count
    out_rows = channels // seq_count
    conv_all = jnp.stack(conv_acc).reshape(depth, seq_count, conv_rows, 2 * channels)
    out_all = jnp.stack(out_acc).reshape(depth, seq_count, out_rows, channels)
    conv_all = conv_all.transpose(1, 0, 2, 3).reshape(seq_count, -1)
    out_all = out_all.transpose(1, 0, 2, 3).reshape(seq_count, -1)
    mine = halving_scatter(jnp.concatenate([conv_all, out_all], axis=1))
    conv_size = conv_all.shape[1]
    conv_grads = mine[:conv_size].reshape(1, depth, conv_rows, 2 * channels) * grad_scale
    out_grads = mine[conv_size:].reshape(1, depth, out_rows, channels) * grad_scale
    return (input_grads[None], conv_grads, out_grads)


def solution(mesh):
    return jax.shard_map(
        shards,
        mesh=mesh,
        in_specs=(
            P("section", None, "seq", None),
            P(None, "seq", None),
            P("section", None, None, None, None),
            P("section", None, None, None),
        ),
        out_specs=(
            P("section", None, "seq", None),
            P("section", None, "seq", None),
            P("section", None, "seq", None),
        ),
        check_vma=False,
    )
```

```python
import math

import jax
import jax.numpy as jnp
from jax import lax
from jax.sharding import PartitionSpec as P

NEAR = 128
FAR = 1024


def shifted(value, axis, steps):
    count = lax.axis_size(axis)
    leading, last = (max(0, -steps), min(count, count - steps))
    return lax.ppermute(value, axis, [(source, source + steps) for source in range(leading, last)])


def halo_sides(block, width):
    rows = block.shape[1]
    from_low = shifted(block[:, rows - width :], "seq", 1)
    from_high = shifted(block[:, :width], "seq", -1)
    earlier = jnp.concatenate([from_low, block[:, : rows - width]], axis=1)
    following = jnp.concatenate([block[:, width:], from_high], axis=1)
    return earlier, following


def far_sides(block, hops):
    return shifted(block, "seq", hops), shifted(block, "seq", -hops)


def mm(a, b):
    return jnp.einsum("mpc,cd->mpd", a, b, preferred_element_type=jnp.float32)


def forward_layer(hidden, earlier, following, conv, out_mat, last):
    chans = hidden.shape[2]
    preact = mm(earlier, conv[0])
    preact = preact + mm(hidden, conv[1])
    preact = preact + mm(following, conv[2])
    tanh_part = jnp.tanh(preact[..., :chans])
    sig_part = jax.nn.sigmoid(preact[..., chans:])
    gated = (tanh_part * sig_part).astype(jnp.bfloat16)
    factor_a = (1.0 - tanh_part * tanh_part) * sig_part
    factor_b = tanh_part * sig_part * (1.0 - sig_part)
    taps = jnp.concatenate([earlier, hidden, following], axis=2)
    saved = (taps, gated, factor_a, factor_b)
    if last:
        return None, saved
    nxt = (hidden.astype(jnp.float32) + mm(gated, out_mat)).astype(jnp.bfloat16)
    return nxt, saved


def backward_layer(flowing, saved, conv, out_mat, layer, far_hops):
    taps, gated, factor_a, factor_b = saved
    chans = flowing.shape[2]
    grad_half = flowing.astype(jnp.bfloat16)
    out_term = jnp.einsum("mpc,mpd->cd", gated, grad_half, preferred_element_type=jnp.float32)
    grad_gated = jnp.einsum("mpd,cd->mpc", grad_half, out_mat, preferred_element_type=jnp.float32)
    grad_pre = jnp.concatenate([grad_gated * factor_a, grad_gated * factor_b], axis=2).astype(
        jnp.bfloat16
    )
    conv_term = jnp.einsum("mpc,mpd->cd", taps, grad_pre, preferred_element_type=jnp.float32)
    weights = conv.reshape(3 * chans, 2 * chans)
    back = jnp.einsum("mpd,cd->mpc", grad_pre, weights, preferred_element_type=jnp.float32)
    grad_first = back[..., :chans].astype(jnp.bfloat16)
    middle = back[..., chans : 2 * chans]
    grad_third = back[..., 2 * chans :].astype(jnp.bfloat16)
    if layer == 0:
        third_earlier, first_following = halo_sides_pair(grad_first, grad_third, NEAR)
    else:
        third_earlier = shifted(grad_third, "seq", far_hops)
        first_following = shifted(grad_first, "seq", -far_hops)
    grad_conv = middle + first_following.astype(jnp.float32) + third_earlier.astype(jnp.float32)
    return flowing + grad_conv, conv_term, out_term


def halo_sides_pair(grad_first, grad_third, width):
    rows = grad_first.shape[1]
    from_low = shifted(grad_third[:, rows - width :], "seq", 1)
    from_high = shifted(grad_first[:, :width], "seq", -1)
    third_earlier = jnp.concatenate([from_low, grad_third[:, : rows - width]], axis=1)
    first_following = jnp.concatenate([grad_first[:, width:], from_high], axis=1)
    return third_earlier, first_following


def halving_scatter(parts):
    count = parts[0].shape[0]
    rank = lax.axis_index("seq")
    bit = 0
    while (1 << bit) < count:
        own = ((rank >> bit) & 1) == 1
        pairs = [(j, j ^ (1 << bit)) for j in range(count)]
        halves = [p.reshape(p.shape[0] // 2, 2, *p.shape[1:]) for p in parts]
        sends = tuple(jnp.where(own, h[:, 0], h[:, 1]).astype(jnp.bfloat16) for h in halves)
        got = lax.ppermute(sends, "seq", pairs)
        parts = [jnp.where(own, h[:, 1], h[:, 0]) + g.astype(jnp.float32) for h, g in zip(halves, got)]
        bit += 1
    return [p[0] for p in parts]


def shards(section_inputs, cotangent, conv_weight, out_weight):
    batch_count = cotangent.shape[0]
    positions = cotangent.shape[1]
    channels = cotangent.shape[2]
    far_hops = FAR // positions
    seq_count = lax.axis_size("seq")
    section_count = lax.axis_size("section")
    section_rank = lax.axis_index("section")
    conv_mat = conv_weight[0]
    out_mat = out_weight[0]
    depth = conv_mat.shape[0]
    grad_scale = 1.0 / math.sqrt(batch_count * positions * seq_count)

    hidden = section_inputs[0]
    stored = []
    for layer in range(depth):
        if layer == 0:
            earlier, following = halo_sides(hidden, NEAR)
        else:
            earlier, following = far_sides(hidden, far_hops)
        hidden, saved = forward_layer(
            hidden, earlier, following, conv_mat[layer], out_mat[layer], layer + 1 == depth
        )
        stored.append(saved)

    top = jnp.where(section_rank == section_count - 1, 1.0, 0.0).astype(jnp.float32)
    flowing = cotangent.astype(jnp.float32) * top
    input_grads = None
    conv_acc = [None] * depth
    out_acc = [None] * depth
    for step in range(section_count):
        for layer in reversed(range(depth)):
            flowing, conv_term, out_term = backward_layer(
                flowing, stored[layer], conv_mat[layer], out_mat[layer], layer, far_hops
            )
            conv_acc[layer] = conv_term if step == 0 else conv_acc[layer] + conv_term
            out_acc[layer] = out_term if step == 0 else out_acc[layer] + out_term
        input_grads = flowing if step == 0 else input_grads + flowing
        if step + 1 < section_count:
            flowing = shifted(flowing.astype(jnp.bfloat16), "section", -1).astype(jnp.float32)

    conv_rows = 3 * channels // seq_count
    out_rows = channels // seq_count
    conv_parts = []
    out_parts = []
    for layer in range(depth):
        conv_mine, out_mine = halving_scatter(
            [
                conv_acc[layer].reshape(seq_count, conv_rows, 2 * channels),
                out_acc[layer].reshape(seq_count, out_rows, channels),
            ]
        )
        conv_parts.append(conv_mine)
        out_parts.append(out_mine)
    conv_grads = jnp.stack(conv_parts)[None] * grad_scale
    out_grads = jnp.stack(out_parts)[None] * grad_scale
    return (input_grads[None], conv_grads, out_grads)


def solution(mesh):
    return jax.shard_map(
        shards,
        mesh=mesh,
        in_specs=(
            P("section", None, "seq", None),
            P(None, "seq", None),
            P("section", None, None, None, None),
            P("section", None, None, None),
        ),
        out_specs=(
            P("section", None, "seq", None),
            P("section", None, "seq", None),
            P("section", None, "seq", None),
        ),
        check_vma=False,
    )
```

```python
import math

import jax
import jax.numpy as jnp
from jax import lax
from jax.sharding import PartitionSpec as P

NEAR = 128
FAR = 1024


def shifted(value, axis, steps):
    count = lax.axis_size(axis)
    leading, last = (max(0, -steps), min(count, count - steps))
    return lax.ppermute(value, axis, [(source, source + steps) for source in range(leading, last)])


def halo_sides(block, width):
    rows = block.shape[1]
    from_low = shifted(block[:, rows - width :], "seq", 1)
    from_high = shifted(block[:, :width], "seq", -1)
    earlier = jnp.concatenate([from_low, block[:, : rows - width]], axis=1)
    following = jnp.concatenate([block[:, width:], from_high], axis=1)
    return earlier, following


def far_sides(block, hops):
    return shifted(block, "seq", hops), shifted(block, "seq", -hops)


def mm(a, b):
    return jnp.einsum("mpc,cd->mpd", a, b, preferred_element_type=jnp.float32)


def forward_layer(hidden, earlier, following, conv, out_mat, last):
    chans = hidden.shape[2]
    preact = mm(earlier, conv[0])
    preact = preact + mm(hidden, conv[1])
    preact = preact + mm(following, conv[2])
    tanh_part = jnp.tanh(preact[..., :chans])
    sig_part = jax.nn.sigmoid(preact[..., chans:])
    gated = (tanh_part * sig_part).astype(jnp.bfloat16)
    factor_a = (1.0 - tanh_part * tanh_part) * sig_part
    factor_b = tanh_part * sig_part * (1.0 - sig_part)
    taps = jnp.concatenate([earlier, hidden, following], axis=2)
    saved = (taps, gated, factor_a, factor_b)
    if last:
        return None, saved
    nxt = (hidden.astype(jnp.float32) + mm(gated, out_mat)).astype(jnp.bfloat16)
    return nxt, saved


def backward_layer(flowing, saved, conv, out_mat, layer, far_hops):
    taps, gated, factor_a, factor_b = saved
    chans = flowing.shape[2]
    grad_half = flowing.astype(jnp.bfloat16)
    out_term = jnp.einsum("mpc,mpd->cd", gated, grad_half, preferred_element_type=jnp.float32)
    grad_gated = jnp.einsum("mpd,cd->mpc", grad_half, out_mat, preferred_element_type=jnp.float32)
    grad_pre = jnp.concatenate([grad_gated * factor_a, grad_gated * factor_b], axis=2).astype(
        jnp.bfloat16
    )
    conv_term = jnp.einsum("mpc,mpd->cd", taps, grad_pre, preferred_element_type=jnp.float32)
    weights = conv.reshape(3 * chans, 2 * chans)
    back = jnp.einsum("mpd,cd->mpc", grad_pre, weights, preferred_element_type=jnp.float32)
    grad_first = back[..., :chans].astype(jnp.bfloat16)
    middle = back[..., chans : 2 * chans]
    grad_third = back[..., 2 * chans :].astype(jnp.bfloat16)
    if layer == 0:
        third_earlier, first_following = halo_sides_pair(grad_first, grad_third, NEAR)
    else:
        third_earlier = shifted(grad_third, "seq", far_hops)
        first_following = shifted(grad_first, "seq", -far_hops)
    grad_conv = middle + first_following.astype(jnp.float32) + third_earlier.astype(jnp.float32)
    return flowing + grad_conv, conv_term, out_term


def halo_sides_pair(grad_first, grad_third, width):
    rows = grad_first.shape[1]
    from_low = shifted(grad_third[:, rows - width :], "seq", 1)
    from_high = shifted(grad_first[:, :width], "seq", -1)
    third_earlier = jnp.concatenate([from_low, grad_third[:, : rows - width]], axis=1)
    first_following = jnp.concatenate([grad_first[:, width:], from_high], axis=1)
    return third_earlier, first_following


def halving_scatter(parts):
    count = parts[0].shape[0]
    rank = lax.axis_index("seq")
    bit = 0
    while (1 << bit) < count:
        own = ((rank >> bit) & 1) == 1
        pairs = [(j, j ^ (1 << bit)) for j in range(count)]
        halves = [p.reshape(p.shape[0] // 2, 2, *p.shape[1:]) for p in parts]
        sends = tuple(jnp.where(own, h[:, 0], h[:, 1]).astype(jnp.bfloat16) for h in halves)
        got = lax.ppermute(sends, "seq", pairs)
        parts = [jnp.where(own, h[:, 1], h[:, 0]) + g.astype(jnp.float32) for h, g in zip(halves, got)]
        bit += 1
    return [p[0] for p in parts]


def shards(section_inputs, cotangent, conv_weight, out_weight):
    batch_count = cotangent.shape[0]
    positions = cotangent.shape[1]
    channels = cotangent.shape[2]
    far_hops = FAR // positions
    seq_count = lax.axis_size("seq")
    section_count = lax.axis_size("section")
    section_rank = lax.axis_index("section")
    conv_mat = conv_weight[0]
    out_mat = out_weight[0]
    depth = conv_mat.shape[0]
    grad_scale = 1.0 / math.sqrt(batch_count * positions * seq_count)

    hidden = section_inputs[0]
    stored = []
    for layer in range(depth):
        if layer == 0:
            earlier, following = halo_sides(hidden, NEAR)
        else:
            earlier, following = far_sides(hidden, far_hops)
        hidden, saved = forward_layer(
            hidden, earlier, following, conv_mat[layer], out_mat[layer], layer + 1 == depth
        )
        stored.append(saved)

    top = jnp.where(section_rank == section_count - 1, 1.0, 0.0).astype(jnp.float32)
    flowing = cotangent.astype(jnp.float32) * top
    input_grads = None
    conv_acc = [None] * depth
    out_acc = [None] * depth
    for step in range(section_count):
        for layer in reversed(range(depth)):
            flowing, conv_term, out_term = backward_layer(
                flowing, stored[layer], conv_mat[layer], out_mat[layer], layer, far_hops
            )
            conv_acc[layer] = conv_term if step == 0 else conv_acc[layer] + conv_term
            out_acc[layer] = out_term if step == 0 else out_acc[layer] + out_term
        input_grads = flowing if step == 0 else input_grads + flowing
        if step + 1 < section_count:
            flowing = shifted(flowing.astype(jnp.bfloat16), "section", -1).astype(jnp.float32)

    conv_rows = 3 * channels // seq_count
    out_rows = channels // seq_count
    conv_all = jnp.concatenate(
        [acc.reshape(seq_count, conv_rows, 2 * channels) for acc in conv_acc], axis=1
    )
    out_all = jnp.concatenate(
        [acc.reshape(seq_count, out_rows, channels) for acc in out_acc], axis=1
    ).reshape(seq_count, depth * out_rows * channels // (2 * channels), 2 * channels)
    (mine,) = halving_scatter([jnp.concatenate([conv_all, out_all], axis=1)])
    conv_grads = mine[: depth * conv_rows].reshape(1, depth, conv_rows, 2 * channels) * grad_scale
    out_grads = mine[depth * conv_rows :].reshape(1, depth, out_rows, channels) * grad_scale
    return (input_grads[None], conv_grads, out_grads)


def solution(mesh):
    return jax.shard_map(
        shards,
        mesh=mesh,
        in_specs=(
            P("section", None, "seq", None),
            P(None, "seq", None),
            P("section", None, None, None, None),
            P("section", None, None, None),
        ),
        out_specs=(
            P("section", None, "seq", None),
            P("section", None, "seq", None),
            P("section", None, "seq", None),
        ),
        check_vma=False,
    )
```

```python
import math

import jax
import jax.numpy as jnp
from jax import lax
from jax.sharding import PartitionSpec as P

NEAR = 128
FAR = 1024


def shifted(value, axis, steps):
    count = lax.axis_size(axis)
    leading, last = (max(0, -steps), min(count, count - steps))
    return lax.ppermute(value, axis, [(source, source + steps) for source in range(leading, last)])


def halo_sides(block, width):
    rows = block.shape[1]
    from_low = shifted(block[:, rows - width :], "seq", 1)
    from_high = shifted(block[:, :width], "seq", -1)
    earlier = jnp.concatenate([from_low, block[:, : rows - width]], axis=1)
    following = jnp.concatenate([block[:, width:], from_high], axis=1)
    return earlier, following


def far_sides(block, hops):
    return shifted(block, "seq", hops), shifted(block, "seq", -hops)


def mm(a, b):
    return jnp.einsum("mpc,cd->mpd", a, b, preferred_element_type=jnp.float32)


def forward_layer(hidden, earlier, following, conv, out_mat, last):
    chans = hidden.shape[2]
    preact = mm(earlier, conv[0])
    preact = preact + mm(hidden, conv[1])
    preact = preact + mm(following, conv[2])
    tanh_part = jnp.tanh(preact[..., :chans])
    sig_part = jax.nn.sigmoid(preact[..., chans:])
    gated = (tanh_part * sig_part).astype(jnp.bfloat16)
    factor_a = (1.0 - tanh_part * tanh_part) * sig_part
    factor_b = tanh_part * sig_part * (1.0 - sig_part)
    taps = jnp.concatenate([earlier, hidden, following], axis=2)
    saved = (taps, gated, factor_a, factor_b)
    if last:
        return None, saved
    nxt = (hidden.astype(jnp.float32) + mm(gated, out_mat)).astype(jnp.bfloat16)
    return nxt, saved


def backward_layer(flowing, saved, conv, out_mat, layer, far_hops):
    taps, gated, factor_a, factor_b = saved
    chans = flowing.shape[2]
    grad_half = flowing.astype(jnp.bfloat16)
    out_term = jnp.einsum("mpc,mpd->cd", gated, grad_half, preferred_element_type=jnp.float32)
    grad_gated = jnp.einsum("mpd,cd->mpc", grad_half, out_mat, preferred_element_type=jnp.float32)
    grad_pre = jnp.concatenate([grad_gated * factor_a, grad_gated * factor_b], axis=2).astype(
        jnp.bfloat16
    )
    conv_term = jnp.einsum("mpc,mpd->cd", taps, grad_pre, preferred_element_type=jnp.float32)
    weights = conv.reshape(3 * chans, 2 * chans)
    back = jnp.einsum("mpd,cd->mpc", grad_pre, weights, preferred_element_type=jnp.float32)
    grad_first = back[..., :chans].astype(jnp.bfloat16)
    middle = back[..., chans : 2 * chans]
    grad_third = back[..., 2 * chans :].astype(jnp.bfloat16)
    if layer == 0:
        third_earlier, first_following = halo_sides_pair(grad_first, grad_third, NEAR)
    else:
        third_earlier = shifted(grad_third, "seq", far_hops)
        first_following = shifted(grad_first, "seq", -far_hops)
    grad_conv = middle + first_following.astype(jnp.float32) + third_earlier.astype(jnp.float32)
    return flowing + grad_conv, conv_term, out_term


def halo_sides_pair(grad_first, grad_third, width):
    rows = grad_first.shape[1]
    from_low = shifted(grad_third[:, rows - width :], "seq", 1)
    from_high = shifted(grad_first[:, :width], "seq", -1)
    third_earlier = jnp.concatenate([from_low, grad_third[:, : rows - width]], axis=1)
    first_following = jnp.concatenate([grad_first[:, width:], from_high], axis=1)
    return third_earlier, first_following


def halving_scatter(parts):
    count = parts[0].shape[0]
    rank = lax.axis_index("seq")
    bit = 0
    while (1 << bit) < count:
        own = ((rank >> bit) & 1) == 1
        pairs = [(j, j ^ (1 << bit)) for j in range(count)]
        halves = [p.reshape(p.shape[0] // 2, 2, *p.shape[1:]) for p in parts]
        sends = tuple(jnp.where(own, h[:, 0], h[:, 1]).astype(jnp.bfloat16) for h in halves)
        got = lax.ppermute(sends, "seq", pairs)
        parts = [jnp.where(own, h[:, 1], h[:, 0]) + g.astype(jnp.float32) for h, g in zip(halves, got)]
        bit += 1
    return [p[0] for p in parts]


def shards(section_inputs, cotangent, conv_weight, out_weight):
    batch_count = cotangent.shape[0]
    positions = cotangent.shape[1]
    channels = cotangent.shape[2]
    far_hops = FAR // positions
    seq_count = lax.axis_size("seq")
    section_count = lax.axis_size("section")
    section_rank = lax.axis_index("section")
    conv_mat = conv_weight[0]
    out_mat = out_weight[0]
    depth = conv_mat.shape[0]
    grad_scale = 1.0 / math.sqrt(batch_count * positions * seq_count)

    stored = []
    for batch in range(batch_count):
        hidden = section_inputs[0, batch : batch + 1]
        layers = []
        for layer in range(depth):
            if layer == 0:
                earlier, following = halo_sides(hidden, NEAR)
            else:
                earlier, following = far_sides(hidden, far_hops)
            hidden, saved = forward_layer(
                hidden, earlier, following, conv_mat[layer], out_mat[layer], layer + 1 == depth
            )
            layers.append(saved)
        stored.append(layers)

    top = jnp.where(section_rank == section_count - 1, 1.0, 0.0).astype(jnp.float32)
    flowing = [cotangent[b : b + 1].astype(jnp.float32) * top for b in range(batch_count)]
    input_grads = [None] * batch_count
    conv_acc = [None] * depth
    out_acc = [None] * depth
    for step in range(section_count):
        for batch in range(batch_count):
            for layer in reversed(range(depth)):
                flowing[batch], conv_term, out_term = backward_layer(
                    flowing[batch], stored[batch][layer], conv_mat[layer], out_mat[layer], layer, far_hops
                )
                first = step == 0 and batch == 0
                conv_acc[layer] = conv_term if first else conv_acc[layer] + conv_term
                out_acc[layer] = out_term if first else out_acc[layer] + out_term
            input_grads[batch] = (
                flowing[batch] if step == 0 else input_grads[batch] + flowing[batch]
            )
            if step + 1 < section_count:
                flowing[batch] = shifted(
                    flowing[batch].astype(jnp.bfloat16), "section", -1
                ).astype(jnp.float32)
    input_grads = jnp.concatenate(input_grads, axis=0)

    conv_rows = 3 * channels // seq_count
    out_rows = channels // seq_count
    conv_all = jnp.concatenate(
        [acc.reshape(seq_count, conv_rows, 2 * channels) for acc in conv_acc], axis=1
    )
    out_all = jnp.concatenate(
        [acc.reshape(seq_count, out_rows, channels) for acc in out_acc], axis=1
    ).reshape(seq_count, depth * out_rows * channels // (2 * channels), 2 * channels)
    (mine,) = halving_scatter([jnp.concatenate([conv_all, out_all], axis=1)])
    conv_grads = mine[: depth * conv_rows].reshape(1, depth, conv_rows, 2 * channels) * grad_scale
    out_grads = mine[depth * conv_rows :].reshape(1, depth, out_rows, channels) * grad_scale
    return (input_grads[None], conv_grads, out_grads)


def solution(mesh):
    return jax.shard_map(
        shards,
        mesh=mesh,
        in_specs=(
            P("section", None, "seq", None),
            P(None, "seq", None),
            P("section", None, None, None, None),
            P("section", None, None, None),
        ),
        out_specs=(
            P("section", None, "seq", None),
            P("section", None, "seq", None),
            P("section", None, "seq", None),
        ),
        check_vma=False,
    )
```

```python
import math

import jax
import jax.numpy as jnp
from jax import lax
from jax.sharding import PartitionSpec as P

NEAR = 128
FAR = 1024


def shifted(value, axis, steps):
    count = lax.axis_size(axis)
    leading, last = (max(0, -steps), min(count, count - steps))
    return lax.ppermute(value, axis, [(source, source + steps) for source in range(leading, last)])


def halo_sides(block, width):
    rows = block.shape[1]
    from_low = shifted(block[:, rows - width :], "seq", 1)
    from_high = shifted(block[:, :width], "seq", -1)
    earlier = jnp.concatenate([from_low, block[:, : rows - width]], axis=1)
    following = jnp.concatenate([block[:, width:], from_high], axis=1)
    return earlier, following


def far_sides(block, hops):
    return shifted(block, "seq", hops), shifted(block, "seq", -hops)


def mm(a, b):
    return jnp.einsum("mpc,cd->mpd", a, b, preferred_element_type=jnp.float32)


def forward_layer(hidden, earlier, following, conv, out_mat, last):
    chans = hidden.shape[2]
    preact = mm(earlier, conv[0])
    preact = preact + mm(hidden, conv[1])
    preact = preact + mm(following, conv[2])
    tanh_part = jnp.tanh(preact[..., :chans])
    sig_part = jax.nn.sigmoid(preact[..., chans:])
    gated = (tanh_part * sig_part).astype(jnp.bfloat16)
    factor_a = (1.0 - tanh_part * tanh_part) * sig_part
    factor_b = tanh_part * sig_part * (1.0 - sig_part)
    taps = jnp.concatenate([earlier, hidden, following], axis=2)
    saved = (taps, gated, factor_a, factor_b)
    if last:
        return None, saved
    nxt = (hidden.astype(jnp.float32) + mm(gated, out_mat)).astype(jnp.bfloat16)
    return nxt, saved


def backward_layer(flowing, saved, conv, out_mat, layer, far_hops):
    taps, gated, factor_a, factor_b = saved
    chans = flowing.shape[2]
    grad_half = flowing.astype(jnp.bfloat16)
    out_term = jnp.einsum("mpc,mpd->cd", gated, grad_half, preferred_element_type=jnp.float32)
    grad_gated = jnp.einsum("mpd,cd->mpc", grad_half, out_mat, preferred_element_type=jnp.float32)
    grad_pre = jnp.concatenate([grad_gated * factor_a, grad_gated * factor_b], axis=2).astype(
        jnp.bfloat16
    )
    conv_term = jnp.einsum("mpc,mpd->cd", taps, grad_pre, preferred_element_type=jnp.float32)
    weights = conv.reshape(3 * chans, 2 * chans)
    back = jnp.einsum("mpd,cd->mpc", grad_pre, weights, preferred_element_type=jnp.float32)
    grad_first = back[..., :chans].astype(jnp.bfloat16)
    middle = back[..., chans : 2 * chans]
    grad_third = back[..., 2 * chans :].astype(jnp.bfloat16)
    if layer == 0:
        return split_near(flowing, middle, grad_first, grad_third, NEAR), conv_term, out_term
    else:
        third_earlier = shifted(grad_third, "seq", far_hops)
        first_following = shifted(grad_first, "seq", -far_hops)
    grad_conv = middle + first_following.astype(jnp.float32) + third_earlier.astype(jnp.float32)
    return flowing + grad_conv, conv_term, out_term


def split_near(flowing, middle, grad_first, grad_third, width):
    rows = grad_first.shape[1]
    low_in = shifted(grad_third[:, rows - width :], "seq", 1)
    high_in = shifted(grad_first[:, :width], "seq", -1)
    f32 = jnp.float32
    inner = flowing[:, width : rows - width] + (
        middle[:, width : rows - width]
        + grad_first[:, 2 * width :].astype(f32)
        + grad_third[:, : rows - 2 * width].astype(f32)
    )
    low = flowing[:, :width] + (
        middle[:, :width] + grad_first[:, width : 2 * width].astype(f32) + low_in.astype(f32)
    )
    high = flowing[:, rows - width :] + (
        middle[:, rows - width :]
        + high_in.astype(f32)
        + grad_third[:, rows - 2 * width : rows - width].astype(f32)
    )
    return low, inner, high


def halo_sides_pair(grad_first, grad_third, width):
    rows = grad_first.shape[1]
    from_low = shifted(grad_third[:, rows - width :], "seq", 1)
    from_high = shifted(grad_first[:, :width], "seq", -1)
    third_earlier = jnp.concatenate([from_low, grad_third[:, : rows - width]], axis=1)
    first_following = jnp.concatenate([grad_first[:, width:], from_high], axis=1)
    return third_earlier, first_following


def halving_scatter(parts):
    count = parts[0].shape[0]
    rank = lax.axis_index("seq")
    bit = 0
    while (1 << bit) < count:
        own = ((rank >> bit) & 1) == 1
        pairs = [(j, j ^ (1 << bit)) for j in range(count)]
        halves = [p.reshape(p.shape[0] // 2, 2, *p.shape[1:]) for p in parts]
        sends = tuple(jnp.where(own, h[:, 0], h[:, 1]).astype(jnp.bfloat16) for h in halves)
        got = lax.ppermute(sends, "seq", pairs)
        parts = [jnp.where(own, h[:, 1], h[:, 0]) + g.astype(jnp.float32) for h, g in zip(halves, got)]
        bit += 1
    return [p[0] for p in parts]


def shards(section_inputs, cotangent, conv_weight, out_weight):
    batch_count = cotangent.shape[0]
    positions = cotangent.shape[1]
    channels = cotangent.shape[2]
    far_hops = FAR // positions
    seq_count = lax.axis_size("seq")
    section_count = lax.axis_size("section")
    section_rank = lax.axis_index("section")
    conv_mat = conv_weight[0]
    out_mat = out_weight[0]
    depth = conv_mat.shape[0]
    grad_scale = 1.0 / math.sqrt(batch_count * positions * seq_count)

    hidden = section_inputs[0]
    stored = []
    for layer in range(depth):
        if layer == 0:
            earlier, following = halo_sides(hidden, NEAR)
        else:
            earlier, following = far_sides(hidden, far_hops)
        hidden, saved = forward_layer(
            hidden, earlier, following, conv_mat[layer], out_mat[layer], layer + 1 == depth
        )
        stored.append(saved)

    top = jnp.where(section_rank == section_count - 1, 1.0, 0.0).astype(jnp.float32)
    flowing = cotangent.astype(jnp.float32) * top
    input_grads = None
    conv_acc = [None] * depth
    out_acc = [None] * depth
    for step in range(section_count):
        for layer in reversed(range(depth)):
            flowing, conv_term, out_term = backward_layer(
                flowing, stored[layer], conv_mat[layer], out_mat[layer], layer, far_hops
            )
            conv_acc[layer] = conv_term if step == 0 else conv_acc[layer] + conv_term
            out_acc[layer] = out_term if step == 0 else out_acc[layer] + out_term
        low, inner, high = flowing
        flowing = jnp.concatenate([low, inner, high], axis=1)
        input_grads = flowing if step == 0 else input_grads + flowing
        if step + 1 < section_count:
            bf16 = jnp.bfloat16
            inner = shifted(inner.astype(bf16), "section", -1)
            edges = shifted(jnp.concatenate([low, high], axis=1).astype(bf16), "section", -1)
            width = low.shape[1]
            flowing = jnp.concatenate(
                [edges[:, :width], inner, edges[:, width:]], axis=1
            ).astype(jnp.float32)

    conv_rows = 3 * channels // seq_count
    out_rows = channels // seq_count
    conv_all = jnp.concatenate(
        [acc.reshape(seq_count, conv_rows, 2 * channels) for acc in conv_acc], axis=1
    )
    out_all = jnp.concatenate(
        [acc.reshape(seq_count, out_rows, channels) for acc in out_acc], axis=1
    ).reshape(seq_count, depth * out_rows * channels // (2 * channels), 2 * channels)
    (mine,) = halving_scatter([jnp.concatenate([conv_all, out_all], axis=1)])
    conv_grads = mine[: depth * conv_rows].reshape(1, depth, conv_rows, 2 * channels) * grad_scale
    out_grads = mine[depth * conv_rows :].reshape(1, depth, out_rows, channels) * grad_scale
    return (input_grads[None], conv_grads, out_grads)


def solution(mesh):
    return jax.shard_map(
        shards,
        mesh=mesh,
        in_specs=(
            P("section", None, "seq", None),
            P(None, "seq", None),
            P("section", None, None, None, None),
            P("section", None, None, None),
        ),
        out_specs=(
            P("section", None, "seq", None),
            P("section", None, "seq", None),
            P("section", None, "seq", None),
        ),
        check_vma=False,
    )
```

```python
import math

import jax
import jax.numpy as jnp
from jax import lax
from jax.sharding import PartitionSpec as P

NEAR = 128
FAR = 1024


def shifted(value, axis, steps):
    count = lax.axis_size(axis)
    leading, last = (max(0, -steps), min(count, count - steps))
    return lax.ppermute(value, axis, [(source, source + steps) for source in range(leading, last)])


def halo_sides(block, width):
    rows = block.shape[1]
    from_low = shifted(block[:, rows - width :], "seq", 1)
    from_high = shifted(block[:, :width], "seq", -1)
    earlier = jnp.concatenate([from_low, block[:, : rows - width]], axis=1)
    following = jnp.concatenate([block[:, width:], from_high], axis=1)
    return earlier, following


def far_sides(block, hops):
    return shifted(block, "seq", hops), shifted(block, "seq", -hops)


def mm(a, b):
    return jnp.einsum("mpc,cd->mpd", a, b, preferred_element_type=jnp.float32)


def forward_layer(hidden, earlier, following, conv, out_mat, last):
    chans = hidden.shape[2]
    preact = mm(earlier, conv[0])
    preact = preact + mm(hidden, conv[1])
    preact = preact + mm(following, conv[2])
    tanh_part = jnp.tanh(preact[..., :chans])
    sig_part = jax.nn.sigmoid(preact[..., chans:])
    gated = (tanh_part * sig_part).astype(jnp.bfloat16)
    factor_a = (1.0 - tanh_part * tanh_part) * sig_part
    factor_b = tanh_part * sig_part * (1.0 - sig_part)
    taps = jnp.concatenate([earlier, hidden, following], axis=2)
    saved = (taps, gated, factor_a, factor_b)
    if last:
        return None, saved
    nxt = (hidden.astype(jnp.float32) + mm(gated, out_mat)).astype(jnp.bfloat16)
    return nxt, saved


def backward_layer(flowing, saved, conv, out_mat, layer, far_hops):
    taps, gated, factor_a, factor_b = saved
    chans = flowing.shape[2]
    grad_half = flowing.astype(jnp.bfloat16)
    out_term = jnp.einsum("mpc,mpd->cd", gated, grad_half, preferred_element_type=jnp.float32)
    grad_gated = jnp.einsum("mpd,cd->mpc", grad_half, out_mat, preferred_element_type=jnp.float32)
    grad_pre = jnp.concatenate([grad_gated * factor_a, grad_gated * factor_b], axis=2).astype(
        jnp.bfloat16
    )
    conv_term = jnp.einsum("mpc,mpd->cd", taps, grad_pre, preferred_element_type=jnp.float32)
    weights = conv.reshape(3 * chans, 2 * chans)
    back = jnp.einsum("mpd,cd->mpc", grad_pre, weights, preferred_element_type=jnp.float32)
    grad_first = back[..., :chans].astype(jnp.bfloat16)
    middle = back[..., chans : 2 * chans]
    grad_third = back[..., 2 * chans :].astype(jnp.bfloat16)
    if layer == 0:
        return split_near(flowing, middle, grad_first, grad_third, NEAR), conv_term, out_term
    else:
        third_earlier = shifted(grad_third, "seq", far_hops)
        first_following = shifted(grad_first, "seq", -far_hops)
    grad_conv = middle + first_following.astype(jnp.float32) + third_earlier.astype(jnp.float32)
    return flowing + grad_conv, conv_term, out_term


def split_near(flowing, middle, grad_first, grad_third, width):
    rows = grad_first.shape[1]
    low_in = shifted(grad_third[:, rows - width :], "seq", 1)
    high_in = shifted(grad_first[:, :width], "seq", -1)
    f32 = jnp.float32
    inner = flowing[:, width : rows - width] + (
        middle[:, width : rows - width]
        + grad_first[:, 2 * width :].astype(f32)
        + grad_third[:, : rows - 2 * width].astype(f32)
    )
    low = flowing[:, :width] + (
        middle[:, :width] + grad_first[:, width : 2 * width].astype(f32) + low_in.astype(f32)
    )
    high = flowing[:, rows - width :] + (
        middle[:, rows - width :]
        + high_in.astype(f32)
        + grad_third[:, rows - 2 * width : rows - width].astype(f32)
    )
    return low, inner, high


def halo_sides_pair(grad_first, grad_third, width):
    rows = grad_first.shape[1]
    from_low = shifted(grad_third[:, rows - width :], "seq", 1)
    from_high = shifted(grad_first[:, :width], "seq", -1)
    third_earlier = jnp.concatenate([from_low, grad_third[:, : rows - width]], axis=1)
    first_following = jnp.concatenate([grad_first[:, width:], from_high], axis=1)
    return third_earlier, first_following


def halving_scatter(parts):
    count = parts[0].shape[0]
    rank = lax.axis_index("seq")
    bit = 0
    while (1 << bit) < count:
        own = ((rank >> bit) & 1) == 1
        pairs = [(j, j ^ (1 << bit)) for j in range(count)]
        halves = [p.reshape(p.shape[0] // 2, 2, *p.shape[1:]) for p in parts]
        sends = tuple(jnp.where(own, h[:, 0], h[:, 1]).astype(jnp.bfloat16) for h in halves)
        got = lax.ppermute(sends, "seq", pairs)
        parts = [jnp.where(own, h[:, 1], h[:, 0]) + g.astype(jnp.float32) for h, g in zip(halves, got)]
        bit += 1
    return [p[0] for p in parts]


def shards(section_inputs, cotangent, conv_weight, out_weight):
    batch_count = cotangent.shape[0]
    positions = cotangent.shape[1]
    channels = cotangent.shape[2]
    far_hops = FAR // positions
    seq_count = lax.axis_size("seq")
    section_count = lax.axis_size("section")
    section_rank = lax.axis_index("section")
    conv_mat = conv_weight[0]
    out_mat = out_weight[0]
    depth = conv_mat.shape[0]
    grad_scale = 1.0 / math.sqrt(batch_count * positions * seq_count)

    hidden = section_inputs[0]
    stored = []
    for layer in range(depth):
        if layer == 0:
            earlier, following = halo_sides(hidden, NEAR)
        else:
            earlier, following = far_sides(hidden, far_hops)
        hidden, saved = forward_layer(
            hidden, earlier, following, conv_mat[layer], out_mat[layer], layer + 1 == depth
        )
        stored.append(saved)

    top = jnp.where(section_rank == section_count - 1, 1.0, 0.0).astype(jnp.float32)
    flowing = cotangent.astype(jnp.float32) * top
    input_grads = None
    conv_acc = [None] * depth
    out_acc = [None] * depth
    for step in range(section_count):
        for layer in reversed(range(depth)):
            flowing, conv_term, out_term = backward_layer(
                flowing, stored[layer], conv_mat[layer], out_mat[layer], layer, far_hops
            )
            conv_acc[layer] = conv_term if step == 0 else conv_acc[layer] + conv_term
            out_acc[layer] = out_term if step == 0 else out_acc[layer] + out_term
        low, inner, high = flowing
        flowing = jnp.concatenate([low, inner, high], axis=1)
        input_grads = flowing if step == 0 else input_grads + flowing
        if step + 1 < section_count:
            bf16 = jnp.bfloat16
            inner = shifted(inner.astype(bf16), "section", -1)
            edges = shifted(jnp.concatenate([low, high], axis=1).astype(bf16), "section", -1)
            width = low.shape[1]
            flowing = jnp.concatenate(
                [edges[:, :width], inner, edges[:, width:]], axis=1
            ).astype(jnp.float32)

    conv_rows = 3 * channels // seq_count
    out_rows = channels // seq_count
    conv_parts = []
    out_parts = []
    for layer in range(depth):
        conv_one = conv_acc[layer].reshape(seq_count, conv_rows, 2 * channels)
        out_one = out_acc[layer].reshape(seq_count, out_rows // 2, 2 * channels)
        (mine,) = halving_scatter([jnp.concatenate([conv_one, out_one], axis=1)])
        conv_parts.append(mine[:conv_rows])
        out_parts.append(mine[conv_rows:].reshape(out_rows, channels))
    conv_grads = jnp.stack(conv_parts)[None] * grad_scale
    out_grads = jnp.stack(out_parts)[None] * grad_scale
    return (input_grads[None], conv_grads, out_grads)


def solution(mesh):
    return jax.shard_map(
        shards,
        mesh=mesh,
        in_specs=(
            P("section", None, "seq", None),
            P(None, "seq", None),
            P("section", None, None, None, None),
            P("section", None, None, None),
        ),
        out_specs=(
            P("section", None, "seq", None),
            P("section", None, "seq", None),
            P("section", None, "seq", None),
        ),
        check_vma=False,
    )
```

```python
import math

import jax
import jax.numpy as jnp
from jax import lax
from jax.sharding import PartitionSpec as P

NEAR = 128
FAR = 1024


def shifted(value, axis, steps):
    count = lax.axis_size(axis)
    leading, last = (max(0, -steps), min(count, count - steps))
    return lax.ppermute(value, axis, [(source, source + steps) for source in range(leading, last)])


def halo_sides(block, width):
    rows = block.shape[1]
    from_low = shifted(block[:, rows - width :], "seq", 1)
    from_high = shifted(block[:, :width], "seq", -1)
    earlier = jnp.concatenate([from_low, block[:, : rows - width]], axis=1)
    following = jnp.concatenate([block[:, width:], from_high], axis=1)
    return earlier, following


def far_sides(block, hops):
    return shifted(block, "seq", hops), shifted(block, "seq", -hops)


def mm(a, b):
    return jnp.einsum("mpc,cd->mpd", a, b, preferred_element_type=jnp.float32)


def forward_layer(hidden, earlier, following, conv, out_mat, last):
    chans = hidden.shape[2]
    preact = mm(earlier, conv[0])
    preact = preact + mm(hidden, conv[1])
    preact = preact + mm(following, conv[2])
    tanh_part = jnp.tanh(preact[..., :chans])
    sig_part = jax.nn.sigmoid(preact[..., chans:])
    gated = (tanh_part * sig_part).astype(jnp.bfloat16)
    factor_a = (1.0 - tanh_part * tanh_part) * sig_part
    factor_b = tanh_part * sig_part * (1.0 - sig_part)
    taps = jnp.concatenate([earlier, hidden, following], axis=2)
    saved = (taps, gated, factor_a, factor_b)
    if last:
        return None, saved
    nxt = (hidden.astype(jnp.float32) + mm(gated, out_mat)).astype(jnp.bfloat16)
    return nxt, saved


def backward_layer(flowing, saved, conv, out_mat, layer, far_hops):
    taps, gated, factor_a, factor_b = saved
    chans = flowing.shape[2]
    grad_half = flowing.astype(jnp.bfloat16)
    out_term = jnp.einsum("mpc,mpd->cd", gated, grad_half, preferred_element_type=jnp.float32)
    grad_gated = jnp.einsum("mpd,cd->mpc", grad_half, out_mat, preferred_element_type=jnp.float32)
    grad_pre = jnp.concatenate([grad_gated * factor_a, grad_gated * factor_b], axis=2).astype(
        jnp.bfloat16
    )
    conv_term = jnp.einsum("mpc,mpd->cd", taps, grad_pre, preferred_element_type=jnp.float32)
    weights = conv.reshape(3 * chans, 2 * chans)
    back = jnp.einsum("mpd,cd->mpc", grad_pre, weights, preferred_element_type=jnp.float32)
    grad_first = back[..., :chans].astype(jnp.bfloat16)
    middle = back[..., chans : 2 * chans]
    grad_third = back[..., 2 * chans :].astype(jnp.bfloat16)
    if layer == 0:
        return split_near(flowing, middle, grad_first, grad_third, NEAR), conv_term, out_term
    else:
        third_earlier = shifted(grad_third, "seq", far_hops)
        first_following = shifted(grad_first, "seq", -far_hops)
    grad_conv = middle + first_following.astype(jnp.float32) + third_earlier.astype(jnp.float32)
    return flowing + grad_conv, conv_term, out_term


def split_near(flowing, middle, grad_first, grad_third, width):
    rows = grad_first.shape[1]
    low_in = shifted(grad_third[:, rows - width :], "seq", 1)
    high_in = shifted(grad_first[:, :width], "seq", -1)
    f32 = jnp.float32
    inner = flowing[:, width : rows - width] + (
        middle[:, width : rows - width]
        + grad_first[:, 2 * width :].astype(f32)
        + grad_third[:, : rows - 2 * width].astype(f32)
    )
    low = flowing[:, :width] + (
        middle[:, :width] + grad_first[:, width : 2 * width].astype(f32) + low_in.astype(f32)
    )
    high = flowing[:, rows - width :] + (
        middle[:, rows - width :]
        + high_in.astype(f32)
        + grad_third[:, rows - 2 * width : rows - width].astype(f32)
    )
    return low, inner, high


def halo_sides_pair(grad_first, grad_third, width):
    rows = grad_first.shape[1]
    from_low = shifted(grad_third[:, rows - width :], "seq", 1)
    from_high = shifted(grad_first[:, :width], "seq", -1)
    third_earlier = jnp.concatenate([from_low, grad_third[:, : rows - width]], axis=1)
    first_following = jnp.concatenate([grad_first[:, width:], from_high], axis=1)
    return third_earlier, first_following


def halving_scatter(parts, order):
    count = parts[0].shape[0]
    bits = count.bit_length() - 1
    rank = lax.axis_index("seq")
    parts = [p.reshape((2,) * bits + p.shape[1:]) for p in parts]
    left = list(reversed(range(bits)))
    for bit in order:
        axis = left.index(bit)
        left.pop(axis)
        own = ((rank >> bit) & 1) == 1
        pairs = [(j, j ^ (1 << bit)) for j in range(count)]
        lows = [lax.index_in_dim(p, 0, axis, keepdims=False) for p in parts]
        highs = [lax.index_in_dim(p, 1, axis, keepdims=False) for p in parts]
        sends = tuple(jnp.where(own, lo, hi).astype(jnp.bfloat16) for lo, hi in zip(lows, highs))
        got = lax.ppermute(sends, "seq", pairs)
        parts = [
            jnp.where(own, hi, lo) + g.astype(jnp.float32) for lo, hi, g in zip(lows, highs, got)
        ]
    return parts


def shards(section_inputs, cotangent, conv_weight, out_weight):
    batch_count = cotangent.shape[0]
    positions = cotangent.shape[1]
    channels = cotangent.shape[2]
    far_hops = FAR // positions
    seq_count = lax.axis_size("seq")
    section_count = lax.axis_size("section")
    section_rank = lax.axis_index("section")
    conv_mat = conv_weight[0]
    out_mat = out_weight[0]
    depth = conv_mat.shape[0]
    grad_scale = 1.0 / math.sqrt(batch_count * positions * seq_count)

    hidden = section_inputs[0]
    stored = []
    for layer in range(depth):
        if layer == 0:
            earlier, following = halo_sides(hidden, NEAR)
        else:
            earlier, following = far_sides(hidden, far_hops)
        hidden, saved = forward_layer(
            hidden, earlier, following, conv_mat[layer], out_mat[layer], layer + 1 == depth
        )
        stored.append(saved)

    top = jnp.where(section_rank == section_count - 1, 1.0, 0.0).astype(jnp.float32)
    flowing = cotangent.astype(jnp.float32) * top
    input_grads = None
    conv_acc = [None] * depth
    out_acc = [None] * depth
    for step in range(section_count):
        for layer in reversed(range(depth)):
            flowing, conv_term, out_term = backward_layer(
                flowing, stored[layer], conv_mat[layer], out_mat[layer], layer, far_hops
            )
            conv_acc[layer] = conv_term if step == 0 else conv_acc[layer] + conv_term
            out_acc[layer] = out_term if step == 0 else out_acc[layer] + out_term
        low, inner, high = flowing
        flowing = jnp.concatenate([low, inner, high], axis=1)
        input_grads = flowing if step == 0 else input_grads + flowing
        if step + 1 < section_count:
            bf16 = jnp.bfloat16
            inner = shifted(inner.astype(bf16), "section", -1)
            edges = shifted(jnp.concatenate([low, high], axis=1).astype(bf16), "section", -1)
            width = low.shape[1]
            flowing = jnp.concatenate(
                [edges[:, :width], inner, edges[:, width:]], axis=1
            ).astype(jnp.float32)

    conv_rows = 3 * channels // seq_count
    out_rows = channels // seq_count
    conv_all = jnp.concatenate(
        [acc.reshape(seq_count, conv_rows, 2 * channels) for acc in conv_acc], axis=1
    )
    out_all = jnp.concatenate(
        [acc.reshape(seq_count, out_rows, channels) for acc in out_acc], axis=1
    ).reshape(seq_count, depth * out_rows * channels // (2 * channels), 2 * channels)
    (mine,) = halving_scatter([jnp.concatenate([conv_all, out_all], axis=1)], (0, 1, 3, 2, 4))
    conv_grads = mine[: depth * conv_rows].reshape(1, depth, conv_rows, 2 * channels) * grad_scale
    out_grads = mine[depth * conv_rows :].reshape(1, depth, out_rows, channels) * grad_scale
    return (input_grads[None], conv_grads, out_grads)


def solution(mesh):
    return jax.shard_map(
        shards,
        mesh=mesh,
        in_specs=(
            P("section", None, "seq", None),
            P(None, "seq", None),
            P("section", None, None, None, None),
            P("section", None, None, None),
        ),
        out_specs=(
            P("section", None, "seq", None),
            P("section", None, "seq", None),
            P("section", None, "seq", None),
        ),
        check_vma=False,
    )
```

```python
import math

import jax
import jax.numpy as jnp
from jax import lax
from jax.sharding import PartitionSpec as P

NEAR = 128
FAR = 1024


def shifted(value, axis, steps):
    count = lax.axis_size(axis)
    leading, last = (max(0, -steps), min(count, count - steps))
    return lax.ppermute(value, axis, [(source, source + steps) for source in range(leading, last)])


def halo_sides(block, width):
    rows = block.shape[1]
    from_low = shifted(block[:, rows - width :], "seq", 1)
    from_high = shifted(block[:, :width], "seq", -1)
    earlier = jnp.concatenate([from_low, block[:, : rows - width]], axis=1)
    following = jnp.concatenate([block[:, width:], from_high], axis=1)
    return earlier, following


def far_sides(block, hops):
    return shifted(block, "seq", hops), shifted(block, "seq", -hops)


def mm(a, b):
    return jnp.einsum("mpc,cd->mpd", a, b, preferred_element_type=jnp.float32)


def forward_layer(hidden, earlier, following, conv, out_mat, last):
    chans = hidden.shape[2]
    preact = mm(earlier, conv[0])
    preact = preact + mm(hidden, conv[1])
    preact = preact + mm(following, conv[2])
    tanh_part = jnp.tanh(preact[..., :chans])
    sig_part = jax.nn.sigmoid(preact[..., chans:])
    gated = (tanh_part * sig_part).astype(jnp.bfloat16)
    factor_a = (1.0 - tanh_part * tanh_part) * sig_part
    factor_b = tanh_part * sig_part * (1.0 - sig_part)
    taps = jnp.concatenate([earlier, hidden, following], axis=2)
    saved = (taps, gated, factor_a, factor_b)
    if last:
        return None, saved
    nxt = (hidden.astype(jnp.float32) + mm(gated, out_mat)).astype(jnp.bfloat16)
    return nxt, saved


def backward_layer(flowing, saved, conv, out_mat, layer, far_hops):
    taps, gated, factor_a, factor_b = saved
    chans = flowing.shape[2]
    grad_half = flowing.astype(jnp.bfloat16)
    grad_gated = jnp.einsum("mpd,cd->mpc", grad_half, out_mat, preferred_element_type=jnp.float32)
    grad_pre = jnp.concatenate([grad_gated * factor_a, grad_gated * factor_b], axis=2).astype(
        jnp.bfloat16
    )
    weights = conv.reshape(3 * chans, 2 * chans)
    back = jnp.einsum("mpd,cd->mpc", grad_pre, weights, preferred_element_type=jnp.float32)
    grad_first = back[..., :chans].astype(jnp.bfloat16)
    middle = back[..., chans : 2 * chans]
    grad_third = back[..., 2 * chans :].astype(jnp.bfloat16)
    if layer == 0:
        return split_near(flowing, middle, grad_first, grad_third, NEAR), grad_pre, grad_half
    else:
        third_earlier = shifted(grad_third, "seq", far_hops)
        first_following = shifted(grad_first, "seq", -far_hops)
    grad_conv = middle + first_following.astype(jnp.float32) + third_earlier.astype(jnp.float32)
    return flowing + grad_conv, grad_pre, grad_half


def split_near(flowing, middle, grad_first, grad_third, width):
    rows = grad_first.shape[1]
    low_in = shifted(grad_third[:, rows - width :], "seq", 1)
    high_in = shifted(grad_first[:, :width], "seq", -1)
    f32 = jnp.float32
    inner = flowing[:, width : rows - width] + (
        middle[:, width : rows - width]
        + grad_first[:, 2 * width :].astype(f32)
        + grad_third[:, : rows - 2 * width].astype(f32)
    )
    low = flowing[:, :width] + (
        middle[:, :width] + grad_first[:, width : 2 * width].astype(f32) + low_in.astype(f32)
    )
    high = flowing[:, rows - width :] + (
        middle[:, rows - width :]
        + high_in.astype(f32)
        + grad_third[:, rows - 2 * width : rows - width].astype(f32)
    )
    return low, inner, high


def halo_sides_pair(grad_first, grad_third, width):
    rows = grad_first.shape[1]
    from_low = shifted(grad_third[:, rows - width :], "seq", 1)
    from_high = shifted(grad_first[:, :width], "seq", -1)
    third_earlier = jnp.concatenate([from_low, grad_third[:, : rows - width]], axis=1)
    first_following = jnp.concatenate([grad_first[:, width:], from_high], axis=1)
    return third_earlier, first_following


def halving_scatter(parts, order):
    count = parts[0].shape[0]
    bits = count.bit_length() - 1
    rank = lax.axis_index("seq")
    parts = [p.reshape((2,) * bits + p.shape[1:]) for p in parts]
    left = list(reversed(range(bits)))
    for bit in order:
        axis = left.index(bit)
        left.pop(axis)
        own = ((rank >> bit) & 1) == 1
        pairs = [(j, j ^ (1 << bit)) for j in range(count)]
        lows = [lax.index_in_dim(p, 0, axis, keepdims=False) for p in parts]
        highs = [lax.index_in_dim(p, 1, axis, keepdims=False) for p in parts]
        sends = tuple(jnp.where(own, lo, hi).astype(jnp.bfloat16) for lo, hi in zip(lows, highs))
        got = lax.ppermute(sends, "seq", pairs)
        parts = [
            jnp.where(own, hi, lo) + g.astype(jnp.float32) for lo, hi, g in zip(lows, highs, got)
        ]
    return parts


def shards(section_inputs, cotangent, conv_weight, out_weight):
    batch_count = cotangent.shape[0]
    positions = cotangent.shape[1]
    channels = cotangent.shape[2]
    far_hops = FAR // positions
    seq_count = lax.axis_size("seq")
    section_count = lax.axis_size("section")
    section_rank = lax.axis_index("section")
    conv_mat = conv_weight[0]
    out_mat = out_weight[0]
    depth = conv_mat.shape[0]
    grad_scale = 1.0 / math.sqrt(batch_count * positions * seq_count)

    hidden = section_inputs[0]
    stored = []
    for layer in range(depth):
        if layer == 0:
            earlier, following = halo_sides(hidden, NEAR)
        else:
            earlier, following = far_sides(hidden, far_hops)
        hidden, saved = forward_layer(
            hidden, earlier, following, conv_mat[layer], out_mat[layer], layer + 1 == depth
        )
        stored.append(saved)

    top = jnp.where(section_rank == section_count - 1, 1.0, 0.0).astype(jnp.float32)
    flowing = cotangent.astype(jnp.float32) * top
    input_grads = None
    conv_acc = [None] * depth
    out_acc = [None] * depth
    for step in range(section_count):
        for layer in reversed(range(depth)):
            flowing, grad_pre, grad_half = backward_layer(
                flowing, stored[layer], conv_mat[layer], out_mat[layer], layer, far_hops
            )
            conv_acc[layer] = grad_pre if step == 0 else conv_acc[layer] + grad_pre
            out_acc[layer] = grad_half if step == 0 else out_acc[layer] + grad_half
        low, inner, high = flowing
        flowing = jnp.concatenate([low, inner, high], axis=1)
        input_grads = flowing if step == 0 else input_grads + flowing
        if step + 1 < section_count:
            bf16 = jnp.bfloat16
            inner = shifted(inner.astype(bf16), "section", -1)
            edges = shifted(jnp.concatenate([low, high], axis=1).astype(bf16), "section", -1)
            width = low.shape[1]
            flowing = jnp.concatenate(
                [edges[:, :width], inner, edges[:, width:]], axis=1
            ).astype(jnp.float32)

    f32 = jnp.float32
    for layer in range(depth):
        taps, gated = stored[layer][0], stored[layer][1]
        conv_acc[layer] = jnp.einsum("mpc,mpd->cd", taps, conv_acc[layer], preferred_element_type=f32)
        out_acc[layer] = jnp.einsum("mpc,mpd->cd", gated, out_acc[layer], preferred_element_type=f32)
    conv_rows = 3 * channels // seq_count
    out_rows = channels // seq_count
    conv_all = jnp.concatenate(
        [acc.reshape(seq_count, conv_rows, 2 * channels) for acc in conv_acc], axis=1
    )
    out_all = jnp.concatenate(
        [acc.reshape(seq_count, out_rows, channels) for acc in out_acc], axis=1
    ).reshape(seq_count, depth * out_rows * channels // (2 * channels), 2 * channels)
    (mine,) = halving_scatter([jnp.concatenate([conv_all, out_all], axis=1)], (0, 1, 3, 2, 4))
    conv_grads = mine[: depth * conv_rows].reshape(1, depth, conv_rows, 2 * channels) * grad_scale
    out_grads = mine[depth * conv_rows :].reshape(1, depth, out_rows, channels) * grad_scale
    return (input_grads[None], conv_grads, out_grads)


def solution(mesh):
    return jax.shard_map(
        shards,
        mesh=mesh,
        in_specs=(
            P("section", None, "seq", None),
            P(None, "seq", None),
            P("section", None, None, None, None),
            P("section", None, None, None),
        ),
        out_specs=(
            P("section", None, "seq", None),
            P("section", None, "seq", None),
            P("section", None, "seq", None),
        ),
        check_vma=False,
    )
```

```python
import math

import jax
import jax.numpy as jnp
from jax import lax
from jax.sharding import PartitionSpec as P

NEAR = 128
FAR = 1024


def shifted(value, axis, steps):
    count = lax.axis_size(axis)
    leading, last = (max(0, -steps), min(count, count - steps))
    return lax.ppermute(value, axis, [(source, source + steps) for source in range(leading, last)])


def halo_sides(block, width):
    rows = block.shape[1]
    from_low = shifted(block[:, rows - width :], "seq", 1)
    from_high = shifted(block[:, :width], "seq", -1)
    earlier = jnp.concatenate([from_low, block[:, : rows - width]], axis=1)
    following = jnp.concatenate([block[:, width:], from_high], axis=1)
    return earlier, following


def far_sides(block, hops):
    return shifted(block, "seq", hops), shifted(block, "seq", -hops)


def mm(a, b):
    return jnp.einsum("mpc,cd->mpd", a, b, preferred_element_type=jnp.float32)


def forward_layer(hidden, earlier, following, conv, out_mat, last):
    chans = hidden.shape[2]
    preact = mm(earlier, conv[0])
    preact = preact + mm(hidden, conv[1])
    preact = preact + mm(following, conv[2])
    tanh_part = jnp.tanh(preact[..., :chans])
    sig_part = jax.nn.sigmoid(preact[..., chans:])
    gated = (tanh_part * sig_part).astype(jnp.bfloat16)
    factor_a = (1.0 - tanh_part * tanh_part) * sig_part
    factor_b = tanh_part * sig_part * (1.0 - sig_part)
    taps = jnp.concatenate([earlier, hidden, following], axis=2)
    saved = (taps, gated, factor_a, factor_b)
    if last:
        return None, saved
    nxt = (hidden.astype(jnp.float32) + mm(gated, out_mat)).astype(jnp.bfloat16)
    return nxt, saved


def backward_layer(flowing, saved, conv, out_mat, layer, far_hops):
    taps, gated, factor_a, factor_b = saved
    chans = flowing.shape[2]
    grad_half = flowing.astype(jnp.bfloat16)
    out_term = jnp.einsum("mpc,mpd->cd", gated, grad_half, preferred_element_type=jnp.float32)
    grad_gated = jnp.einsum("mpd,cd->mpc", grad_half, out_mat, preferred_element_type=jnp.float32)
    grad_pre = jnp.concatenate([grad_gated * factor_a, grad_gated * factor_b], axis=2).astype(
        jnp.bfloat16
    )
    conv_term = jnp.einsum("mpc,mpd->cd", taps, grad_pre, preferred_element_type=jnp.float32)
    weights = conv.reshape(3 * chans, 2 * chans)
    back = jnp.einsum("mpd,cd->mpc", grad_pre, weights, preferred_element_type=jnp.float32)
    grad_first = back[..., :chans].astype(jnp.bfloat16)
    middle = back[..., chans : 2 * chans]
    grad_third = back[..., 2 * chans :].astype(jnp.bfloat16)
    if layer == 0:
        return split_near(flowing, middle, grad_first, grad_third, NEAR), conv_term, out_term
    else:
        third_earlier = shifted(grad_third, "seq", far_hops)
        first_following = shifted(grad_first, "seq", -far_hops)
    grad_conv = middle + first_following.astype(jnp.float32) + third_earlier.astype(jnp.float32)
    return flowing + grad_conv, conv_term, out_term


def split_rows(value, width):
    return jnp.concatenate([value[:, :width], value[:, -width:]], axis=1), value[:, width:-width]


def join_rows(edges, inner, width):
    return jnp.concatenate([edges[:, :width], inner, edges[:, width:]], axis=1)


def backward_far(pieces, saved, conv, out_mat, far_hops):
    taps, gated, factor_a, factor_b = saved
    chans = pieces[0].shape[2]
    width = NEAR
    weights = conv.reshape(3 * chans, 2 * chans)
    f32 = jnp.float32
    factors = [split_rows(factor_a, width), split_rows(factor_b, width)]
    outs, pres, halves = [], [], []
    for index, flowing in enumerate(pieces):
        grad_half = flowing.astype(jnp.bfloat16)
        grad_gated = jnp.einsum("mpd,cd->mpc", grad_half, out_mat, preferred_element_type=f32)
        grad_pre = jnp.concatenate(
            [grad_gated * factors[0][index], grad_gated * factors[1][index]], axis=2
        ).astype(jnp.bfloat16)
        back = jnp.einsum("mpd,cd->mpc", grad_pre, weights, preferred_element_type=f32)
        grad_first = back[..., :chans].astype(jnp.bfloat16)
        middle = back[..., chans : 2 * chans]
        grad_third = back[..., 2 * chans :].astype(jnp.bfloat16)
        third_earlier = shifted(grad_third, "seq", far_hops)
        first_following = shifted(grad_first, "seq", -far_hops)
        outs.append(flowing + (middle + first_following.astype(f32) + third_earlier.astype(f32)))
        pres.append(grad_pre)
        halves.append(grad_half)
    grad_pre = join_rows(pres[0], pres[1], width)
    grad_half = join_rows(halves[0], halves[1], width)
    out_term = jnp.einsum("mpc,mpd->cd", gated, grad_half, preferred_element_type=f32)
    conv_term = jnp.einsum("mpc,mpd->cd", taps, grad_pre, preferred_element_type=f32)
    return join_rows(outs[0], outs[1], width), conv_term, out_term


def split_near(flowing, middle, grad_first, grad_third, width):
    rows = grad_first.shape[1]
    low_in = shifted(grad_third[:, rows - width :], "seq", 1)
    high_in = shifted(grad_first[:, :width], "seq", -1)
    f32 = jnp.float32
    inner = flowing[:, width : rows - width] + (
        middle[:, width : rows - width]
        + grad_first[:, 2 * width :].astype(f32)
        + grad_third[:, : rows - 2 * width].astype(f32)
    )
    low = flowing[:, :width] + (
        middle[:, :width] + grad_first[:, width : 2 * width].astype(f32) + low_in.astype(f32)
    )
    high = flowing[:, rows - width :] + (
        middle[:, rows - width :]
        + high_in.astype(f32)
        + grad_third[:, rows - 2 * width : rows - width].astype(f32)
    )
    return low, inner, high


def halo_sides_pair(grad_first, grad_third, width):
    rows = grad_first.shape[1]
    from_low = shifted(grad_third[:, rows - width :], "seq", 1)
    from_high = shifted(grad_first[:, :width], "seq", -1)
    third_earlier = jnp.concatenate([from_low, grad_third[:, : rows - width]], axis=1)
    first_following = jnp.concatenate([grad_first[:, width:], from_high], axis=1)
    return third_earlier, first_following


def halving_scatter(parts, order):
    count = parts[0].shape[0]
    bits = count.bit_length() - 1
    rank = lax.axis_index("seq")
    parts = [p.reshape((2,) * bits + p.shape[1:]) for p in parts]
    left = list(reversed(range(bits)))
    for bit in order:
        axis = left.index(bit)
        left.pop(axis)
        own = ((rank >> bit) & 1) == 1
        pairs = [(j, j ^ (1 << bit)) for j in range(count)]
        lows = [lax.index_in_dim(p, 0, axis, keepdims=False) for p in parts]
        highs = [lax.index_in_dim(p, 1, axis, keepdims=False) for p in parts]
        sends = tuple(jnp.where(own, lo, hi).astype(jnp.bfloat16) for lo, hi in zip(lows, highs))
        got = lax.ppermute(sends, "seq", pairs)
        parts = [
            jnp.where(own, hi, lo) + g.astype(jnp.float32) for lo, hi, g in zip(lows, highs, got)
        ]
    return parts


def shards(section_inputs, cotangent, conv_weight, out_weight):
    batch_count = cotangent.shape[0]
    positions = cotangent.shape[1]
    channels = cotangent.shape[2]
    far_hops = FAR // positions
    seq_count = lax.axis_size("seq")
    section_count = lax.axis_size("section")
    section_rank = lax.axis_index("section")
    conv_mat = conv_weight[0]
    out_mat = out_weight[0]
    depth = conv_mat.shape[0]
    grad_scale = 1.0 / math.sqrt(batch_count * positions * seq_count)

    hidden = section_inputs[0]
    stored = []
    for layer in range(depth):
        if layer == 0:
            earlier, following = halo_sides(hidden, NEAR)
        else:
            earlier, following = far_sides(hidden, far_hops)
        hidden, saved = forward_layer(
            hidden, earlier, following, conv_mat[layer], out_mat[layer], layer + 1 == depth
        )
        stored.append(saved)

    top = jnp.where(section_rank == section_count - 1, 1.0, 0.0).astype(jnp.float32)
    flowing = split_rows(cotangent.astype(jnp.float32) * top, NEAR)
    input_grads = None
    conv_acc = [None] * depth
    out_acc = [None] * depth
    for step in range(section_count):
        for layer in reversed(range(depth)):
            if layer == depth - 1:
                flowing, conv_term, out_term = backward_far(
                    flowing, stored[layer], conv_mat[layer], out_mat[layer], far_hops
                )
            else:
                flowing, conv_term, out_term = backward_layer(
                    flowing, stored[layer], conv_mat[layer], out_mat[layer], layer, far_hops
                )
            conv_acc[layer] = conv_term if step == 0 else conv_acc[layer] + conv_term
            out_acc[layer] = out_term if step == 0 else out_acc[layer] + out_term
        low, inner, high = flowing
        flowing = jnp.concatenate([low, inner, high], axis=1)
        input_grads = flowing if step == 0 else input_grads + flowing
        if step + 1 < section_count:
            bf16 = jnp.bfloat16
            inner = shifted(inner.astype(bf16), "section", -1)
            edges = shifted(jnp.concatenate([low, high], axis=1).astype(bf16), "section", -1)
            flowing = (edges.astype(jnp.float32), inner.astype(jnp.float32))

    conv_rows = 3 * channels // seq_count
    out_rows = channels // seq_count
    conv_all = jnp.concatenate(
        [acc.reshape(seq_count, conv_rows, 2 * channels) for acc in conv_acc], axis=1
    )
    out_all = jnp.concatenate(
        [acc.reshape(seq_count, out_rows, channels) for acc in out_acc], axis=1
    ).reshape(seq_count, depth * out_rows * channels // (2 * channels), 2 * channels)
    (mine,) = halving_scatter([jnp.concatenate([conv_all, out_all], axis=1)], (0, 1, 3, 2, 4))
    conv_grads = mine[: depth * conv_rows].reshape(1, depth, conv_rows, 2 * channels) * grad_scale
    out_grads = mine[depth * conv_rows :].reshape(1, depth, out_rows, channels) * grad_scale
    return (input_grads[None], conv_grads, out_grads)


def solution(mesh):
    return jax.shard_map(
        shards,
        mesh=mesh,
        in_specs=(
            P("section", None, "seq", None),
            P(None, "seq", None),
            P("section", None, None, None, None),
            P("section", None, None, None),
        ),
        out_specs=(
            P("section", None, "seq", None),
            P("section", None, "seq", None),
            P("section", None, "seq", None),
        ),
        check_vma=False,
    )
```

```python
import math

import jax
import jax.numpy as jnp
from jax import lax
from jax.sharding import PartitionSpec as P

NEAR = 128
FAR = 1024


def shifted(value, axis, steps):
    count = lax.axis_size(axis)
    leading, last = (max(0, -steps), min(count, count - steps))
    return lax.ppermute(value, axis, [(source, source + steps) for source in range(leading, last)])


def halo_sides(block, width):
    rows = block.shape[1]
    from_low = shifted(block[:, rows - width :], "seq", 1)
    from_high = shifted(block[:, :width], "seq", -1)
    earlier = jnp.concatenate([from_low, block[:, : rows - width]], axis=1)
    following = jnp.concatenate([block[:, width:], from_high], axis=1)
    return earlier, following


def far_sides(block, hops):
    return shifted(block, "seq", hops), shifted(block, "seq", -hops)


def mm(a, b):
    return jnp.einsum("mpc,cd->mpd", a, b, preferred_element_type=jnp.float32)


def forward_layer(hidden, earlier, following, conv, out_mat, last):
    chans = hidden.shape[2]
    preact = mm(earlier, conv[0])
    preact = preact + mm(hidden, conv[1])
    preact = preact + mm(following, conv[2])
    tanh_part = jnp.tanh(preact[..., :chans])
    sig_part = jax.nn.sigmoid(preact[..., chans:])
    gated = (tanh_part * sig_part).astype(jnp.bfloat16)
    factor_a = (1.0 - tanh_part * tanh_part) * sig_part
    factor_b = tanh_part * sig_part * (1.0 - sig_part)
    taps = jnp.concatenate([earlier, hidden, following], axis=2)
    saved = (taps, gated, factor_a, factor_b)
    if last:
        return None, saved
    nxt = (hidden.astype(jnp.float32) + mm(gated, out_mat)).astype(jnp.bfloat16)
    return nxt, saved


def backward_layer(flowing, saved, conv, out_mat, layer, far_hops):
    taps, gated, factor_a, factor_b = saved
    chans = flowing.shape[2]
    grad_half = flowing.astype(jnp.bfloat16)
    out_term = jnp.einsum("mpc,mpd->cd", gated, grad_half, preferred_element_type=jnp.float32)
    grad_gated = jnp.einsum("mpd,cd->mpc", grad_half, out_mat, preferred_element_type=jnp.float32)
    grad_pre = jnp.concatenate([grad_gated * factor_a, grad_gated * factor_b], axis=2).astype(
        jnp.bfloat16
    )
    conv_term = jnp.einsum("mpc,mpd->cd", taps, grad_pre, preferred_element_type=jnp.float32)
    weights = conv.reshape(3 * chans, 2 * chans)
    back = jnp.einsum("mpd,cd->mpc", grad_pre, weights, preferred_element_type=jnp.float32)
    grad_first = back[..., :chans].astype(jnp.bfloat16)
    middle = back[..., chans : 2 * chans]
    grad_third = back[..., 2 * chans :].astype(jnp.bfloat16)
    if layer == 0:
        return split_near(flowing, middle, grad_first, grad_third, NEAR), conv_term, out_term
    else:
        third_earlier = shifted(grad_third, "seq", far_hops)
        first_following = shifted(grad_first, "seq", -far_hops)
    grad_conv = middle + first_following.astype(jnp.float32) + third_earlier.astype(jnp.float32)
    return flowing + grad_conv, conv_term, out_term


def split_rows(value, width):
    return jnp.concatenate([value[:, :width], value[:, -width:]], axis=1), value[:, width:-width]


def join_rows(edges, inner, width):
    return jnp.concatenate([edges[:, :width], inner, edges[:, width:]], axis=1)


def backward_far(pieces, saved, conv, out_mat, far_hops):
    taps, gated, factor_a, factor_b = saved
    chans = pieces[0].shape[2]
    width = NEAR
    weights = conv.reshape(3 * chans, 2 * chans)
    f32 = jnp.float32
    factors = [split_rows(factor_a, width), split_rows(factor_b, width)]
    outs, pres, halves = [], [], []
    for index, flowing in enumerate(pieces):
        grad_half = flowing.astype(jnp.bfloat16)
        grad_gated = jnp.einsum("mpd,cd->mpc", grad_half, out_mat, preferred_element_type=f32)
        grad_pre = jnp.concatenate(
            [grad_gated * factors[0][index], grad_gated * factors[1][index]], axis=2
        ).astype(jnp.bfloat16)
        back = jnp.einsum("mpd,cd->mpc", grad_pre, weights, preferred_element_type=f32)
        grad_first = back[..., :chans].astype(jnp.bfloat16)
        middle = back[..., chans : 2 * chans]
        grad_third = back[..., 2 * chans :].astype(jnp.bfloat16)
        third_earlier = shifted(grad_third, "seq", far_hops)
        first_following = shifted(grad_first, "seq", -far_hops)
        outs.append(flowing + (middle + first_following.astype(f32) + third_earlier.astype(f32)))
        pres.append(grad_pre)
        halves.append(grad_half)
    grad_pre = join_rows(pres[0], pres[1], width)
    grad_half = join_rows(halves[0], halves[1], width)
    out_term = jnp.einsum("mpc,mpd->cd", gated, grad_half, preferred_element_type=f32)
    conv_term = jnp.einsum("mpc,mpd->cd", taps, grad_pre, preferred_element_type=f32)
    return join_rows(outs[0], outs[1], width), conv_term, out_term


def split_near(flowing, middle, grad_first, grad_third, width):
    rows = grad_first.shape[1]
    low_in = shifted(grad_third[:, rows - width :], "seq", 1)
    high_in = shifted(grad_first[:, :width], "seq", -1)
    f32 = jnp.float32
    inner = flowing[:, width : rows - width] + (
        middle[:, width : rows - width]
        + grad_first[:, 2 * width :].astype(f32)
        + grad_third[:, : rows - 2 * width].astype(f32)
    )
    low = flowing[:, :width] + (
        middle[:, :width] + grad_first[:, width : 2 * width].astype(f32) + low_in.astype(f32)
    )
    high = flowing[:, rows - width :] + (
        middle[:, rows - width :]
        + high_in.astype(f32)
        + grad_third[:, rows - 2 * width : rows - width].astype(f32)
    )
    return low, inner, high


def halo_sides_pair(grad_first, grad_third, width):
    rows = grad_first.shape[1]
    from_low = shifted(grad_third[:, rows - width :], "seq", 1)
    from_high = shifted(grad_first[:, :width], "seq", -1)
    third_earlier = jnp.concatenate([from_low, grad_third[:, : rows - width]], axis=1)
    first_following = jnp.concatenate([grad_first[:, width:], from_high], axis=1)
    return third_earlier, first_following


def halving_scatter(parts, order):
    count = parts[0].shape[0]
    bits = count.bit_length() - 1
    rank = lax.axis_index("seq")
    parts = [p.reshape((2,) * bits + p.shape[1:]) for p in parts]
    left = list(reversed(range(bits)))
    for bit in order:
        axis = left.index(bit)
        left.pop(axis)
        own = ((rank >> bit) & 1) == 1
        pairs = [(j, j ^ (1 << bit)) for j in range(count)]
        lows = [lax.index_in_dim(p, 0, axis, keepdims=False) for p in parts]
        highs = [lax.index_in_dim(p, 1, axis, keepdims=False) for p in parts]
        sends = tuple(jnp.where(own, lo, hi).astype(jnp.bfloat16) for lo, hi in zip(lows, highs))
        got = lax.ppermute(sends, "seq", pairs)
        parts = [
            jnp.where(own, hi, lo) + g.astype(jnp.float32) for lo, hi, g in zip(lows, highs, got)
        ]
    return parts


def shards(section_inputs, cotangent, conv_weight, out_weight):
    batch_count = cotangent.shape[0]
    positions = cotangent.shape[1]
    channels = cotangent.shape[2]
    far_hops = FAR // positions
    seq_count = lax.axis_size("seq")
    section_count = lax.axis_size("section")
    section_rank = lax.axis_index("section")
    conv_mat = conv_weight[0]
    out_mat = out_weight[0]
    depth = conv_mat.shape[0]
    grad_scale = 1.0 / math.sqrt(batch_count * positions * seq_count)

    hidden = section_inputs[0]
    width = NEAR
    rows = hidden.shape[1]
    from_low = shifted(hidden[:, rows - width :], "seq", 1)
    from_high = shifted(hidden[:, :width], "seq", -1)
    edge_parts = (
        jnp.concatenate([from_low, hidden[:, rows - 2 * width : rows - width]], axis=1),
        jnp.concatenate([hidden[:, :width], hidden[:, rows - width :]], axis=1),
        jnp.concatenate([hidden[:, width : 2 * width], from_high], axis=1),
    )
    inner_parts = (
        hidden[:, : rows - 2 * width],
        hidden[:, width : rows - width],
        hidden[:, 2 * width :],
    )
    pieces = []
    for earlier, middle_rows, following in (edge_parts, inner_parts):
        pieces.append(
            forward_layer(middle_rows, earlier, following, conv_mat[0], out_mat[0], False)
        )
    saved0 = tuple(join_rows(e, i, width) for e, i in zip(pieces[0][1], pieces[1][1]))
    stored = [saved0]
    nxt = [p[0] for p in pieces]
    earlier = join_rows(*[shifted(v, "seq", far_hops) for v in nxt], width)
    following = join_rows(*[shifted(v, "seq", -far_hops) for v in nxt], width)
    hidden = join_rows(nxt[0], nxt[1], width)
    for layer in range(1, depth):
        if layer > 1:
            earlier, following = far_sides(hidden, far_hops)
        hidden, saved = forward_layer(
            hidden, earlier, following, conv_mat[layer], out_mat[layer], layer + 1 == depth
        )
        stored.append(saved)

    top = jnp.where(section_rank == section_count - 1, 1.0, 0.0).astype(jnp.float32)
    flowing = split_rows(cotangent.astype(jnp.float32) * top, NEAR)
    input_grads = None
    conv_acc = [None] * depth
    out_acc = [None] * depth
    for step in range(section_count):
        for layer in reversed(range(depth)):
            if layer == depth - 1:
                flowing, conv_term, out_term = backward_far(
                    flowing, stored[layer], conv_mat[layer], out_mat[layer], far_hops
                )
            else:
                flowing, conv_term, out_term = backward_layer(
                    flowing, stored[layer], conv_mat[layer], out_mat[layer], layer, far_hops
                )
            conv_acc[layer] = conv_term if step == 0 else conv_acc[layer] + conv_term
            out_acc[layer] = out_term if step == 0 else out_acc[layer] + out_term
        low, inner, high = flowing
        flowing = jnp.concatenate([low, inner, high], axis=1)
        input_grads = flowing if step == 0 else input_grads + flowing
        if step + 1 < section_count:
            bf16 = jnp.bfloat16
            inner = shifted(inner.astype(bf16), "section", -1)
            edges = shifted(jnp.concatenate([low, high], axis=1).astype(bf16), "section", -1)
            flowing = (edges.astype(jnp.float32), inner.astype(jnp.float32))

    conv_rows = 3 * channels // seq_count
    out_rows = channels // seq_count
    conv_all = jnp.concatenate(
        [acc.reshape(seq_count, conv_rows, 2 * channels) for acc in conv_acc], axis=1
    )
    out_all = jnp.concatenate(
        [acc.reshape(seq_count, out_rows, channels) for acc in out_acc], axis=1
    ).reshape(seq_count, depth * out_rows * channels // (2 * channels), 2 * channels)
    (mine,) = halving_scatter([jnp.concatenate([conv_all, out_all], axis=1)], (0, 1, 3, 2, 4))
    conv_grads = mine[: depth * conv_rows].reshape(1, depth, conv_rows, 2 * channels) * grad_scale
    out_grads = mine[depth * conv_rows :].reshape(1, depth, out_rows, channels) * grad_scale
    return (input_grads[None], conv_grads, out_grads)


def solution(mesh):
    return jax.shard_map(
        shards,
        mesh=mesh,
        in_specs=(
            P("section", None, "seq", None),
            P(None, "seq", None),
            P("section", None, None, None, None),
            P("section", None, None, None),
        ),
        out_specs=(
            P("section", None, "seq", None),
            P("section", None, "seq", None),
            P("section", None, "seq", None),
        ),
        check_vma=False,
    )
```

```python
import math

import jax
import jax.numpy as jnp
from jax import lax
from jax.sharding import PartitionSpec as P

NEAR = 128
FAR = 1024


def shifted(value, axis, steps):
    count = lax.axis_size(axis)
    leading, last = (max(0, -steps), min(count, count - steps))
    return lax.ppermute(value, axis, [(source, source + steps) for source in range(leading, last)])


def halo_sides(block, width):
    rows = block.shape[1]
    from_low = shifted(block[:, rows - width :], "seq", 1)
    from_high = shifted(block[:, :width], "seq", -1)
    earlier = jnp.concatenate([from_low, block[:, : rows - width]], axis=1)
    following = jnp.concatenate([block[:, width:], from_high], axis=1)
    return earlier, following


def far_sides(block, hops):
    return shifted(block, "seq", hops), shifted(block, "seq", -hops)


def mm(a, b):
    return jnp.einsum("mpc,cd->mpd", a, b, preferred_element_type=jnp.float32)


def forward_layer(hidden, earlier, following, conv, out_mat, last):
    chans = hidden.shape[2]
    preact = mm(earlier, conv[0])
    preact = preact + mm(hidden, conv[1])
    preact = preact + mm(following, conv[2])
    tanh_part = jnp.tanh(preact[..., :chans])
    sig_part = jax.nn.sigmoid(preact[..., chans:])
    gated = (tanh_part * sig_part).astype(jnp.bfloat16)
    factor_a = (1.0 - tanh_part * tanh_part) * sig_part
    factor_b = tanh_part * sig_part * (1.0 - sig_part)
    taps = jnp.concatenate([earlier, hidden, following], axis=2)
    saved = (taps, gated, factor_a, factor_b)
    if last:
        return None, saved
    nxt = (hidden.astype(jnp.float32) + mm(gated, out_mat)).astype(jnp.bfloat16)
    return nxt, saved


def backward_layer(flowing, saved, conv, out_mat, layer, far_hops):
    taps, gated, factor_a, factor_b = saved
    chans = flowing.shape[2]
    grad_half = flowing.astype(jnp.bfloat16)
    out_term = jnp.einsum("mpc,mpd->cd", gated, grad_half, preferred_element_type=jnp.float32)
    grad_gated = jnp.einsum("mpd,cd->mpc", grad_half, out_mat, preferred_element_type=jnp.float32)
    grad_pre = jnp.concatenate([grad_gated * factor_a, grad_gated * factor_b], axis=2).astype(
        jnp.bfloat16
    )
    conv_term = jnp.einsum("mpc,mpd->cd", taps, grad_pre, preferred_element_type=jnp.float32)
    weights = conv.reshape(3 * chans, 2 * chans)
    back = jnp.einsum("mpd,cd->mpc", grad_pre, weights, preferred_element_type=jnp.float32)
    grad_first = back[..., :chans].astype(jnp.bfloat16)
    middle = back[..., chans : 2 * chans]
    grad_third = back[..., 2 * chans :].astype(jnp.bfloat16)
    if layer == 0:
        return split_near(flowing, middle, grad_first, grad_third, NEAR), conv_term, out_term
    else:
        third_earlier = shifted(grad_third, "seq", far_hops)
        first_following = shifted(grad_first, "seq", -far_hops)
    grad_conv = middle + first_following.astype(jnp.float32) + third_earlier.astype(jnp.float32)
    return flowing + grad_conv, conv_term, out_term


def split_rows(value, width):
    return jnp.concatenate([value[:, :width], value[:, -width:]], axis=1), value[:, width:-width]


def join_rows(edges, inner, width):
    return jnp.concatenate([edges[:, :width], inner, edges[:, width:]], axis=1)


def backward_far(pieces, saved, conv, out_mat, far_hops):
    taps, gated, factor_a, factor_b = saved
    chans = pieces[0].shape[2]
    width = NEAR
    weights = conv.reshape(3 * chans, 2 * chans)
    f32 = jnp.float32
    factors = [split_rows(factor_a, width), split_rows(factor_b, width)]
    outs, pres, halves = [], [], []
    for index, flowing in enumerate(pieces):
        grad_half = flowing.astype(jnp.bfloat16)
        grad_gated = jnp.einsum("mpd,cd->mpc", grad_half, out_mat, preferred_element_type=f32)
        grad_pre = jnp.concatenate(
            [grad_gated * factors[0][index], grad_gated * factors[1][index]], axis=2
        ).astype(jnp.bfloat16)
        back = jnp.einsum("mpd,cd->mpc", grad_pre, weights, preferred_element_type=f32)
        grad_first = back[..., :chans].astype(jnp.bfloat16)
        middle = back[..., chans : 2 * chans]
        grad_third = back[..., 2 * chans :].astype(jnp.bfloat16)
        third_earlier = shifted(grad_third, "seq", far_hops)
        first_following = shifted(grad_first, "seq", -far_hops)
        outs.append(flowing + (middle + first_following.astype(f32) + third_earlier.astype(f32)))
        pres.append(grad_pre)
        halves.append(grad_half)
    grad_pre = join_rows(pres[0], pres[1], width)
    grad_half = join_rows(halves[0], halves[1], width)
    out_term = jnp.einsum("mpc,mpd->cd", gated, grad_half, preferred_element_type=f32)
    conv_term = jnp.einsum("mpc,mpd->cd", taps, grad_pre, preferred_element_type=f32)
    return join_rows(outs[0], outs[1], width), conv_term, out_term


def split_near(flowing, middle, grad_first, grad_third, width):
    rows = grad_first.shape[1]
    low_in = shifted(grad_third[:, rows - width :], "seq", 1)
    high_in = shifted(grad_first[:, :width], "seq", -1)
    f32 = jnp.float32
    inner = flowing[:, width : rows - width] + (
        middle[:, width : rows - width]
        + grad_first[:, 2 * width :].astype(f32)
        + grad_third[:, : rows - 2 * width].astype(f32)
    )
    low = flowing[:, :width] + (
        middle[:, :width] + grad_first[:, width : 2 * width].astype(f32) + low_in.astype(f32)
    )
    high = flowing[:, rows - width :] + (
        middle[:, rows - width :]
        + high_in.astype(f32)
        + grad_third[:, rows - 2 * width : rows - width].astype(f32)
    )
    return low, inner, high


def halo_sides_pair(grad_first, grad_third, width):
    rows = grad_first.shape[1]
    from_low = shifted(grad_third[:, rows - width :], "seq", 1)
    from_high = shifted(grad_first[:, :width], "seq", -1)
    third_earlier = jnp.concatenate([from_low, grad_third[:, : rows - width]], axis=1)
    first_following = jnp.concatenate([grad_first[:, width:], from_high], axis=1)
    return third_earlier, first_following


def halving_scatter(parts, order):
    count = parts[0].shape[0]
    bits = count.bit_length() - 1
    rank = lax.axis_index("seq")
    parts = [p.reshape((2,) * bits + p.shape[1:]) for p in parts]
    left = list(reversed(range(bits)))
    for bit in order:
        axis = left.index(bit)
        left.pop(axis)
        own = ((rank >> bit) & 1) == 1
        pairs = [(j, j ^ (1 << bit)) for j in range(count)]
        lows = [lax.index_in_dim(p, 0, axis, keepdims=False) for p in parts]
        highs = [lax.index_in_dim(p, 1, axis, keepdims=False) for p in parts]
        sends = tuple(jnp.where(own, lo, hi).astype(jnp.bfloat16) for lo, hi in zip(lows, highs))
        got = lax.ppermute(sends, "seq", pairs)
        parts = [
            jnp.where(own, hi, lo) + g.astype(jnp.float32) for lo, hi, g in zip(lows, highs, got)
        ]
    return parts


def shards(section_inputs, cotangent, conv_weight, out_weight):
    batch_count = cotangent.shape[0]
    positions = cotangent.shape[1]
    channels = cotangent.shape[2]
    far_hops = FAR // positions
    seq_count = lax.axis_size("seq")
    section_count = lax.axis_size("section")
    section_rank = lax.axis_index("section")
    conv_mat = conv_weight[0]
    out_mat = out_weight[0]
    depth = conv_mat.shape[0]
    grad_scale = 1.0 / math.sqrt(batch_count * positions * seq_count)

    hidden = section_inputs[0]
    stored = []
    for layer in range(depth):
        if layer == 0:
            earlier, following = halo_sides(hidden, NEAR)
        else:
            earlier, following = far_sides(hidden, far_hops)
        hidden, saved = forward_layer(
            hidden, earlier, following, conv_mat[layer], out_mat[layer], layer + 1 == depth
        )
        stored.append(saved)

    top = jnp.where(section_rank == section_count - 1, 1.0, 0.0).astype(jnp.float32)
    flowing = cotangent.astype(jnp.float32) * top
    input_grads = None
    conv_acc = [None] * depth
    out_acc = [None] * depth
    for step in range(section_count):
        for layer in reversed(range(depth)):
            if layer == depth - 1 and step > 0:
                flowing, conv_term, out_term = backward_far(
                    flowing, stored[layer], conv_mat[layer], out_mat[layer], far_hops
                )
            else:
                flowing, conv_term, out_term = backward_layer(
                    flowing, stored[layer], conv_mat[layer], out_mat[layer], layer, far_hops
                )
            conv_acc[layer] = conv_term if step == 0 else conv_acc[layer] + conv_term
            out_acc[layer] = out_term if step == 0 else out_acc[layer] + out_term
        low, inner, high = flowing
        flowing = jnp.concatenate([low, inner, high], axis=1)
        input_grads = flowing if step == 0 else input_grads + flowing
        if step + 1 < section_count:
            bf16 = jnp.bfloat16
            inner = shifted(inner.astype(bf16), "section", -1)
            edges = shifted(jnp.concatenate([low, high], axis=1).astype(bf16), "section", -1)
            flowing = (edges.astype(jnp.float32), inner.astype(jnp.float32))

    conv_rows = 3 * channels // seq_count
    out_rows = channels // seq_count
    conv_all = jnp.concatenate(
        [acc.reshape(seq_count, conv_rows, 2 * channels) for acc in conv_acc], axis=1
    )
    out_all = jnp.concatenate(
        [acc.reshape(seq_count, out_rows, channels) for acc in out_acc], axis=1
    ).reshape(seq_count, depth * out_rows * channels // (2 * channels), 2 * channels)
    (mine,) = halving_scatter([jnp.concatenate([conv_all, out_all], axis=1)], (0, 1, 3, 2, 4))
    conv_grads = mine[: depth * conv_rows].reshape(1, depth, conv_rows, 2 * channels) * grad_scale
    out_grads = mine[depth * conv_rows :].reshape(1, depth, out_rows, channels) * grad_scale
    return (input_grads[None], conv_grads, out_grads)


def solution(mesh):
    return jax.shard_map(
        shards,
        mesh=mesh,
        in_specs=(
            P("section", None, "seq", None),
            P(None, "seq", None),
            P("section", None, None, None, None),
            P("section", None, None, None),
        ),
        out_specs=(
            P("section", None, "seq", None),
            P("section", None, "seq", None),
            P("section", None, "seq", None),
        ),
        check_vma=False,
    )
```

```python
import math

import jax
import jax.numpy as jnp
from jax import lax
from jax.sharding import PartitionSpec as P

NEAR = 128
FAR = 1024


def shifted(value, axis, steps):
    count = lax.axis_size(axis)
    leading, last = (max(0, -steps), min(count, count - steps))
    return lax.ppermute(value, axis, [(source, source + steps) for source in range(leading, last)])


def halo_sides(block, width):
    rows = block.shape[1]
    from_low = shifted(block[:, rows - width :], "seq", 1)
    from_high = shifted(block[:, :width], "seq", -1)
    earlier = jnp.concatenate([from_low, block[:, : rows - width]], axis=1)
    following = jnp.concatenate([block[:, width:], from_high], axis=1)
    return earlier, following


def far_sides(block, hops):
    return shifted(block, "seq", hops), shifted(block, "seq", -hops)


def mm(a, b):
    return jnp.einsum("mpc,cd->mpd", a, b, preferred_element_type=jnp.float32)


def forward_layer(hidden, earlier, following, conv, out_mat, last):
    chans = hidden.shape[2]
    preact = mm(earlier, conv[0])
    preact = preact + mm(hidden, conv[1])
    preact = preact + mm(following, conv[2])
    tanh_part = jnp.tanh(preact[..., :chans])
    sig_part = jax.nn.sigmoid(preact[..., chans:])
    gated = (tanh_part * sig_part).astype(jnp.bfloat16)
    factor_a = (1.0 - tanh_part * tanh_part) * sig_part
    factor_b = tanh_part * sig_part * (1.0 - sig_part)
    taps = jnp.concatenate([earlier, hidden, following], axis=2)
    saved = (taps, gated, factor_a, factor_b)
    if last:
        return None, saved
    nxt = (hidden.astype(jnp.float32) + mm(gated, out_mat)).astype(jnp.bfloat16)
    return nxt, saved


def backward_layer(flowing, saved, conv, out_mat, layer, far_hops):
    taps, gated, factor_a, factor_b = saved
    chans = flowing.shape[2]
    grad_half = flowing.astype(jnp.bfloat16)
    out_term = jnp.einsum("mpc,mpd->cd", gated, grad_half, preferred_element_type=jnp.float32)
    grad_gated = jnp.einsum("mpd,cd->mpc", grad_half, out_mat, preferred_element_type=jnp.float32)
    grad_pre = jnp.concatenate([grad_gated * factor_a, grad_gated * factor_b], axis=2).astype(
        jnp.bfloat16
    )
    conv_term = jnp.einsum("mpc,mpd->cd", taps, grad_pre, preferred_element_type=jnp.float32)
    weights = conv.reshape(3 * chans, 2 * chans)
    back = jnp.einsum("mpd,cd->mpc", grad_pre, weights, preferred_element_type=jnp.float32)
    grad_first = back[..., :chans].astype(jnp.bfloat16)
    middle = back[..., chans : 2 * chans]
    grad_third = back[..., 2 * chans :].astype(jnp.bfloat16)
    if layer == 0:
        return split_near(flowing, middle, grad_first, grad_third, NEAR), conv_term, out_term
    else:
        third_earlier = shifted(grad_third, "seq", far_hops)
        first_following = shifted(grad_first, "seq", -far_hops)
    grad_conv = middle + first_following.astype(jnp.float32) + third_earlier.astype(jnp.float32)
    return flowing + grad_conv, conv_term, out_term


def split_rows(value, width):
    return jnp.concatenate([value[:, :width], value[:, -width:]], axis=1), value[:, width:-width]


def join_rows(edges, inner, width):
    return jnp.concatenate([edges[:, :width], inner, edges[:, width:]], axis=1)


def backward_far(pieces, saved, conv, out_mat, far_hops):
    taps, gated, factor_a, factor_b = saved
    chans = pieces[0].shape[2]
    width = NEAR
    weights = conv.reshape(3 * chans, 2 * chans)
    f32 = jnp.float32
    factors = [split_rows(factor_a, width), split_rows(factor_b, width)]
    outs, pres, halves = [], [], []
    for index, flowing in enumerate(pieces):
        grad_half = flowing.astype(jnp.bfloat16)
        grad_gated = jnp.einsum("mpd,cd->mpc", grad_half, out_mat, preferred_element_type=f32)
        grad_pre = jnp.concatenate(
            [grad_gated * factors[0][index], grad_gated * factors[1][index]], axis=2
        ).astype(jnp.bfloat16)
        back = jnp.einsum("mpd,cd->mpc", grad_pre, weights, preferred_element_type=f32)
        grad_first = back[..., :chans].astype(jnp.bfloat16)
        middle = back[..., chans : 2 * chans]
        grad_third = back[..., 2 * chans :].astype(jnp.bfloat16)
        third_earlier = shifted(grad_third, "seq", far_hops)
        first_following = shifted(grad_first, "seq", -far_hops)
        outs.append(flowing + (middle + first_following.astype(f32) + third_earlier.astype(f32)))
        pres.append(grad_pre)
        halves.append(grad_half)
    grad_pre = join_rows(pres[0], pres[1], width)
    grad_half = join_rows(halves[0], halves[1], width)
    out_term = jnp.einsum("mpc,mpd->cd", gated, grad_half, preferred_element_type=f32)
    conv_term = jnp.einsum("mpc,mpd->cd", taps, grad_pre, preferred_element_type=f32)
    return tuple(outs), conv_term, out_term


def backward_near_pieces(pieces, saved, conv, out_mat):
    taps, gated, factor_a, factor_b = saved
    chans = pieces[0].shape[2]
    width = NEAR
    weights = conv.reshape(3 * chans, 2 * chans)
    f32 = jnp.float32
    factors = [split_rows(factor_a, width), split_rows(factor_b, width)]
    firsts, middles, thirds, pres, halves = [], [], [], [], []
    for index, flowing in enumerate(pieces):
        grad_half = flowing.astype(jnp.bfloat16)
        grad_gated = jnp.einsum("mpd,cd->mpc", grad_half, out_mat, preferred_element_type=f32)
        grad_pre = jnp.concatenate(
            [grad_gated * factors[0][index], grad_gated * factors[1][index]], axis=2
        ).astype(jnp.bfloat16)
        back = jnp.einsum("mpd,cd->mpc", grad_pre, weights, preferred_element_type=f32)
        firsts.append(back[..., :chans].astype(jnp.bfloat16))
        middles.append(back[..., chans : 2 * chans])
        thirds.append(back[..., 2 * chans :].astype(jnp.bfloat16))
        pres.append(grad_pre)
        halves.append(grad_half)
    (first_e, first_i), (third_e, third_i) = firsts, thirds
    (middle_e, middle_i), (flow_e, flow_i) = middles, pieces
    low_in = shifted(third_e[:, width:], "seq", 1)
    high_in = shifted(first_e[:, :width], "seq", -1)
    first_up = jnp.concatenate([first_i[:, width:], first_e[:, width:]], axis=1)
    third_up = jnp.concatenate([third_e[:, :width], third_i[:, :width]], axis=1)
    inner = flow_i + (middle_i + first_up.astype(f32) + third_up.astype(f32))
    low = flow_e[:, :width] + (
        middle_e[:, :width] + first_i[:, :width].astype(f32) + low_in.astype(f32)
    )
    high = flow_e[:, width:] + (
        middle_e[:, width:] + high_in.astype(f32) + third_i[:, width:].astype(f32)
    )
    grad_pre = join_rows(pres[0], pres[1], width)
    grad_half = join_rows(halves[0], halves[1], width)
    out_term = jnp.einsum("mpc,mpd->cd", gated, grad_half, preferred_element_type=f32)
    conv_term = jnp.einsum("mpc,mpd->cd", taps, grad_pre, preferred_element_type=f32)
    return (low, inner, high), conv_term, out_term


def split_near(flowing, middle, grad_first, grad_third, width):
    rows = grad_first.shape[1]
    low_in = shifted(grad_third[:, rows - width :], "seq", 1)
    high_in = shifted(grad_first[:, :width], "seq", -1)
    f32 = jnp.float32
    inner = flowing[:, width : rows - width] + (
        middle[:, width : rows - width]
        + grad_first[:, 2 * width :].astype(f32)
        + grad_third[:, : rows - 2 * width].astype(f32)
    )
    low = flowing[:, :width] + (
        middle[:, :width] + grad_first[:, width : 2 * width].astype(f32) + low_in.astype(f32)
    )
    high = flowing[:, rows - width :] + (
        middle[:, rows - width :]
        + high_in.astype(f32)
        + grad_third[:, rows - 2 * width : rows - width].astype(f32)
    )
    return low, inner, high


def halo_sides_pair(grad_first, grad_third, width):
    rows = grad_first.shape[1]
    from_low = shifted(grad_third[:, rows - width :], "seq", 1)
    from_high = shifted(grad_first[:, :width], "seq", -1)
    third_earlier = jnp.concatenate([from_low, grad_third[:, : rows - width]], axis=1)
    first_following = jnp.concatenate([grad_first[:, width:], from_high], axis=1)
    return third_earlier, first_following


def halving_scatter(parts, order):
    count = parts[0].shape[0]
    bits = count.bit_length() - 1
    rank = lax.axis_index("seq")
    parts = [p.reshape((2,) * bits + p.shape[1:]) for p in parts]
    left = list(reversed(range(bits)))
    for bit in order:
        axis = left.index(bit)
        left.pop(axis)
        own = ((rank >> bit) & 1) == 1
        pairs = [(j, j ^ (1 << bit)) for j in range(count)]
        lows = [lax.index_in_dim(p, 0, axis, keepdims=False) for p in parts]
        highs = [lax.index_in_dim(p, 1, axis, keepdims=False) for p in parts]
        sends = tuple(jnp.where(own, lo, hi).astype(jnp.bfloat16) for lo, hi in zip(lows, highs))
        got = lax.ppermute(sends, "seq", pairs)
        parts = [
            jnp.where(own, hi, lo) + g.astype(jnp.float32) for lo, hi, g in zip(lows, highs, got)
        ]
    return parts


def shards(section_inputs, cotangent, conv_weight, out_weight):
    batch_count = cotangent.shape[0]
    positions = cotangent.shape[1]
    channels = cotangent.shape[2]
    far_hops = FAR // positions
    seq_count = lax.axis_size("seq")
    section_count = lax.axis_size("section")
    section_rank = lax.axis_index("section")
    conv_mat = conv_weight[0]
    out_mat = out_weight[0]
    depth = conv_mat.shape[0]
    grad_scale = 1.0 / math.sqrt(batch_count * positions * seq_count)

    hidden = section_inputs[0]
    stored = []
    for layer in range(depth):
        if layer == 0:
            earlier, following = halo_sides(hidden, NEAR)
        else:
            earlier, following = far_sides(hidden, far_hops)
        hidden, saved = forward_layer(
            hidden, earlier, following, conv_mat[layer], out_mat[layer], layer + 1 == depth
        )
        stored.append(saved)

    top = jnp.where(section_rank == section_count - 1, 1.0, 0.0).astype(jnp.float32)
    flowing = cotangent.astype(jnp.float32) * top
    input_grads = None
    conv_acc = [None] * depth
    out_acc = [None] * depth
    for step in range(section_count):
        for layer in reversed(range(depth)):
            if layer == depth - 1 and step > 0:
                flowing, conv_term, out_term = backward_far(
                    flowing, stored[layer], conv_mat[layer], out_mat[layer], far_hops
                )
            elif layer == 0 and depth == 2 and step > 0:
                flowing, conv_term, out_term = backward_near_pieces(
                    flowing, stored[layer], conv_mat[layer], out_mat[layer]
                )
            else:
                flowing, conv_term, out_term = backward_layer(
                    flowing, stored[layer], conv_mat[layer], out_mat[layer], layer, far_hops
                )
            conv_acc[layer] = conv_term if step == 0 else conv_acc[layer] + conv_term
            out_acc[layer] = out_term if step == 0 else out_acc[layer] + out_term
        low, inner, high = flowing
        flowing = jnp.concatenate([low, inner, high], axis=1)
        input_grads = flowing if step == 0 else input_grads + flowing
        if step + 1 < section_count:
            bf16 = jnp.bfloat16
            inner = shifted(inner.astype(bf16), "section", -1)
            edges = shifted(jnp.concatenate([low, high], axis=1).astype(bf16), "section", -1)
            flowing = (edges.astype(jnp.float32), inner.astype(jnp.float32))

    conv_rows = 3 * channels // seq_count
    out_rows = channels // seq_count
    conv_all = jnp.concatenate(
        [acc.reshape(seq_count, conv_rows, 2 * channels) for acc in conv_acc], axis=1
    )
    out_all = jnp.concatenate(
        [acc.reshape(seq_count, out_rows, channels) for acc in out_acc], axis=1
    ).reshape(seq_count, depth * out_rows * channels // (2 * channels), 2 * channels)
    (mine,) = halving_scatter([jnp.concatenate([conv_all, out_all], axis=1)], (0, 1, 3, 2, 4))
    conv_grads = mine[: depth * conv_rows].reshape(1, depth, conv_rows, 2 * channels) * grad_scale
    out_grads = mine[depth * conv_rows :].reshape(1, depth, out_rows, channels) * grad_scale
    return (input_grads[None], conv_grads, out_grads)


def solution(mesh):
    return jax.shard_map(
        shards,
        mesh=mesh,
        in_specs=(
            P("section", None, "seq", None),
            P(None, "seq", None),
            P("section", None, None, None, None),
            P("section", None, None, None),
        ),
        out_specs=(
            P("section", None, "seq", None),
            P("section", None, "seq", None),
            P("section", None, "seq", None),
        ),
        check_vma=False,
    )
```

```python
import math

import jax
import jax.numpy as jnp
from jax import lax
from jax.sharding import PartitionSpec as P

NEAR = 128
FAR = 1024


def shifted(value, axis, steps):
    count = lax.axis_size(axis)
    leading, last = (max(0, -steps), min(count, count - steps))
    return lax.ppermute(value, axis, [(source, source + steps) for source in range(leading, last)])


def halo_sides(block, width):
    rows = block.shape[1]
    from_low = shifted(block[:, rows - width :], "seq", 1)
    from_high = shifted(block[:, :width], "seq", -1)
    earlier = jnp.concatenate([from_low, block[:, : rows - width]], axis=1)
    following = jnp.concatenate([block[:, width:], from_high], axis=1)
    return earlier, following


def far_sides(block, hops):
    return shifted(block, "seq", hops), shifted(block, "seq", -hops)


def mm(a, b):
    return jnp.einsum("mpc,cd->mpd", a, b, preferred_element_type=jnp.float32)


def forward_layer(hidden, earlier, following, conv, out_mat, last):
    chans = hidden.shape[2]
    preact = mm(earlier, conv[0])
    preact = preact + mm(hidden, conv[1])
    preact = preact + mm(following, conv[2])
    tanh_part = jnp.tanh(preact[..., :chans])
    sig_part = jax.nn.sigmoid(preact[..., chans:])
    gated = (tanh_part * sig_part).astype(jnp.bfloat16)
    factor_a = (1.0 - tanh_part * tanh_part) * sig_part
    factor_b = tanh_part * sig_part * (1.0 - sig_part)
    taps = jnp.concatenate([earlier, hidden, following], axis=2)
    saved = (taps, gated, factor_a, factor_b)
    if last:
        return None, saved
    nxt = (hidden.astype(jnp.float32) + mm(gated, out_mat)).astype(jnp.bfloat16)
    return nxt, saved


def backward_layer(flowing, saved, conv, out_mat, layer, far_hops):
    taps, gated, factor_a, factor_b = saved
    chans = flowing.shape[2]
    grad_half = flowing.astype(jnp.bfloat16)
    out_term = jnp.einsum("mpc,mpd->cd", gated, grad_half, preferred_element_type=jnp.float32)
    grad_gated = jnp.einsum("mpd,cd->mpc", grad_half, out_mat, preferred_element_type=jnp.float32)
    grad_pre = jnp.concatenate([grad_gated * factor_a, grad_gated * factor_b], axis=2).astype(
        jnp.bfloat16
    )
    conv_term = jnp.einsum("mpc,mpd->cd", taps, grad_pre, preferred_element_type=jnp.float32)
    weights = conv.reshape(3 * chans, 2 * chans)
    back = jnp.einsum("mpd,cd->mpc", grad_pre, weights, preferred_element_type=jnp.float32)
    grad_first = back[..., :chans].astype(jnp.bfloat16)
    middle = back[..., chans : 2 * chans]
    grad_third = back[..., 2 * chans :].astype(jnp.bfloat16)
    if layer == 0:
        return split_near(flowing, middle, grad_first, grad_third, NEAR), conv_term, out_term
    else:
        third_earlier = shifted(grad_third, "seq", far_hops)
        first_following = shifted(grad_first, "seq", -far_hops)
    grad_conv = middle + first_following.astype(jnp.float32) + third_earlier.astype(jnp.float32)
    return flowing + grad_conv, conv_term, out_term


def split_rows(value, width):
    return jnp.concatenate([value[:, :width], value[:, -width:]], axis=1), value[:, width:-width]


def join_rows(edges, inner, width):
    return jnp.concatenate([edges[:, :width], inner, edges[:, width:]], axis=1)


def backward_far(pieces, saved, conv, out_mat, far_hops):
    taps, gated, factor_a, factor_b = saved
    chans = pieces[0].shape[2]
    width = NEAR
    weights = conv.reshape(3 * chans, 2 * chans)
    f32 = jnp.float32
    factors = [split_rows(factor_a, width), split_rows(factor_b, width)]
    outs, pres, halves = [], [], []
    for index, flowing in enumerate(pieces):
        grad_half = flowing.astype(jnp.bfloat16)
        grad_gated = jnp.einsum("mpd,cd->mpc", grad_half, out_mat, preferred_element_type=f32)
        grad_pre = jnp.concatenate(
            [grad_gated * factors[0][index], grad_gated * factors[1][index]], axis=2
        ).astype(jnp.bfloat16)
        back = jnp.einsum("mpd,cd->mpc", grad_pre, weights, preferred_element_type=f32)
        grad_first = back[..., :chans].astype(jnp.bfloat16)
        middle = back[..., chans : 2 * chans]
        grad_third = back[..., 2 * chans :].astype(jnp.bfloat16)
        third_earlier = shifted(grad_third, "seq", far_hops)
        first_following = shifted(grad_first, "seq", -far_hops)
        outs.append(flowing + (middle + first_following.astype(f32) + third_earlier.astype(f32)))
        pres.append(grad_pre)
        halves.append(grad_half)
    grad_pre = join_rows(pres[0], pres[1], width)
    grad_half = join_rows(halves[0], halves[1], width)
    out_term = jnp.einsum("mpc,mpd->cd", gated, grad_half, preferred_element_type=f32)
    conv_term = jnp.einsum("mpc,mpd->cd", taps, grad_pre, preferred_element_type=f32)
    return tuple(outs), conv_term, out_term


def backward_near_pieces(pieces, saved, conv, out_mat):
    taps, gated, factor_a, factor_b = saved
    chans = pieces[0].shape[2]
    width = NEAR
    weights = conv.reshape(3 * chans, 2 * chans)
    f32 = jnp.float32
    factors = [split_rows(factor_a, width), split_rows(factor_b, width)]
    firsts, middles, thirds, pres, halves = [], [], [], [], []
    for index, flowing in enumerate(pieces):
        grad_half = flowing.astype(jnp.bfloat16)
        grad_gated = jnp.einsum("mpd,cd->mpc", grad_half, out_mat, preferred_element_type=f32)
        grad_pre = jnp.concatenate(
            [grad_gated * factors[0][index], grad_gated * factors[1][index]], axis=2
        ).astype(jnp.bfloat16)
        back = jnp.einsum("mpd,cd->mpc", grad_pre, weights, preferred_element_type=f32)
        firsts.append(back[..., :chans].astype(jnp.bfloat16))
        middles.append(back[..., chans : 2 * chans])
        thirds.append(back[..., 2 * chans :].astype(jnp.bfloat16))
        pres.append(grad_pre)
        halves.append(grad_half)
    (first_e, first_i), (third_e, third_i) = firsts, thirds
    (middle_e, middle_i), (flow_e, flow_i) = middles, pieces
    low_in = shifted(third_e[:, width:], "seq", 1)
    high_in = shifted(first_e[:, :width], "seq", -1)
    first_up = jnp.concatenate([first_i[:, width:], first_e[:, width:]], axis=1)
    third_up = jnp.concatenate([third_e[:, :width], third_i[:, :width]], axis=1)
    inner = flow_i + (middle_i + first_up.astype(f32) + third_up.astype(f32))
    low = flow_e[:, :width] + (
        middle_e[:, :width] + first_i[:, :width].astype(f32) + low_in.astype(f32)
    )
    high = flow_e[:, width:] + (
        middle_e[:, width:] + high_in.astype(f32) + third_i[:, width:].astype(f32)
    )
    grad_pre = join_rows(pres[0], pres[1], width)
    grad_half = join_rows(halves[0], halves[1], width)
    out_term = jnp.einsum("mpc,mpd->cd", gated, grad_half, preferred_element_type=f32)
    conv_term = jnp.einsum("mpc,mpd->cd", taps, grad_pre, preferred_element_type=f32)
    return (low, inner, high), conv_term, out_term


def split_near(flowing, middle, grad_first, grad_third, width):
    rows = grad_first.shape[1]
    low_in = shifted(grad_third[:, rows - width :], "seq", 1)
    high_in = shifted(grad_first[:, :width], "seq", -1)
    f32 = jnp.float32
    inner = flowing[:, width : rows - width] + (
        middle[:, width : rows - width]
        + grad_first[:, 2 * width :].astype(f32)
        + grad_third[:, : rows - 2 * width].astype(f32)
    )
    low = flowing[:, :width] + (
        middle[:, :width] + grad_first[:, width : 2 * width].astype(f32) + low_in.astype(f32)
    )
    high = flowing[:, rows - width :] + (
        middle[:, rows - width :]
        + high_in.astype(f32)
        + grad_third[:, rows - 2 * width : rows - width].astype(f32)
    )
    return low, inner, high


def halo_sides_pair(grad_first, grad_third, width):
    rows = grad_first.shape[1]
    from_low = shifted(grad_third[:, rows - width :], "seq", 1)
    from_high = shifted(grad_first[:, :width], "seq", -1)
    third_earlier = jnp.concatenate([from_low, grad_third[:, : rows - width]], axis=1)
    first_following = jnp.concatenate([grad_first[:, width:], from_high], axis=1)
    return third_earlier, first_following


def halving_scatter(parts, order):
    count = parts[0].shape[0]
    bits = count.bit_length() - 1
    rank = lax.axis_index("seq")
    parts = [p.reshape((2,) * bits + p.shape[1:]) for p in parts]
    left = list(reversed(range(bits)))
    for bit in order:
        axis = left.index(bit)
        left.pop(axis)
        own = ((rank >> bit) & 1) == 1
        pairs = [(j, j ^ (1 << bit)) for j in range(count)]
        lows = [lax.index_in_dim(p, 0, axis, keepdims=False) for p in parts]
        highs = [lax.index_in_dim(p, 1, axis, keepdims=False) for p in parts]
        sends = tuple(jnp.where(own, lo, hi).astype(jnp.bfloat16) for lo, hi in zip(lows, highs))
        got = lax.ppermute(sends, "seq", pairs)
        parts = [
            jnp.where(own, hi, lo) + g.astype(jnp.float32) for lo, hi, g in zip(lows, highs, got)
        ]
    return parts


def shards(section_inputs, cotangent, conv_weight, out_weight):
    batch_count = cotangent.shape[0]
    positions = cotangent.shape[1]
    channels = cotangent.shape[2]
    far_hops = FAR // positions
    seq_count = lax.axis_size("seq")
    section_count = lax.axis_size("section")
    section_rank = lax.axis_index("section")
    conv_mat = conv_weight[0]
    out_mat = out_weight[0]
    depth = conv_mat.shape[0]
    grad_scale = 1.0 / math.sqrt(batch_count * positions * seq_count)

    hidden = section_inputs[0]
    stored = []
    for layer in range(depth):
        if layer == 0:
            earlier, following = halo_sides(hidden, NEAR)
        else:
            earlier, following = far_sides(hidden, far_hops)
        hidden, saved = forward_layer(
            hidden, earlier, following, conv_mat[layer], out_mat[layer], layer + 1 == depth
        )
        stored.append(saved)

    top = jnp.where(section_rank == section_count - 1, 1.0, 0.0).astype(jnp.float32)
    flowing = cotangent.astype(jnp.float32) * top
    input_grads = None
    conv_acc = [None] * depth
    out_acc = [None] * depth
    for step in range(section_count):
        for layer in reversed(range(depth)):
            if layer == depth - 1 and step > 0:
                flowing, conv_term, out_term = backward_far(
                    flowing, stored[layer], conv_mat[layer], out_mat[layer], far_hops
                )
            elif layer == 0 and depth == 2:
                if step == 0:
                    flowing = split_rows(flowing, NEAR)
                flowing, conv_term, out_term = backward_near_pieces(
                    flowing, stored[layer], conv_mat[layer], out_mat[layer]
                )
            else:
                flowing, conv_term, out_term = backward_layer(
                    flowing, stored[layer], conv_mat[layer], out_mat[layer], layer, far_hops
                )
            conv_acc[layer] = conv_term if step == 0 else conv_acc[layer] + conv_term
            out_acc[layer] = out_term if step == 0 else out_acc[layer] + out_term
        low, inner, high = flowing
        flowing = jnp.concatenate([low, inner, high], axis=1)
        input_grads = flowing if step == 0 else input_grads + flowing
        if step + 1 < section_count:
            bf16 = jnp.bfloat16
            inner = shifted(inner.astype(bf16), "section", -1)
            edges = shifted(jnp.concatenate([low, high], axis=1).astype(bf16), "section", -1)
            flowing = (edges.astype(jnp.float32), inner.astype(jnp.float32))

    conv_rows = 3 * channels // seq_count
    out_rows = channels // seq_count
    conv_all = jnp.concatenate(
        [acc.reshape(seq_count, conv_rows, 2 * channels) for acc in conv_acc], axis=1
    )
    out_all = jnp.concatenate(
        [acc.reshape(seq_count, out_rows, channels) for acc in out_acc], axis=1
    ).reshape(seq_count, depth * out_rows * channels // (2 * channels), 2 * channels)
    (mine,) = halving_scatter([jnp.concatenate([conv_all, out_all], axis=1)], (0, 1, 3, 2, 4))
    conv_grads = mine[: depth * conv_rows].reshape(1, depth, conv_rows, 2 * channels) * grad_scale
    out_grads = mine[depth * conv_rows :].reshape(1, depth, out_rows, channels) * grad_scale
    return (input_grads[None], conv_grads, out_grads)


def solution(mesh):
    return jax.shard_map(
        shards,
        mesh=mesh,
        in_specs=(
            P("section", None, "seq", None),
            P(None, "seq", None),
            P("section", None, None, None, None),
            P("section", None, None, None),
        ),
        out_specs=(
            P("section", None, "seq", None),
            P("section", None, "seq", None),
            P("section", None, "seq", None),
        ),
        check_vma=False,
    )
```

```python
import math

import jax
import jax.numpy as jnp
from jax import lax
from jax.sharding import PartitionSpec as P

NEAR = 128
FAR = 1024


def shifted(value, axis, steps):
    count = lax.axis_size(axis)
    leading, last = (max(0, -steps), min(count, count - steps))
    return lax.ppermute(value, axis, [(source, source + steps) for source in range(leading, last)])


def halo_sides(block, width):
    rows = block.shape[1]
    from_low = shifted(block[:, rows - width :], "seq", 1)
    from_high = shifted(block[:, :width], "seq", -1)
    earlier = jnp.concatenate([from_low, block[:, : rows - width]], axis=1)
    following = jnp.concatenate([block[:, width:], from_high], axis=1)
    return earlier, following


def far_sides(block, hops):
    return shifted(block, "seq", hops), shifted(block, "seq", -hops)


def mm(a, b):
    return jnp.einsum("mpc,cd->mpd", a, b, preferred_element_type=jnp.float32)


def forward_layer(hidden, earlier, following, conv, out_mat, last):
    chans = hidden.shape[2]
    preact = mm(earlier, conv[0])
    preact = preact + mm(hidden, conv[1])
    preact = preact + mm(following, conv[2])
    tanh_part = jnp.tanh(preact[..., :chans])
    sig_part = jax.nn.sigmoid(preact[..., chans:])
    gated = (tanh_part * sig_part).astype(jnp.bfloat16)
    factor_a = (1.0 - tanh_part * tanh_part) * sig_part
    factor_b = tanh_part * sig_part * (1.0 - sig_part)
    taps = jnp.concatenate([earlier, hidden, following], axis=2)
    saved = (taps, gated, factor_a, factor_b)
    if last:
        return None, saved
    nxt = (hidden.astype(jnp.float32) + mm(gated, out_mat)).astype(jnp.bfloat16)
    return nxt, saved


def backward_layer(flowing, saved, conv, out_mat, layer, far_hops):
    taps, gated, factor_a, factor_b = saved
    chans = flowing.shape[2]
    grad_half = flowing.astype(jnp.bfloat16)
    out_term = jnp.einsum("mpc,mpd->cd", gated, grad_half, preferred_element_type=jnp.float32)
    grad_gated = jnp.einsum("mpd,cd->mpc", grad_half, out_mat, preferred_element_type=jnp.float32)
    grad_pre = jnp.concatenate([grad_gated * factor_a, grad_gated * factor_b], axis=2).astype(
        jnp.bfloat16
    )
    conv_term = jnp.einsum("mpc,mpd->cd", taps, grad_pre, preferred_element_type=jnp.float32)
    weights = conv.reshape(3 * chans, 2 * chans)
    back = jnp.einsum("mpd,cd->mpc", grad_pre, weights, preferred_element_type=jnp.float32)
    grad_first = back[..., :chans].astype(jnp.bfloat16)
    middle = back[..., chans : 2 * chans]
    grad_third = back[..., 2 * chans :].astype(jnp.bfloat16)
    if layer == 0:
        return split_near(flowing, middle, grad_first, grad_third, NEAR), conv_term, out_term
    else:
        third_earlier = shifted(grad_third, "seq", far_hops)
        first_following = shifted(grad_first, "seq", -far_hops)
    grad_conv = middle + first_following.astype(jnp.float32) + third_earlier.astype(jnp.float32)
    return flowing + grad_conv, conv_term, out_term


def split_rows(value, width):
    return jnp.concatenate([value[:, :width], value[:, -width:]], axis=1), value[:, width:-width]


def join_rows(edges, inner, width):
    return jnp.concatenate([edges[:, :width], inner, edges[:, width:]], axis=1)


def backward_far(pieces, saved, conv, out_mat, far_hops):
    taps, gated, factor_a, factor_b = saved
    chans = pieces[0].shape[2]
    width = NEAR
    weights = conv.reshape(3 * chans, 2 * chans)
    f32 = jnp.float32
    factors = [split_rows(factor_a, width), split_rows(factor_b, width)]
    outs, pres, halves = [], [], []
    for index, flowing in enumerate(pieces):
        grad_half = flowing.astype(jnp.bfloat16)
        grad_gated = jnp.einsum("mpd,cd->mpc", grad_half, out_mat, preferred_element_type=f32)
        grad_pre = jnp.concatenate(
            [grad_gated * factors[0][index], grad_gated * factors[1][index]], axis=2
        ).astype(jnp.bfloat16)
        back = jnp.einsum("mpd,cd->mpc", grad_pre, weights, preferred_element_type=f32)
        grad_first = back[..., :chans].astype(jnp.bfloat16)
        middle = back[..., chans : 2 * chans]
        grad_third = back[..., 2 * chans :].astype(jnp.bfloat16)
        third_earlier = shifted(grad_third, "seq", far_hops)
        first_following = shifted(grad_first, "seq", -far_hops)
        outs.append(flowing + (middle + first_following.astype(f32) + third_earlier.astype(f32)))
        pres.append(grad_pre)
        halves.append(grad_half)
    grad_pre = join_rows(pres[0], pres[1], width)
    grad_half = join_rows(halves[0], halves[1], width)
    out_term = jnp.einsum("mpc,mpd->cd", gated, grad_half, preferred_element_type=f32)
    conv_term = jnp.einsum("mpc,mpd->cd", taps, grad_pre, preferred_element_type=f32)
    return tuple(outs), conv_term, out_term


def backward_near_pieces(pieces, saved, conv, out_mat):
    taps, gated, factor_a, factor_b = saved
    chans = pieces[0].shape[2]
    width = NEAR
    weights = conv.reshape(3 * chans, 2 * chans)
    f32 = jnp.float32
    factors = [split_rows(factor_a, width), split_rows(factor_b, width)]
    firsts, middles, thirds, pres, halves = [], [], [], [], []
    for index, flowing in enumerate(pieces):
        grad_half = flowing.astype(jnp.bfloat16)
        grad_gated = jnp.einsum("mpd,cd->mpc", grad_half, out_mat, preferred_element_type=f32)
        grad_pre = jnp.concatenate(
            [grad_gated * factors[0][index], grad_gated * factors[1][index]], axis=2
        ).astype(jnp.bfloat16)
        back = jnp.einsum("mpd,cd->mpc", grad_pre, weights, preferred_element_type=f32)
        firsts.append(back[..., :chans].astype(jnp.bfloat16))
        middles.append(back[..., chans : 2 * chans])
        thirds.append(back[..., 2 * chans :].astype(jnp.bfloat16))
        pres.append(grad_pre)
        halves.append(grad_half)
    (first_e, first_i), (third_e, third_i) = firsts, thirds
    (middle_e, middle_i), (flow_e, flow_i) = middles, pieces
    low_in = shifted(third_e[:, width:], "seq", 1)
    high_in = shifted(first_e[:, :width], "seq", -1)
    first_up = jnp.concatenate([first_i[:, width:], first_e[:, width:]], axis=1)
    third_up = jnp.concatenate([third_e[:, :width], third_i[:, :width]], axis=1)
    inner = flow_i + (middle_i + first_up.astype(f32) + third_up.astype(f32))
    low = flow_e[:, :width] + (
        middle_e[:, :width] + first_i[:, :width].astype(f32) + low_in.astype(f32)
    )
    high = flow_e[:, width:] + (
        middle_e[:, width:] + high_in.astype(f32) + third_i[:, width:].astype(f32)
    )
    grad_pre = join_rows(pres[0], pres[1], width)
    grad_half = join_rows(halves[0], halves[1], width)
    out_term = jnp.einsum("mpc,mpd->cd", gated, grad_half, preferred_element_type=f32)
    conv_term = jnp.einsum("mpc,mpd->cd", taps, grad_pre, preferred_element_type=f32)
    return (low, inner, high), conv_term, out_term


def split_near(flowing, middle, grad_first, grad_third, width):
    rows = grad_first.shape[1]
    low_in = shifted(grad_third[:, rows - width :], "seq", 1)
    high_in = shifted(grad_first[:, :width], "seq", -1)
    f32 = jnp.float32
    inner = flowing[:, width : rows - width] + (
        middle[:, width : rows - width]
        + grad_first[:, 2 * width :].astype(f32)
        + grad_third[:, : rows - 2 * width].astype(f32)
    )
    low = flowing[:, :width] + (
        middle[:, :width] + grad_first[:, width : 2 * width].astype(f32) + low_in.astype(f32)
    )
    high = flowing[:, rows - width :] + (
        middle[:, rows - width :]
        + high_in.astype(f32)
        + grad_third[:, rows - 2 * width : rows - width].astype(f32)
    )
    return low, inner, high


def halo_sides_pair(grad_first, grad_third, width):
    rows = grad_first.shape[1]
    from_low = shifted(grad_third[:, rows - width :], "seq", 1)
    from_high = shifted(grad_first[:, :width], "seq", -1)
    third_earlier = jnp.concatenate([from_low, grad_third[:, : rows - width]], axis=1)
    first_following = jnp.concatenate([grad_first[:, width:], from_high], axis=1)
    return third_earlier, first_following


def halving_scatter(parts, order):
    count = parts[0].shape[0]
    bits = count.bit_length() - 1
    rank = lax.axis_index("seq")
    parts = [p.reshape((2,) * bits + p.shape[1:]) for p in parts]
    left = list(reversed(range(bits)))
    for group in order:
        owns = [(rank >> bit) & 1 for bit in group]
        for bit in group:
            left.remove(bit)

        def sub_at(p, values):
            by_axis = sorted(zip([axis_of[bit] for bit in group], values), reverse=True)
            sub = p
            for axis, value in by_axis:
                sub = lax.index_in_dim(sub, value, axis, keepdims=False)
            return sub

        axis_of = {}
        remaining = [bit for bit in reversed(range(bits)) if bit in left or bit in group]
        for bit in group:
            axis_of[bit] = remaining.index(bit)

        def chosen(p, flips):
            result = None
            for values in range(1 << len(group)):
                vals = [(values >> k) & 1 for k in range(len(group))]
                hit = None
                for k in range(len(group)):
                    cond = (owns[k] ^ flips[k]) == vals[k]
                    hit = cond if hit is None else hit & cond
                sub = sub_at(p, vals)
                result = sub if result is None else jnp.where(hit, sub, result)
            return result

        kept = [chosen(p, [0] * len(group)) for p in parts]
        for flips_code in range(1, 1 << len(group)):
            flips = [(flips_code >> k) & 1 for k in range(len(group))]
            mask = sum(f << bit for f, bit in zip(flips, group))
            pairs = [(j, j ^ mask) for j in range(count)]
            sends = tuple(chosen(p, flips).astype(jnp.bfloat16) for p in parts)
            got = lax.ppermute(sends, "seq", pairs)
            kept = [k + g.astype(jnp.float32) for k, g in zip(kept, got)]
        parts = kept
    return parts


def shards(section_inputs, cotangent, conv_weight, out_weight):
    batch_count = cotangent.shape[0]
    positions = cotangent.shape[1]
    channels = cotangent.shape[2]
    far_hops = FAR // positions
    seq_count = lax.axis_size("seq")
    section_count = lax.axis_size("section")
    section_rank = lax.axis_index("section")
    conv_mat = conv_weight[0]
    out_mat = out_weight[0]
    depth = conv_mat.shape[0]
    grad_scale = 1.0 / math.sqrt(batch_count * positions * seq_count)

    hidden = section_inputs[0]
    stored = []
    for layer in range(depth):
        if layer == 0:
            earlier, following = halo_sides(hidden, NEAR)
        else:
            earlier, following = far_sides(hidden, far_hops)
        hidden, saved = forward_layer(
            hidden, earlier, following, conv_mat[layer], out_mat[layer], layer + 1 == depth
        )
        stored.append(saved)

    top = jnp.where(section_rank == section_count - 1, 1.0, 0.0).astype(jnp.float32)
    flowing = cotangent.astype(jnp.float32) * top
    input_grads = None
    conv_acc = [None] * depth
    out_acc = [None] * depth
    for step in range(section_count):
        for layer in reversed(range(depth)):
            if layer == depth - 1 and step > 0:
                flowing, conv_term, out_term = backward_far(
                    flowing, stored[layer], conv_mat[layer], out_mat[layer], far_hops
                )
            elif layer == 0 and depth == 2 and step > 0:
                flowing, conv_term, out_term = backward_near_pieces(
                    flowing, stored[layer], conv_mat[layer], out_mat[layer]
                )
            else:
                flowing, conv_term, out_term = backward_layer(
                    flowing, stored[layer], conv_mat[layer], out_mat[layer], layer, far_hops
                )
            conv_acc[layer] = conv_term if step == 0 else conv_acc[layer] + conv_term
            out_acc[layer] = out_term if step == 0 else out_acc[layer] + out_term
        low, inner, high = flowing
        flowing = jnp.concatenate([low, inner, high], axis=1)
        input_grads = flowing if step == 0 else input_grads + flowing
        if step + 1 < section_count:
            bf16 = jnp.bfloat16
            inner = shifted(inner.astype(bf16), "section", -1)
            edges = shifted(jnp.concatenate([low, high], axis=1).astype(bf16), "section", -1)
            flowing = (edges.astype(jnp.float32), inner.astype(jnp.float32))

    conv_rows = 3 * channels // seq_count
    out_rows = channels // seq_count
    conv_all = jnp.concatenate(
        [acc.reshape(seq_count, conv_rows, 2 * channels) for acc in conv_acc], axis=1
    )
    out_all = jnp.concatenate(
        [acc.reshape(seq_count, out_rows, channels) for acc in out_acc], axis=1
    ).reshape(seq_count, depth * out_rows * channels // (2 * channels), 2 * channels)
    (mine,) = halving_scatter([jnp.concatenate([conv_all, out_all], axis=1)], ((0,), (1,), (3,), (2, 4)))
    conv_grads = mine[: depth * conv_rows].reshape(1, depth, conv_rows, 2 * channels) * grad_scale
    out_grads = mine[depth * conv_rows :].reshape(1, depth, out_rows, channels) * grad_scale
    return (input_grads[None], conv_grads, out_grads)


def solution(mesh):
    return jax.shard_map(
        shards,
        mesh=mesh,
        in_specs=(
            P("section", None, "seq", None),
            P(None, "seq", None),
            P("section", None, None, None, None),
            P("section", None, None, None),
        ),
        out_specs=(
            P("section", None, "seq", None),
            P("section", None, "seq", None),
            P("section", None, "seq", None),
        ),
        check_vma=False,
    )
```

```python
import math

import jax
import jax.numpy as jnp
from jax import lax
from jax.sharding import PartitionSpec as P

NEAR = 128
FAR = 1024


def shifted(value, axis, steps):
    count = lax.axis_size(axis)
    leading, last = (max(0, -steps), min(count, count - steps))
    return lax.ppermute(value, axis, [(source, source + steps) for source in range(leading, last)])


def halo_sides(block, width):
    rows = block.shape[1]
    from_low = shifted(block[:, rows - width :], "seq", 1)
    from_high = shifted(block[:, :width], "seq", -1)
    earlier = jnp.concatenate([from_low, block[:, : rows - width]], axis=1)
    following = jnp.concatenate([block[:, width:], from_high], axis=1)
    return earlier, following


def far_sides(block, hops):
    return shifted(block, "seq", hops), shifted(block, "seq", -hops)


def mm(a, b):
    return jnp.einsum("mpc,cd->mpd", a, b, preferred_element_type=jnp.float32)


def forward_layer(hidden, earlier, following, conv, out_mat, last):
    chans = hidden.shape[2]
    preact = mm(earlier, conv[0])
    preact = preact + mm(hidden, conv[1])
    preact = preact + mm(following, conv[2])
    tanh_part = jnp.tanh(preact[..., :chans])
    sig_part = jax.nn.sigmoid(preact[..., chans:])
    gated = (tanh_part * sig_part).astype(jnp.bfloat16)
    factor_a = (1.0 - tanh_part * tanh_part) * sig_part
    factor_b = tanh_part * sig_part * (1.0 - sig_part)
    taps = jnp.concatenate([earlier, hidden, following], axis=2)
    saved = (taps, gated, factor_a, factor_b)
    if last:
        return None, saved
    nxt = (hidden.astype(jnp.float32) + mm(gated, out_mat)).astype(jnp.bfloat16)
    return nxt, saved


def backward_layer(flowing, saved, conv, out_mat, layer, far_hops):
    taps, gated, factor_a, factor_b = saved
    chans = flowing.shape[2]
    grad_half = flowing.astype(jnp.bfloat16)
    out_term = jnp.einsum("mpc,mpd->cd", gated, grad_half, preferred_element_type=jnp.float32)
    grad_gated = jnp.einsum("mpd,cd->mpc", grad_half, out_mat, preferred_element_type=jnp.float32)
    grad_pre = jnp.concatenate([grad_gated * factor_a, grad_gated * factor_b], axis=2).astype(
        jnp.bfloat16
    )
    conv_term = jnp.einsum("mpc,mpd->cd", taps, grad_pre, preferred_element_type=jnp.float32)
    weights = conv.reshape(3 * chans, 2 * chans)
    back = jnp.einsum("mpd,cd->mpc", grad_pre, weights, preferred_element_type=jnp.float32)
    grad_first = back[..., :chans].astype(jnp.bfloat16)
    middle = back[..., chans : 2 * chans]
    grad_third = back[..., 2 * chans :].astype(jnp.bfloat16)
    if layer == 0:
        return split_near(flowing, middle, grad_first, grad_third, NEAR), conv_term, out_term
    else:
        third_earlier = shifted(grad_third, "seq", far_hops)
        first_following = shifted(grad_first, "seq", -far_hops)
    grad_conv = middle + first_following.astype(jnp.float32) + third_earlier.astype(jnp.float32)
    return flowing + grad_conv, conv_term, out_term


def split_rows(value, width):
    return jnp.concatenate([value[:, :width], value[:, -width:]], axis=1), value[:, width:-width]


def join_rows(edges, inner, width):
    return jnp.concatenate([edges[:, :width], inner, edges[:, width:]], axis=1)


def backward_far(pieces, saved, conv, out_mat, far_hops):
    taps, gated, factor_a, factor_b = saved
    chans = pieces[0].shape[2]
    width = NEAR
    weights = conv.reshape(3 * chans, 2 * chans)
    f32 = jnp.float32
    factors = [split_rows(factor_a, width), split_rows(factor_b, width)]
    outs, pres, halves = [], [], []
    for index, flowing in enumerate(pieces):
        grad_half = flowing.astype(jnp.bfloat16)
        grad_gated = jnp.einsum("mpd,cd->mpc", grad_half, out_mat, preferred_element_type=f32)
        grad_pre = jnp.concatenate(
            [grad_gated * factors[0][index], grad_gated * factors[1][index]], axis=2
        ).astype(jnp.bfloat16)
        back = jnp.einsum("mpd,cd->mpc", grad_pre, weights, preferred_element_type=f32)
        grad_first = back[..., :chans].astype(jnp.bfloat16)
        middle = back[..., chans : 2 * chans]
        grad_third = back[..., 2 * chans :].astype(jnp.bfloat16)
        third_earlier = shifted(grad_third, "seq", far_hops)
        first_following = shifted(grad_first, "seq", -far_hops)
        outs.append(flowing + (middle + first_following.astype(f32) + third_earlier.astype(f32)))
        pres.append(grad_pre)
        halves.append(grad_half)
    grad_pre = join_rows(pres[0], pres[1], width)
    grad_half = join_rows(halves[0], halves[1], width)
    out_term = jnp.einsum("mpc,mpd->cd", gated, grad_half, preferred_element_type=f32)
    conv_term = jnp.einsum("mpc,mpd->cd", taps, grad_pre, preferred_element_type=f32)
    return tuple(outs), conv_term, out_term


def backward_near_pieces(pieces, saved, conv, out_mat):
    taps, gated, factor_a, factor_b = saved
    chans = pieces[0].shape[2]
    width = NEAR
    weights = conv.reshape(3 * chans, 2 * chans)
    f32 = jnp.float32
    factors = [split_rows(factor_a, width), split_rows(factor_b, width)]
    firsts, middles, thirds, pres, halves = [], [], [], [], []
    for index, flowing in enumerate(pieces):
        grad_half = flowing.astype(jnp.bfloat16)
        grad_gated = jnp.einsum("mpd,cd->mpc", grad_half, out_mat, preferred_element_type=f32)
        grad_pre = jnp.concatenate(
            [grad_gated * factors[0][index], grad_gated * factors[1][index]], axis=2
        ).astype(jnp.bfloat16)
        back = jnp.einsum("mpd,cd->mpc", grad_pre, weights, preferred_element_type=f32)
        firsts.append(back[..., :chans].astype(jnp.bfloat16))
        middles.append(back[..., chans : 2 * chans])
        thirds.append(back[..., 2 * chans :].astype(jnp.bfloat16))
        pres.append(grad_pre)
        halves.append(grad_half)
    (first_e, first_i), (third_e, third_i) = firsts, thirds
    (middle_e, middle_i), (flow_e, flow_i) = middles, pieces
    low_in = shifted(third_e[:, width:], "seq", 1)
    high_in = shifted(first_e[:, :width], "seq", -1)
    first_up = jnp.concatenate([first_i[:, width:], first_e[:, width:]], axis=1)
    third_up = jnp.concatenate([third_e[:, :width], third_i[:, :width]], axis=1)
    inner = flow_i + (middle_i + first_up.astype(f32) + third_up.astype(f32))
    low = flow_e[:, :width] + (
        middle_e[:, :width] + first_i[:, :width].astype(f32) + low_in.astype(f32)
    )
    high = flow_e[:, width:] + (
        middle_e[:, width:] + high_in.astype(f32) + third_i[:, width:].astype(f32)
    )
    grad_pre = join_rows(pres[0], pres[1], width)
    grad_half = join_rows(halves[0], halves[1], width)
    out_term = jnp.einsum("mpc,mpd->cd", gated, grad_half, preferred_element_type=f32)
    conv_term = jnp.einsum("mpc,mpd->cd", taps, grad_pre, preferred_element_type=f32)
    return (low, inner, high), conv_term, out_term


def split_near(flowing, middle, grad_first, grad_third, width):
    rows = grad_first.shape[1]
    low_in = shifted(grad_third[:, rows - width :], "seq", 1)
    high_in = shifted(grad_first[:, :width], "seq", -1)
    f32 = jnp.float32
    inner = flowing[:, width : rows - width] + (
        middle[:, width : rows - width]
        + grad_first[:, 2 * width :].astype(f32)
        + grad_third[:, : rows - 2 * width].astype(f32)
    )
    low = flowing[:, :width] + (
        middle[:, :width] + grad_first[:, width : 2 * width].astype(f32) + low_in.astype(f32)
    )
    high = flowing[:, rows - width :] + (
        middle[:, rows - width :]
        + high_in.astype(f32)
        + grad_third[:, rows - 2 * width : rows - width].astype(f32)
    )
    return low, inner, high


def halo_sides_pair(grad_first, grad_third, width):
    rows = grad_first.shape[1]
    from_low = shifted(grad_third[:, rows - width :], "seq", 1)
    from_high = shifted(grad_first[:, :width], "seq", -1)
    third_earlier = jnp.concatenate([from_low, grad_third[:, : rows - width]], axis=1)
    first_following = jnp.concatenate([grad_first[:, width:], from_high], axis=1)
    return third_earlier, first_following


def halving_scatter(parts, order):
    count = parts[0].shape[0]
    bits = count.bit_length() - 1
    rank = lax.axis_index("seq")
    parts = [p.reshape((2,) * bits + p.shape[1:]) for p in parts]
    left = list(reversed(range(bits)))
    for bit in order:
        axis = left.index(bit)
        left.pop(axis)
        own = ((rank >> bit) & 1) == 1
        pairs = [(j, j ^ (1 << bit)) for j in range(count)]
        lows = [lax.index_in_dim(p, 0, axis, keepdims=False) for p in parts]
        highs = [lax.index_in_dim(p, 1, axis, keepdims=False) for p in parts]
        sends = tuple(jnp.where(own, lo, hi).astype(jnp.bfloat16) for lo, hi in zip(lows, highs))
        got = lax.ppermute(sends, "seq", pairs)
        parts = [
            jnp.where(own, hi, lo) + g.astype(jnp.float32) for lo, hi, g in zip(lows, highs, got)
        ]
    return parts


def shards(section_inputs, cotangent, conv_weight, out_weight):
    batch_count = cotangent.shape[0]
    positions = cotangent.shape[1]
    channels = cotangent.shape[2]
    far_hops = FAR // positions
    seq_count = lax.axis_size("seq")
    section_count = lax.axis_size("section")
    section_rank = lax.axis_index("section")
    conv_mat = conv_weight[0]
    out_mat = out_weight[0]
    depth = conv_mat.shape[0]
    grad_scale = 1.0 / math.sqrt(batch_count * positions * seq_count)

    hidden = section_inputs[0]
    stored = []
    for layer in range(depth):
        if layer == 0:
            earlier, following = halo_sides(hidden, NEAR)
        else:
            earlier, following = far_sides(hidden, far_hops)
        hidden, saved = forward_layer(
            hidden, earlier, following, conv_mat[layer], out_mat[layer], layer + 1 == depth
        )
        stored.append(saved)

    top = jnp.where(section_rank == section_count - 1, 1.0, 0.0).astype(jnp.float32)
    flowing = cotangent.astype(jnp.float32) * top
    input_grads = None
    conv_acc = [None] * depth
    out_acc = [None] * depth
    for step in range(section_count):
        for layer in reversed(range(depth)):
            if layer == depth - 1 and step > 0:
                flowing, conv_term, out_term = backward_far(
                    flowing, stored[layer], conv_mat[layer], out_mat[layer], far_hops
                )
            elif layer == 0 and depth == 2 and step > 0:
                flowing, conv_term, out_term = backward_near_pieces(
                    flowing, stored[layer], conv_mat[layer], out_mat[layer]
                )
            else:
                flowing, conv_term, out_term = backward_layer(
                    flowing, stored[layer], conv_mat[layer], out_mat[layer], layer, far_hops
                )
            conv_acc[layer] = conv_term if step == 0 else conv_acc[layer] + conv_term
            out_acc[layer] = out_term if step == 0 else out_acc[layer] + out_term
        low, inner, high = flowing
        flowing = jnp.concatenate([low, inner, high], axis=1)
        input_grads = flowing if step == 0 else input_grads + flowing
        if step + 1 < section_count:
            bf16 = jnp.bfloat16
            inner = shifted(inner.astype(bf16), "section", -1)
            edges = shifted(jnp.concatenate([low, high], axis=1).astype(bf16), "section", -1)
            flowing = (edges.astype(jnp.float32), inner.astype(jnp.float32))

    conv_rows = 3 * channels // seq_count
    out_rows = channels // seq_count
    conv_all = jnp.concatenate(
        [acc.reshape(seq_count, conv_rows, 2 * channels) for acc in conv_acc], axis=1
    )
    out_all = jnp.concatenate(
        [acc.reshape(seq_count, out_rows, channels) for acc in out_acc], axis=1
    ).reshape(seq_count, depth * out_rows * channels // (2 * channels), 2 * channels)
    (mine,) = halving_scatter([jnp.concatenate([conv_all, out_all], axis=1)], (0, 3, 1, 2, 4))
    conv_grads = mine[: depth * conv_rows].reshape(1, depth, conv_rows, 2 * channels) * grad_scale
    out_grads = mine[depth * conv_rows :].reshape(1, depth, out_rows, channels) * grad_scale
    return (input_grads[None], conv_grads, out_grads)


def solution(mesh):
    return jax.shard_map(
        shards,
        mesh=mesh,
        in_specs=(
            P("section", None, "seq", None),
            P(None, "seq", None),
            P("section", None, None, None, None),
            P("section", None, None, None),
        ),
        out_specs=(
            P("section", None, "seq", None),
            P("section", None, "seq", None),
            P("section", None, "seq", None),
        ),
        check_vma=False,
    )
```

```python
import math

import jax
import jax.numpy as jnp
from jax import lax
from jax.sharding import PartitionSpec as P

NEAR = 128
FAR = 1024


def shifted(value, axis, steps):
    count = lax.axis_size(axis)
    leading, last = (max(0, -steps), min(count, count - steps))
    return lax.ppermute(value, axis, [(source, source + steps) for source in range(leading, last)])


def halo_sides(block, width):
    rows = block.shape[1]
    from_low = shifted(block[:, rows - width :], "seq", 1)
    from_high = shifted(block[:, :width], "seq", -1)
    earlier = jnp.concatenate([from_low, block[:, : rows - width]], axis=1)
    following = jnp.concatenate([block[:, width:], from_high], axis=1)
    return earlier, following


def far_sides(block, hops):
    return shifted(block, "seq", hops), shifted(block, "seq", -hops)


def mm(a, b):
    return jnp.einsum("mpc,cd->mpd", a, b, preferred_element_type=jnp.float32)


def forward_layer(hidden, earlier, following, conv, out_mat, last):
    chans = hidden.shape[2]
    preact = mm(earlier, conv[0])
    preact = preact + mm(hidden, conv[1])
    preact = preact + mm(following, conv[2])
    tanh_part = jnp.tanh(preact[..., :chans])
    sig_part = jax.nn.sigmoid(preact[..., chans:])
    gated = (tanh_part * sig_part).astype(jnp.bfloat16)
    factor_a = (1.0 - tanh_part * tanh_part) * sig_part
    factor_b = tanh_part * sig_part * (1.0 - sig_part)
    taps = jnp.concatenate([earlier, hidden, following], axis=2)
    saved = (taps, gated, factor_a, factor_b)
    if last:
        return None, saved
    nxt = (hidden.astype(jnp.float32) + mm(gated, out_mat)).astype(jnp.bfloat16)
    return nxt, saved


def backward_layer(flowing, saved, conv, out_mat, layer, far_hops):
    taps, gated, factor_a, factor_b = saved
    chans = flowing.shape[2]
    grad_half = flowing.astype(jnp.bfloat16)
    out_term = jnp.einsum("mpc,mpd->cd", gated, grad_half, preferred_element_type=jnp.float32)
    grad_gated = jnp.einsum("mpd,cd->mpc", grad_half, out_mat, preferred_element_type=jnp.float32)
    grad_pre = jnp.concatenate([grad_gated * factor_a, grad_gated * factor_b], axis=2).astype(
        jnp.bfloat16
    )
    conv_term = jnp.einsum("mpc,mpd->cd", taps, grad_pre, preferred_element_type=jnp.float32)
    weights = conv.reshape(3 * chans, 2 * chans)
    back = jnp.einsum("mpd,cd->mpc", grad_pre, weights, preferred_element_type=jnp.float32)
    grad_first = back[..., :chans].astype(jnp.bfloat16)
    middle = back[..., chans : 2 * chans]
    grad_third = back[..., 2 * chans :].astype(jnp.bfloat16)
    if layer == 0:
        return split_near(flowing, middle, grad_first, grad_third, NEAR), conv_term, out_term
    else:
        third_earlier = shifted(grad_third, "seq", far_hops)
        first_following = shifted(grad_first, "seq", -far_hops)
    grad_conv = middle + first_following.astype(jnp.float32) + third_earlier.astype(jnp.float32)
    return flowing + grad_conv, conv_term, out_term


def split_rows(value, width):
    return jnp.concatenate([value[:, :width], value[:, -width:]], axis=1), value[:, width:-width]


def join_rows(edges, inner, width):
    return jnp.concatenate([edges[:, :width], inner, edges[:, width:]], axis=1)


def backward_far(pieces, saved, conv, out_mat, far_hops):
    taps, gated, factor_a, factor_b = saved
    chans = pieces[0].shape[2]
    width = NEAR
    weights = conv.reshape(3 * chans, 2 * chans)
    f32 = jnp.float32
    factors = [split_rows(factor_a, width), split_rows(factor_b, width)]
    outs, pres, halves = [], [], []
    for index, flowing in enumerate(pieces):
        grad_half = flowing.astype(jnp.bfloat16)
        grad_gated = jnp.einsum("mpd,cd->mpc", grad_half, out_mat, preferred_element_type=f32)
        grad_pre = jnp.concatenate(
            [grad_gated * factors[0][index], grad_gated * factors[1][index]], axis=2
        ).astype(jnp.bfloat16)
        back = jnp.einsum("mpd,cd->mpc", grad_pre, weights, preferred_element_type=f32)
        grad_first = back[..., :chans].astype(jnp.bfloat16)
        middle = back[..., chans : 2 * chans]
        grad_third = back[..., 2 * chans :].astype(jnp.bfloat16)
        third_earlier = shifted(grad_third, "seq", far_hops)
        first_following = shifted(grad_first, "seq", -far_hops)
        outs.append(flowing + (middle + first_following.astype(f32) + third_earlier.astype(f32)))
        pres.append(grad_pre)
        halves.append(grad_half)
    grad_pre = join_rows(pres[0], pres[1], width)
    grad_half = join_rows(halves[0], halves[1], width)
    out_term = jnp.einsum("mpc,mpd->cd", gated, grad_half, preferred_element_type=f32)
    conv_term = jnp.einsum("mpc,mpd->cd", taps, grad_pre, preferred_element_type=f32)
    return tuple(outs), conv_term, out_term


def backward_near_pieces(pieces, saved, conv, out_mat):
    taps, gated, factor_a, factor_b = saved
    chans = pieces[0].shape[2]
    width = NEAR
    weights = conv.reshape(3 * chans, 2 * chans)
    f32 = jnp.float32
    factors = [split_rows(factor_a, width), split_rows(factor_b, width)]
    firsts, middles, thirds, pres, halves = [], [], [], [], []
    for index, flowing in enumerate(pieces):
        grad_half = flowing.astype(jnp.bfloat16)
        grad_gated = jnp.einsum("mpd,cd->mpc", grad_half, out_mat, preferred_element_type=f32)
        grad_pre = jnp.concatenate(
            [grad_gated * factors[0][index], grad_gated * factors[1][index]], axis=2
        ).astype(jnp.bfloat16)
        back = jnp.einsum("mpd,cd->mpc", grad_pre, weights, preferred_element_type=f32)
        firsts.append(back[..., :chans].astype(jnp.bfloat16))
        middles.append(back[..., chans : 2 * chans])
        thirds.append(back[..., 2 * chans :].astype(jnp.bfloat16))
        pres.append(grad_pre)
        halves.append(grad_half)
    (first_e, first_i), (third_e, third_i) = firsts, thirds
    (middle_e, middle_i), (flow_e, flow_i) = middles, pieces
    low_in = shifted(third_e[:, width:], "seq", 1)
    high_in = shifted(first_e[:, :width], "seq", -1)
    first_up = jnp.concatenate([first_i[:, width:], first_e[:, width:]], axis=1)
    third_up = jnp.concatenate([third_e[:, :width], third_i[:, :width]], axis=1)
    inner = flow_i + (middle_i + first_up.astype(f32) + third_up.astype(f32))
    low = flow_e[:, :width] + (
        middle_e[:, :width] + first_i[:, :width].astype(f32) + low_in.astype(f32)
    )
    high = flow_e[:, width:] + (
        middle_e[:, width:] + high_in.astype(f32) + third_i[:, width:].astype(f32)
    )
    grad_pre = join_rows(pres[0], pres[1], width)
    grad_half = join_rows(halves[0], halves[1], width)
    out_term = jnp.einsum("mpc,mpd->cd", gated, grad_half, preferred_element_type=f32)
    conv_term = jnp.einsum("mpc,mpd->cd", taps, grad_pre, preferred_element_type=f32)
    return (low, inner, high), conv_term, out_term


def split_near(flowing, middle, grad_first, grad_third, width):
    rows = grad_first.shape[1]
    low_in = shifted(grad_third[:, rows - width :], "seq", 1)
    high_in = shifted(grad_first[:, :width], "seq", -1)
    f32 = jnp.float32
    inner = flowing[:, width : rows - width] + (
        middle[:, width : rows - width]
        + grad_first[:, 2 * width :].astype(f32)
        + grad_third[:, : rows - 2 * width].astype(f32)
    )
    low = flowing[:, :width] + (
        middle[:, :width] + grad_first[:, width : 2 * width].astype(f32) + low_in.astype(f32)
    )
    high = flowing[:, rows - width :] + (
        middle[:, rows - width :]
        + high_in.astype(f32)
        + grad_third[:, rows - 2 * width : rows - width].astype(f32)
    )
    return low, inner, high


def halo_sides_pair(grad_first, grad_third, width):
    rows = grad_first.shape[1]
    from_low = shifted(grad_third[:, rows - width :], "seq", 1)
    from_high = shifted(grad_first[:, :width], "seq", -1)
    third_earlier = jnp.concatenate([from_low, grad_third[:, : rows - width]], axis=1)
    first_following = jnp.concatenate([grad_first[:, width:], from_high], axis=1)
    return third_earlier, first_following


def halving_scatter(parts, order):
    count = parts[0].shape[0]
    bits = count.bit_length() - 1
    rank = lax.axis_index("seq")
    parts = [p.reshape((2,) * bits + p.shape[1:]) for p in parts]
    left = list(reversed(range(bits)))
    for bit in order:
        axis = left.index(bit)
        left.pop(axis)
        own = ((rank >> bit) & 1) == 1
        pairs = [(j, j ^ (1 << bit)) for j in range(count)]
        lows = [lax.index_in_dim(p, 0, axis, keepdims=False) for p in parts]
        highs = [lax.index_in_dim(p, 1, axis, keepdims=False) for p in parts]
        sends = tuple(jnp.where(own, lo, hi).astype(jnp.bfloat16) for lo, hi in zip(lows, highs))
        got = lax.ppermute(sends, "seq", pairs)
        parts = [
            jnp.where(own, hi, lo) + g.astype(jnp.float32) for lo, hi, g in zip(lows, highs, got)
        ]
    return parts


def shards(section_inputs, cotangent, conv_weight, out_weight):
    batch_count = cotangent.shape[0]
    positions = cotangent.shape[1]
    channels = cotangent.shape[2]
    far_hops = FAR // positions
    seq_count = lax.axis_size("seq")
    section_count = lax.axis_size("section")
    section_rank = lax.axis_index("section")
    conv_mat = conv_weight[0]
    out_mat = out_weight[0]
    depth = conv_mat.shape[0]
    grad_scale = 1.0 / math.sqrt(batch_count * positions * seq_count)

    hidden = section_inputs[0]
    stored = []
    for layer in range(depth):
        if layer == 0:
            earlier, following = halo_sides(hidden, NEAR)
        else:
            earlier, following = far_sides(hidden, far_hops)
        hidden, saved = forward_layer(
            hidden, earlier, following, conv_mat[layer], out_mat[layer], layer + 1 == depth
        )
        stored.append(saved)

    top = jnp.where(section_rank == section_count - 1, 1.0, 0.0).astype(jnp.float32)
    flowing = cotangent.astype(jnp.float32) * top
    input_grads = None
    conv_acc = [None] * depth
    out_acc = [None] * depth
    for step in range(section_count):
        for layer in reversed(range(depth)):
            if layer == depth - 1 and step > 0:
                flowing, conv_term, out_term = backward_far(
                    flowing, stored[layer], conv_mat[layer], out_mat[layer], far_hops
                )
            elif layer == 0 and depth == 2 and step > 0:
                flowing, conv_term, out_term = backward_near_pieces(
                    flowing, stored[layer], conv_mat[layer], out_mat[layer]
                )
            else:
                flowing, conv_term, out_term = backward_layer(
                    flowing, stored[layer], conv_mat[layer], out_mat[layer], layer, far_hops
                )
            conv_acc[layer] = conv_term if step == 0 else conv_acc[layer] + conv_term
            out_acc[layer] = out_term if step == 0 else out_acc[layer] + out_term
        low, inner, high = flowing
        flowing = jnp.concatenate([low, inner, high], axis=1)
        input_grads = flowing if step == 0 else input_grads + flowing
        if step + 1 < section_count:
            bf16 = jnp.bfloat16
            inner = shifted(inner.astype(bf16), "section", -1)
            edges = shifted(jnp.concatenate([low, high], axis=1).astype(bf16), "section", -1)
            flowing = (edges.astype(jnp.float32), inner.astype(jnp.float32))

    conv_rows = 3 * channels // seq_count
    out_rows = channels // seq_count
    conv_all = jnp.concatenate(
        [acc.reshape(seq_count, conv_rows, 2 * channels) for acc in conv_acc], axis=1
    )
    out_all = jnp.concatenate(
        [acc.reshape(seq_count, out_rows, channels) for acc in out_acc], axis=1
    ).reshape(seq_count, depth * out_rows * channels // (2 * channels), 2 * channels)
    buffer = jnp.concatenate([conv_all, out_all], axis=1)
    buffer, input_grads = lax.optimization_barrier((buffer, input_grads))
    (mine,) = halving_scatter([buffer], (0, 1, 3, 2, 4))
    conv_grads = mine[: depth * conv_rows].reshape(1, depth, conv_rows, 2 * channels) * grad_scale
    out_grads = mine[depth * conv_rows :].reshape(1, depth, out_rows, channels) * grad_scale
    return (input_grads[None], conv_grads, out_grads)


def solution(mesh):
    return jax.shard_map(
        shards,
        mesh=mesh,
        in_specs=(
            P("section", None, "seq", None),
            P(None, "seq", None),
            P("section", None, None, None, None),
            P("section", None, None, None),
        ),
        out_specs=(
            P("section", None, "seq", None),
            P("section", None, "seq", None),
            P("section", None, "seq", None),
        ),
        check_vma=False,
    )
```

```python
import math

import jax
import jax.numpy as jnp
from jax import lax
from jax.sharding import PartitionSpec as P

NEAR = 128
FAR = 1024


def shifted(value, axis, steps):
    count = lax.axis_size(axis)
    leading, last = (max(0, -steps), min(count, count - steps))
    return lax.ppermute(value, axis, [(source, source + steps) for source in range(leading, last)])


def halo_sides(block, width):
    rows = block.shape[1]
    from_low = shifted(block[:, rows - width :], "seq", 1)
    from_high = shifted(block[:, :width], "seq", -1)
    earlier = jnp.concatenate([from_low, block[:, : rows - width]], axis=1)
    following = jnp.concatenate([block[:, width:], from_high], axis=1)
    return earlier, following


def far_sides(block, hops):
    return shifted(block, "seq", hops), shifted(block, "seq", -hops)


def mm(a, b):
    return jnp.einsum("mpc,cd->mpd", a, b, preferred_element_type=jnp.float32)


def forward_layer(hidden, earlier, following, conv, out_mat, last):
    chans = hidden.shape[2]
    preact = mm(earlier, conv[0])
    preact = preact + mm(hidden, conv[1])
    preact = preact + mm(following, conv[2])
    tanh_part = jnp.tanh(preact[..., :chans])
    sig_part = jax.nn.sigmoid(preact[..., chans:])
    gated = (tanh_part * sig_part).astype(jnp.bfloat16)
    factor_a = (1.0 - tanh_part * tanh_part) * sig_part
    factor_b = tanh_part * sig_part * (1.0 - sig_part)
    taps = jnp.concatenate([earlier, hidden, following], axis=2)
    saved = (taps, gated, factor_a, factor_b)
    if last:
        return None, saved
    nxt = (hidden.astype(jnp.float32) + mm(gated, out_mat)).astype(jnp.bfloat16)
    return nxt, saved


def backward_layer(flowing, saved, conv, out_mat, layer, far_hops):
    taps, gated, factor_a, factor_b = saved
    chans = flowing.shape[2]
    grad_half = flowing.astype(jnp.bfloat16)
    out_term = jnp.einsum("mpc,mpd->cd", gated, grad_half, preferred_element_type=jnp.float32)
    grad_gated = jnp.einsum("mpd,cd->mpc", grad_half, out_mat, preferred_element_type=jnp.float32)
    grad_pre = jnp.concatenate([grad_gated * factor_a, grad_gated * factor_b], axis=2).astype(
        jnp.bfloat16
    )
    conv_term = jnp.einsum("mpc,mpd->cd", taps, grad_pre, preferred_element_type=jnp.float32)
    weights = conv.reshape(3 * chans, 2 * chans)
    back = jnp.einsum("mpd,cd->mpc", grad_pre, weights, preferred_element_type=jnp.float32)
    grad_first = back[..., :chans].astype(jnp.bfloat16)
    middle = back[..., chans : 2 * chans]
    grad_third = back[..., 2 * chans :].astype(jnp.bfloat16)
    if layer == 0:
        return split_near(flowing, middle, grad_first, grad_third, NEAR), conv_term, out_term
    else:
        third_earlier = shifted(grad_third, "seq", far_hops)
        first_following = shifted(grad_first, "seq", -far_hops)
    grad_conv = middle + first_following.astype(jnp.float32) + third_earlier.astype(jnp.float32)
    return flowing + grad_conv, conv_term, out_term


def split_rows(value, width):
    return jnp.concatenate([value[:, :width], value[:, -width:]], axis=1), value[:, width:-width]


def join_rows(edges, inner, width):
    return jnp.concatenate([edges[:, :width], inner, edges[:, width:]], axis=1)


def piece_terms(taps, gated, pres, halves, width):
    f32 = jnp.float32
    taps_parts, gated_parts = split_rows(taps, width), split_rows(gated, width)
    out_term = sum(
        jnp.einsum("mpc,mpd->cd", g, h, preferred_element_type=f32)
        for g, h in zip(gated_parts, halves)
    )
    conv_term = sum(
        jnp.einsum("mpc,mpd->cd", t, p, preferred_element_type=f32)
        for t, p in zip(taps_parts, pres)
    )
    return out_term, conv_term


def backward_far(pieces, saved, conv, out_mat, far_hops):
    taps, gated, factor_a, factor_b = saved
    chans = pieces[0].shape[2]
    width = NEAR
    weights = conv.reshape(3 * chans, 2 * chans)
    f32 = jnp.float32
    factors = [split_rows(factor_a, width), split_rows(factor_b, width)]
    outs, pres, halves = [], [], []
    for index, flowing in enumerate(pieces):
        grad_half = flowing.astype(jnp.bfloat16)
        grad_gated = jnp.einsum("mpd,cd->mpc", grad_half, out_mat, preferred_element_type=f32)
        grad_pre = jnp.concatenate(
            [grad_gated * factors[0][index], grad_gated * factors[1][index]], axis=2
        ).astype(jnp.bfloat16)
        back = jnp.einsum("mpd,cd->mpc", grad_pre, weights, preferred_element_type=f32)
        grad_first = back[..., :chans].astype(jnp.bfloat16)
        middle = back[..., chans : 2 * chans]
        grad_third = back[..., 2 * chans :].astype(jnp.bfloat16)
        third_earlier = shifted(grad_third, "seq", far_hops)
        first_following = shifted(grad_first, "seq", -far_hops)
        outs.append(flowing + (middle + first_following.astype(f32) + third_earlier.astype(f32)))
        pres.append(grad_pre)
        halves.append(grad_half)
    out_term, conv_term = piece_terms(taps, gated, pres, halves, width)
    return tuple(outs), conv_term, out_term


def backward_near_pieces(pieces, saved, conv, out_mat):
    taps, gated, factor_a, factor_b = saved
    chans = pieces[0].shape[2]
    width = NEAR
    weights = conv.reshape(3 * chans, 2 * chans)
    f32 = jnp.float32
    factors = [split_rows(factor_a, width), split_rows(factor_b, width)]
    firsts, middles, thirds, pres, halves = [], [], [], [], []
    for index, flowing in enumerate(pieces):
        grad_half = flowing.astype(jnp.bfloat16)
        grad_gated = jnp.einsum("mpd,cd->mpc", grad_half, out_mat, preferred_element_type=f32)
        grad_pre = jnp.concatenate(
            [grad_gated * factors[0][index], grad_gated * factors[1][index]], axis=2
        ).astype(jnp.bfloat16)
        back = jnp.einsum("mpd,cd->mpc", grad_pre, weights, preferred_element_type=f32)
        firsts.append(back[..., :chans].astype(jnp.bfloat16))
        middles.append(back[..., chans : 2 * chans])
        thirds.append(back[..., 2 * chans :].astype(jnp.bfloat16))
        pres.append(grad_pre)
        halves.append(grad_half)
    (first_e, first_i), (third_e, third_i) = firsts, thirds
    (middle_e, middle_i), (flow_e, flow_i) = middles, pieces
    low_in = shifted(third_e[:, width:], "seq", 1)
    high_in = shifted(first_e[:, :width], "seq", -1)
    first_up = jnp.concatenate([first_i[:, width:], first_e[:, width:]], axis=1)
    third_up = jnp.concatenate([third_e[:, :width], third_i[:, :width]], axis=1)
    inner = flow_i + (middle_i + first_up.astype(f32) + third_up.astype(f32))
    low = flow_e[:, :width] + (
        middle_e[:, :width] + first_i[:, :width].astype(f32) + low_in.astype(f32)
    )
    high = flow_e[:, width:] + (
        middle_e[:, width:] + high_in.astype(f32) + third_i[:, width:].astype(f32)
    )
    out_term, conv_term = piece_terms(taps, gated, pres, halves, width)
    return (low, inner, high), conv_term, out_term


def split_near(flowing, middle, grad_first, grad_third, width):
    rows = grad_first.shape[1]
    low_in = shifted(grad_third[:, rows - width :], "seq", 1)
    high_in = shifted(grad_first[:, :width], "seq", -1)
    f32 = jnp.float32
    inner = flowing[:, width : rows - width] + (
        middle[:, width : rows - width]
        + grad_first[:, 2 * width :].astype(f32)
        + grad_third[:, : rows - 2 * width].astype(f32)
    )
    low = flowing[:, :width] + (
        middle[:, :width] + grad_first[:, width : 2 * width].astype(f32) + low_in.astype(f32)
    )
    high = flowing[:, rows - width :] + (
        middle[:, rows - width :]
        + high_in.astype(f32)
        + grad_third[:, rows - 2 * width : rows - width].astype(f32)
    )
    return low, inner, high


def halo_sides_pair(grad_first, grad_third, width):
    rows = grad_first.shape[1]
    from_low = shifted(grad_third[:, rows - width :], "seq", 1)
    from_high = shifted(grad_first[:, :width], "seq", -1)
    third_earlier = jnp.concatenate([from_low, grad_third[:, : rows - width]], axis=1)
    first_following = jnp.concatenate([grad_first[:, width:], from_high], axis=1)
    return third_earlier, first_following


def halving_scatter(parts, order):
    count = parts[0].shape[0]
    bits = count.bit_length() - 1
    rank = lax.axis_index("seq")
    parts = [p.reshape((2,) * bits + p.shape[1:]) for p in parts]
    left = list(reversed(range(bits)))
    for bit in order:
        axis = left.index(bit)
        left.pop(axis)
        own = ((rank >> bit) & 1) == 1
        pairs = [(j, j ^ (1 << bit)) for j in range(count)]
        lows = [lax.index_in_dim(p, 0, axis, keepdims=False) for p in parts]
        highs = [lax.index_in_dim(p, 1, axis, keepdims=False) for p in parts]
        sends = tuple(jnp.where(own, lo, hi).astype(jnp.bfloat16) for lo, hi in zip(lows, highs))
        got = lax.ppermute(sends, "seq", pairs)
        parts = [
            jnp.where(own, hi, lo) + g.astype(jnp.float32) for lo, hi, g in zip(lows, highs, got)
        ]
    return parts


def shards(section_inputs, cotangent, conv_weight, out_weight):
    batch_count = cotangent.shape[0]
    positions = cotangent.shape[1]
    channels = cotangent.shape[2]
    far_hops = FAR // positions
    seq_count = lax.axis_size("seq")
    section_count = lax.axis_size("section")
    section_rank = lax.axis_index("section")
    conv_mat = conv_weight[0]
    out_mat = out_weight[0]
    depth = conv_mat.shape[0]
    grad_scale = 1.0 / math.sqrt(batch_count * positions * seq_count)

    hidden = section_inputs[0]
    stored = []
    for layer in range(depth):
        if layer == 0:
            earlier, following = halo_sides(hidden, NEAR)
        else:
            earlier, following = far_sides(hidden, far_hops)
        hidden, saved = forward_layer(
            hidden, earlier, following, conv_mat[layer], out_mat[layer], layer + 1 == depth
        )
        stored.append(saved)

    top = jnp.where(section_rank == section_count - 1, 1.0, 0.0).astype(jnp.float32)
    flowing = cotangent.astype(jnp.float32) * top
    input_grads = None
    conv_acc = [None] * depth
    out_acc = [None] * depth
    for step in range(section_count):
        for layer in reversed(range(depth)):
            if layer == depth - 1 and step > 0:
                flowing, conv_term, out_term = backward_far(
                    flowing, stored[layer], conv_mat[layer], out_mat[layer], far_hops
                )
            elif layer == 0 and depth == 2 and step > 0:
                flowing, conv_term, out_term = backward_near_pieces(
                    flowing, stored[layer], conv_mat[layer], out_mat[layer]
                )
            else:
                flowing, conv_term, out_term = backward_layer(
                    flowing, stored[layer], conv_mat[layer], out_mat[layer], layer, far_hops
                )
            conv_acc[layer] = conv_term if step == 0 else conv_acc[layer] + conv_term
            out_acc[layer] = out_term if step == 0 else out_acc[layer] + out_term
        low, inner, high = flowing
        flowing = jnp.concatenate([low, inner, high], axis=1)
        input_grads = flowing if step == 0 else input_grads + flowing
        if step + 1 < section_count:
            bf16 = jnp.bfloat16
            inner = shifted(inner.astype(bf16), "section", -1)
            edges = shifted(jnp.concatenate([low, high], axis=1).astype(bf16), "section", -1)
            flowing = (edges.astype(jnp.float32), inner.astype(jnp.float32))

    conv_rows = 3 * channels // seq_count
    out_rows = channels // seq_count
    conv_all = jnp.concatenate(
        [acc.reshape(seq_count, conv_rows, 2 * channels) for acc in conv_acc], axis=1
    )
    out_all = jnp.concatenate(
        [acc.reshape(seq_count, out_rows, channels) for acc in out_acc], axis=1
    ).reshape(seq_count, depth * out_rows * channels // (2 * channels), 2 * channels)
    (mine,) = halving_scatter([jnp.concatenate([conv_all, out_all], axis=1)], (0, 1, 3, 2, 4))
    conv_grads = mine[: depth * conv_rows].reshape(1, depth, conv_rows, 2 * channels) * grad_scale
    out_grads = mine[depth * conv_rows :].reshape(1, depth, out_rows, channels) * grad_scale
    return (input_grads[None], conv_grads, out_grads)


def solution(mesh):
    return jax.shard_map(
        shards,
        mesh=mesh,
        in_specs=(
            P("section", None, "seq", None),
            P(None, "seq", None),
            P("section", None, None, None, None),
            P("section", None, None, None),
        ),
        out_specs=(
            P("section", None, "seq", None),
            P("section", None, "seq", None),
            P("section", None, "seq", None),
        ),
        check_vma=False,
    )
```

```python
import math

import jax
import jax.numpy as jnp
from jax import lax
from jax.sharding import PartitionSpec as P

NEAR = 128
FAR = 1024


def shifted(value, axis, steps):
    count = lax.axis_size(axis)
    leading, last = (max(0, -steps), min(count, count - steps))
    return lax.ppermute(value, axis, [(source, source + steps) for source in range(leading, last)])


def halo_sides(block, width):
    rows = block.shape[1]
    from_low = shifted(block[:, rows - width :], "seq", 1)
    from_high = shifted(block[:, :width], "seq", -1)
    earlier = jnp.concatenate([from_low, block[:, : rows - width]], axis=1)
    following = jnp.concatenate([block[:, width:], from_high], axis=1)
    return earlier, following


def far_sides(block, hops):
    return shifted(block, "seq", hops), shifted(block, "seq", -hops)


def mm(a, b):
    return jnp.einsum("mpc,cd->mpd", a, b, preferred_element_type=jnp.float32)


def forward_layer(hidden, earlier, following, conv, out_mat, last):
    chans = hidden.shape[2]
    preact = mm(earlier, conv[0])
    preact = preact + mm(hidden, conv[1])
    preact = preact + mm(following, conv[2])
    tanh_part = jnp.tanh(preact[..., :chans])
    sig_part = jax.nn.sigmoid(preact[..., chans:])
    gated = (tanh_part * sig_part).astype(jnp.bfloat16)
    factor_a = (1.0 - tanh_part * tanh_part) * sig_part
    factor_b = tanh_part * sig_part * (1.0 - sig_part)
    taps = jnp.concatenate([earlier, hidden, following], axis=2)
    saved = (taps, gated, factor_a, factor_b)
    if last:
        return None, saved
    nxt = (hidden.astype(jnp.float32) + mm(gated, out_mat)).astype(jnp.bfloat16)
    return nxt, saved


def backward_layer(flowing, saved, conv, out_mat, layer, far_hops):
    taps, gated, factor_a, factor_b = saved
    chans = flowing.shape[2]
    grad_half = flowing.astype(jnp.bfloat16)
    out_term = jnp.einsum("mpc,mpd->cd", gated, grad_half, preferred_element_type=jnp.float32)
    grad_gated = jnp.einsum("mpd,cd->mpc", grad_half, out_mat, preferred_element_type=jnp.float32)
    grad_pre = jnp.concatenate([grad_gated * factor_a, grad_gated * factor_b], axis=2).astype(
        jnp.bfloat16
    )
    conv_term = jnp.einsum("mpc,mpd->cd", taps, grad_pre, preferred_element_type=jnp.float32)
    weights = conv.reshape(3 * chans, 2 * chans)
    back = jnp.einsum("mpd,cd->mpc", grad_pre, weights, preferred_element_type=jnp.float32)
    grad_first = back[..., :chans].astype(jnp.bfloat16)
    middle = back[..., chans : 2 * chans]
    grad_third = back[..., 2 * chans :].astype(jnp.bfloat16)
    if layer == 0:
        return split_near(flowing, middle, grad_first, grad_third, NEAR), conv_term, out_term
    else:
        third_earlier = shifted(grad_third, "seq", far_hops)
        first_following = shifted(grad_first, "seq", -far_hops)
    grad_conv = middle + first_following.astype(jnp.float32) + third_earlier.astype(jnp.float32)
    return flowing + grad_conv, conv_term, out_term


def split_rows(value, width):
    return jnp.concatenate([value[:, :width], value[:, -width:]], axis=1), value[:, width:-width]


def join_rows(edges, inner, width):
    return jnp.concatenate([edges[:, :width], inner, edges[:, width:]], axis=1)


def backward_far(pieces, saved, conv, out_mat, far_hops):
    taps, gated, factor_a, factor_b = saved
    chans = pieces[0].shape[2]
    width = NEAR
    weights = conv.reshape(3 * chans, 2 * chans)
    f32 = jnp.float32
    factors = [split_rows(factor_a, width), split_rows(factor_b, width)]
    outs, pres, halves = [], [], []
    for index, flowing in enumerate(pieces):
        grad_half = flowing.astype(jnp.bfloat16)
        grad_gated = jnp.einsum("mpd,cd->mpc", grad_half, out_mat, preferred_element_type=f32)
        grad_pre = jnp.concatenate(
            [grad_gated * factors[0][index], grad_gated * factors[1][index]], axis=2
        ).astype(jnp.bfloat16)
        back = jnp.einsum("mpd,cd->mpc", grad_pre, weights, preferred_element_type=f32)
        grad_first = back[..., :chans].astype(jnp.bfloat16)
        middle = back[..., chans : 2 * chans]
        grad_third = back[..., 2 * chans :].astype(jnp.bfloat16)
        third_earlier = shifted(grad_third, "seq", far_hops)
        first_following = shifted(grad_first, "seq", -far_hops)
        outs.append(flowing + (middle + first_following.astype(f32) + third_earlier.astype(f32)))
        pres.append(grad_pre)
        halves.append(grad_half)
    grad_pre = join_rows(pres[0], pres[1], width)
    grad_half = join_rows(halves[0], halves[1], width)
    out_term = jnp.einsum("mpc,mpd->cd", gated, grad_half, preferred_element_type=f32)
    conv_term = jnp.einsum("mpc,mpd->cd", taps, grad_pre, preferred_element_type=f32)
    return tuple(outs), conv_term, out_term


def backward_near_pieces(pieces, saved, conv, out_mat):
    taps, gated, factor_a, factor_b = saved
    chans = pieces[0].shape[2]
    width = NEAR
    weights = conv.reshape(3 * chans, 2 * chans)
    f32 = jnp.float32
    factors = [split_rows(factor_a, width), split_rows(factor_b, width)]
    firsts, middles, thirds, pres, halves = [], [], [], [], []
    for index, flowing in enumerate(pieces):
        grad_half = flowing.astype(jnp.bfloat16)
        grad_gated = jnp.einsum("mpd,cd->mpc", grad_half, out_mat, preferred_element_type=f32)
        grad_pre = jnp.concatenate(
            [grad_gated * factors[0][index], grad_gated * factors[1][index]], axis=2
        ).astype(jnp.bfloat16)
        back = jnp.einsum("mpd,cd->mpc", grad_pre, weights, preferred_element_type=f32)
        firsts.append(back[..., :chans].astype(jnp.bfloat16))
        middles.append(back[..., chans : 2 * chans])
        thirds.append(back[..., 2 * chans :].astype(jnp.bfloat16))
        pres.append(grad_pre)
        halves.append(grad_half)
    (first_e, first_i), (third_e, third_i) = firsts, thirds
    (middle_e, middle_i), (flow_e, flow_i) = middles, pieces
    low_in = shifted(third_e[:, width:], "seq", 1)
    high_in = shifted(first_e[:, :width], "seq", -1)
    first_up = jnp.concatenate([first_i[:, width:], first_e[:, width:]], axis=1)
    third_up = jnp.concatenate([third_e[:, :width], third_i[:, :width]], axis=1)
    inner = flow_i + (middle_i + first_up.astype(f32) + third_up.astype(f32))
    low = flow_e[:, :width] + (
        middle_e[:, :width] + first_i[:, :width].astype(f32) + low_in.astype(f32)
    )
    high = flow_e[:, width:] + (
        middle_e[:, width:] + high_in.astype(f32) + third_i[:, width:].astype(f32)
    )
    grad_pre = join_rows(pres[0], pres[1], width)
    grad_half = join_rows(halves[0], halves[1], width)
    out_term = jnp.einsum("mpc,mpd->cd", gated, grad_half, preferred_element_type=f32)
    conv_term = jnp.einsum("mpc,mpd->cd", taps, grad_pre, preferred_element_type=f32)
    return (low, inner, high), conv_term, out_term


def split_near(flowing, middle, grad_first, grad_third, width):
    rows = grad_first.shape[1]
    low_in = shifted(grad_third[:, rows - width :], "seq", 1)
    high_in = shifted(grad_first[:, :width], "seq", -1)
    f32 = jnp.float32
    inner = flowing[:, width : rows - width] + (
        middle[:, width : rows - width]
        + grad_first[:, 2 * width :].astype(f32)
        + grad_third[:, : rows - 2 * width].astype(f32)
    )
    low = flowing[:, :width] + (
        middle[:, :width] + grad_first[:, width : 2 * width].astype(f32) + low_in.astype(f32)
    )
    high = flowing[:, rows - width :] + (
        middle[:, rows - width :]
        + high_in.astype(f32)
        + grad_third[:, rows - 2 * width : rows - width].astype(f32)
    )
    return low, inner, high


def halo_sides_pair(grad_first, grad_third, width):
    rows = grad_first.shape[1]
    from_low = shifted(grad_third[:, rows - width :], "seq", 1)
    from_high = shifted(grad_first[:, :width], "seq", -1)
    third_earlier = jnp.concatenate([from_low, grad_third[:, : rows - width]], axis=1)
    first_following = jnp.concatenate([grad_first[:, width:], from_high], axis=1)
    return third_earlier, first_following


def halving_scatter(parts, order):
    count = parts[0].shape[0]
    bits = count.bit_length() - 1
    rank = lax.axis_index("seq")
    parts = [p.reshape((2,) * bits + p.shape[1:]) for p in parts]
    left = list(reversed(range(bits)))
    for bit in order:
        axis = left.index(bit)
        left.pop(axis)
        own = ((rank >> bit) & 1) == 1
        pairs = [(j, j ^ (1 << bit)) for j in range(count)]
        lows = [lax.index_in_dim(p, 0, axis, keepdims=False) for p in parts]
        highs = [lax.index_in_dim(p, 1, axis, keepdims=False) for p in parts]
        sends = tuple(jnp.where(own, lo, hi).astype(jnp.bfloat16) for lo, hi in zip(lows, highs))
        got = lax.ppermute(sends, "seq", pairs)
        parts = [
            jnp.where(own, hi, lo) + g.astype(jnp.float32) for lo, hi, g in zip(lows, highs, got)
        ]
    return parts


def shards(section_inputs, cotangent, conv_weight, out_weight):
    batch_count = cotangent.shape[0]
    positions = cotangent.shape[1]
    channels = cotangent.shape[2]
    far_hops = FAR // positions
    seq_count = lax.axis_size("seq")
    section_count = lax.axis_size("section")
    section_rank = lax.axis_index("section")
    conv_mat = conv_weight[0]
    out_mat = out_weight[0]
    depth = conv_mat.shape[0]
    grad_scale = 1.0 / math.sqrt(batch_count * positions * seq_count)

    hidden = section_inputs[0]
    stored = []
    for layer in range(depth):
        if layer == 0:
            earlier, following = halo_sides(hidden, NEAR)
        else:
            earlier, following = far_sides(hidden, far_hops)
        hidden, saved = forward_layer(
            hidden, earlier, following, conv_mat[layer], out_mat[layer], layer + 1 == depth
        )
        stored.append(saved)

    top = jnp.where(section_rank == section_count - 1, 1.0, 0.0).astype(jnp.float32)
    flowing = cotangent.astype(jnp.float32) * top
    input_grads = None
    conv_acc = [None] * depth
    out_acc = [None] * depth
    for step in range(section_count):
        for layer in reversed(range(depth)):
            if layer == depth - 1 and step > 0:
                flowing, conv_term, out_term = backward_far(
                    flowing, stored[layer], conv_mat[layer], out_mat[layer], far_hops
                )
            elif layer == 0 and depth == 2 and step > 0:
                flowing, conv_term, out_term = backward_near_pieces(
                    flowing, stored[layer], conv_mat[layer], out_mat[layer]
                )
            else:
                flowing, conv_term, out_term = backward_layer(
                    flowing, stored[layer], conv_mat[layer], out_mat[layer], layer, far_hops
                )
            conv_acc[layer] = conv_term if step == 0 else conv_acc[layer] + conv_term
            out_acc[layer] = out_term if step == 0 else out_acc[layer] + out_term
        low, inner, high = flowing
        flowing = jnp.concatenate([low, inner, high], axis=1)
        input_grads = flowing if step == 0 else input_grads + flowing
        if step + 1 < section_count:
            bf16 = jnp.bfloat16
            inner = shifted(inner.astype(bf16), "section", -1)
            edges = shifted(jnp.concatenate([low, high], axis=1).astype(bf16), "section", -1)
            flowing = (edges.astype(jnp.float32), inner.astype(jnp.float32))

    conv_rows = 3 * channels // seq_count
    out_rows = channels // seq_count
    conv_all = jnp.concatenate(
        [acc.reshape(seq_count, conv_rows, 2 * channels) for acc in conv_acc], axis=1
    )
    out_all = jnp.concatenate(
        [acc.reshape(seq_count, out_rows, channels) for acc in out_acc], axis=1
    ).reshape(seq_count, depth * out_rows * channels // (2 * channels), 2 * channels)
    (mine,) = halving_scatter([jnp.concatenate([conv_all, out_all], axis=1)], (0, 1, 3, 4, 2))
    conv_grads = mine[: depth * conv_rows].reshape(1, depth, conv_rows, 2 * channels) * grad_scale
    out_grads = mine[depth * conv_rows :].reshape(1, depth, out_rows, channels) * grad_scale
    return (input_grads[None], conv_grads, out_grads)


def solution(mesh):
    return jax.shard_map(
        shards,
        mesh=mesh,
        in_specs=(
            P("section", None, "seq", None),
            P(None, "seq", None),
            P("section", None, None, None, None),
            P("section", None, None, None),
        ),
        out_specs=(
            P("section", None, "seq", None),
            P("section", None, "seq", None),
            P("section", None, "seq", None),
        ),
        check_vma=False,
    )
```

```python
import math

import jax
import jax.numpy as jnp
from jax import lax
from jax.sharding import PartitionSpec as P

NEAR = 128
FAR = 1024


def shifted(value, axis, steps):
    count = lax.axis_size(axis)
    leading, last = (max(0, -steps), min(count, count - steps))
    return lax.ppermute(value, axis, [(source, source + steps) for source in range(leading, last)])


def halo_sides(block, width):
    rows = block.shape[1]
    from_low = shifted(block[:, rows - width :], "seq", 1)
    from_high = shifted(block[:, :width], "seq", -1)
    earlier = jnp.concatenate([from_low, block[:, : rows - width]], axis=1)
    following = jnp.concatenate([block[:, width:], from_high], axis=1)
    return earlier, following


def far_sides(block, hops):
    return shifted(block, "seq", hops), shifted(block, "seq", -hops)


def mm(a, b):
    return jnp.einsum("mpc,cd->mpd", a, b, preferred_element_type=jnp.float32)


def forward_layer(hidden, earlier, following, conv, out_mat, last):
    chans = hidden.shape[2]
    preact = mm(earlier, conv[0])
    preact = preact + mm(hidden, conv[1])
    preact = preact + mm(following, conv[2])
    tanh_part = jnp.tanh(preact[..., :chans])
    sig_part = jax.nn.sigmoid(preact[..., chans:])
    gated = (tanh_part * sig_part).astype(jnp.bfloat16)
    factor_a = (1.0 - tanh_part * tanh_part) * sig_part
    factor_b = tanh_part * sig_part * (1.0 - sig_part)
    taps = jnp.concatenate([earlier, hidden, following], axis=2)
    saved = (taps, gated, factor_a, factor_b)
    if last:
        return None, saved
    nxt = (hidden.astype(jnp.float32) + mm(gated, out_mat)).astype(jnp.bfloat16)
    return nxt, saved


def backward_layer(flowing, saved, conv, out_mat, layer, far_hops):
    taps, gated, factor_a, factor_b = saved
    chans = flowing.shape[2]
    grad_half = flowing.astype(jnp.bfloat16)
    out_term = jnp.einsum("mpc,mpd->cd", gated, grad_half, preferred_element_type=jnp.float32)
    grad_gated = jnp.einsum("mpd,cd->mpc", grad_half, out_mat, preferred_element_type=jnp.float32)
    grad_pre = jnp.concatenate([grad_gated * factor_a, grad_gated * factor_b], axis=2).astype(
        jnp.bfloat16
    )
    conv_term = jnp.einsum("mpc,mpd->cd", taps, grad_pre, preferred_element_type=jnp.float32)
    weights = conv.reshape(3 * chans, 2 * chans)
    back = jnp.einsum("mpd,cd->mpc", grad_pre, weights, preferred_element_type=jnp.float32)
    grad_first = back[..., :chans].astype(jnp.bfloat16)
    middle = back[..., chans : 2 * chans]
    grad_third = back[..., 2 * chans :].astype(jnp.bfloat16)
    if layer == 0:
        return split_near(flowing, middle, grad_first, grad_third, NEAR), conv_term, out_term
    else:
        third_earlier = shifted(grad_third, "seq", far_hops)
        first_following = shifted(grad_first, "seq", -far_hops)
    grad_conv = middle + first_following.astype(jnp.float32) + third_earlier.astype(jnp.float32)
    return flowing + grad_conv, conv_term, out_term


def split_rows(value, width):
    return jnp.concatenate([value[:, :width], value[:, -width:]], axis=1), value[:, width:-width]


def join_rows(edges, inner, width):
    return jnp.concatenate([edges[:, :width], inner, edges[:, width:]], axis=1)


def backward_far(pieces, saved, conv, out_mat, far_hops):
    taps, gated, factor_a, factor_b = saved
    chans = pieces[0].shape[2]
    width = NEAR
    weights = conv.reshape(3 * chans, 2 * chans)
    f32 = jnp.float32
    factors = [split_rows(factor_a, width), split_rows(factor_b, width)]
    outs, pres, halves = [], [], []
    for index, flowing in enumerate(pieces):
        grad_half = flowing.astype(jnp.bfloat16)
        grad_gated = jnp.einsum("mpd,cd->mpc", grad_half, out_mat, preferred_element_type=f32)
        grad_pre = jnp.concatenate(
            [grad_gated * factors[0][index], grad_gated * factors[1][index]], axis=2
        ).astype(jnp.bfloat16)
        back = jnp.einsum("mpd,cd->mpc", grad_pre, weights, preferred_element_type=f32)
        grad_first = back[..., :chans].astype(jnp.bfloat16)
        middle = back[..., chans : 2 * chans]
        grad_third = back[..., 2 * chans :].astype(jnp.bfloat16)
        third_earlier = shifted(grad_third, "seq", far_hops)
        first_following = shifted(grad_first, "seq", -far_hops)
        outs.append(flowing + (middle + first_following.astype(f32) + third_earlier.astype(f32)))
        pres.append(grad_pre)
        halves.append(grad_half)
    grad_pre = join_rows(pres[0], pres[1], width)
    grad_half = join_rows(halves[0], halves[1], width)
    out_term = jnp.einsum("mpc,mpd->cd", gated, grad_half, preferred_element_type=f32)
    conv_term = jnp.einsum("mpc,mpd->cd", taps, grad_pre, preferred_element_type=f32)
    return tuple(outs), conv_term, out_term


def backward_near_pieces(pieces, saved, conv, out_mat):
    taps, gated, factor_a, factor_b = saved
    chans = pieces[0].shape[2]
    width = NEAR
    weights = conv.reshape(3 * chans, 2 * chans)
    f32 = jnp.float32
    factors = [split_rows(factor_a, width), split_rows(factor_b, width)]
    firsts, middles, thirds, pres, halves = [], [], [], [], []
    for index, flowing in enumerate(pieces):
        grad_half = flowing.astype(jnp.bfloat16)
        grad_gated = jnp.einsum("mpd,cd->mpc", grad_half, out_mat, preferred_element_type=f32)
        grad_pre = jnp.concatenate(
            [grad_gated * factors[0][index], grad_gated * factors[1][index]], axis=2
        ).astype(jnp.bfloat16)
        back = jnp.einsum("mpd,cd->mpc", grad_pre, weights, preferred_element_type=f32)
        firsts.append(back[..., :chans].astype(jnp.bfloat16))
        middles.append(back[..., chans : 2 * chans])
        thirds.append(back[..., 2 * chans :].astype(jnp.bfloat16))
        pres.append(grad_pre)
        halves.append(grad_half)
    (first_e, first_i), (third_e, third_i) = firsts, thirds
    (middle_e, middle_i), (flow_e, flow_i) = middles, pieces
    low_in = shifted(third_e[:, width:], "seq", 1)
    high_in = shifted(first_e[:, :width], "seq", -1)
    first_up = jnp.concatenate([first_i[:, width:], first_e[:, width:]], axis=1)
    third_up = jnp.concatenate([third_e[:, :width], third_i[:, :width]], axis=1)
    inner = flow_i + (middle_i + first_up.astype(f32) + third_up.astype(f32))
    low = flow_e[:, :width] + (
        middle_e[:, :width] + first_i[:, :width].astype(f32) + low_in.astype(f32)
    )
    high = flow_e[:, width:] + (
        middle_e[:, width:] + high_in.astype(f32) + third_i[:, width:].astype(f32)
    )
    grad_pre = join_rows(pres[0], pres[1], width)
    grad_half = join_rows(halves[0], halves[1], width)
    out_term = jnp.einsum("mpc,mpd->cd", gated, grad_half, preferred_element_type=f32)
    conv_term = jnp.einsum("mpc,mpd->cd", taps, grad_pre, preferred_element_type=f32)
    return (low, inner, high), conv_term, out_term


def split_near(flowing, middle, grad_first, grad_third, width):
    rows = grad_first.shape[1]
    low_in = shifted(grad_third[:, rows - width :], "seq", 1)
    high_in = shifted(grad_first[:, :width], "seq", -1)
    f32 = jnp.float32
    inner = flowing[:, width : rows - width] + (
        middle[:, width : rows - width]
        + grad_first[:, 2 * width :].astype(f32)
        + grad_third[:, : rows - 2 * width].astype(f32)
    )
    low = flowing[:, :width] + (
        middle[:, :width] + grad_first[:, width : 2 * width].astype(f32) + low_in.astype(f32)
    )
    high = flowing[:, rows - width :] + (
        middle[:, rows - width :]
        + high_in.astype(f32)
        + grad_third[:, rows - 2 * width : rows - width].astype(f32)
    )
    return low, inner, high


def halo_sides_pair(grad_first, grad_third, width):
    rows = grad_first.shape[1]
    from_low = shifted(grad_third[:, rows - width :], "seq", 1)
    from_high = shifted(grad_first[:, :width], "seq", -1)
    third_earlier = jnp.concatenate([from_low, grad_third[:, : rows - width]], axis=1)
    first_following = jnp.concatenate([grad_first[:, width:], from_high], axis=1)
    return third_earlier, first_following


def halving_scatter(parts, order):
    count = parts[0].shape[0]
    bits = count.bit_length() - 1
    rank = lax.axis_index("seq")
    parts = [p.reshape((2,) * bits + p.shape[1:]) for p in parts]
    left = list(reversed(range(bits)))
    for bit in order:
        axis = left.index(bit)
        left.pop(axis)
        own = ((rank >> bit) & 1) == 1
        pairs = [(j, j ^ (1 << bit)) for j in range(count)]
        lows = [lax.index_in_dim(p, 0, axis, keepdims=False) for p in parts]
        highs = [lax.index_in_dim(p, 1, axis, keepdims=False) for p in parts]
        sends = tuple(jnp.where(own, lo, hi).astype(jnp.bfloat16) for lo, hi in zip(lows, highs))
        got = lax.ppermute(sends, "seq", pairs)
        parts = [
            jnp.where(own, hi, lo) + g.astype(jnp.float32) for lo, hi, g in zip(lows, highs, got)
        ]
    return parts


def shards(section_inputs, cotangent, conv_weight, out_weight):
    batch_count = cotangent.shape[0]
    positions = cotangent.shape[1]
    channels = cotangent.shape[2]
    far_hops = FAR // positions
    seq_count = lax.axis_size("seq")
    section_count = lax.axis_size("section")
    section_rank = lax.axis_index("section")
    conv_mat = conv_weight[0]
    out_mat = out_weight[0]
    depth = conv_mat.shape[0]
    grad_scale = 1.0 / math.sqrt(batch_count * positions * seq_count)

    hidden = section_inputs[0]
    stored = []
    for layer in range(depth):
        if layer == 0:
            earlier, following = halo_sides(hidden, NEAR)
        else:
            earlier, following = far_sides(hidden, far_hops)
        hidden, saved = forward_layer(
            hidden, earlier, following, conv_mat[layer], out_mat[layer], layer + 1 == depth
        )
        stored.append(saved)

    top = jnp.where(section_rank == section_count - 1, 1.0, 0.0).astype(jnp.float32)
    flowing = cotangent.astype(jnp.float32) * top
    input_grads = None
    conv_acc = [None] * depth
    out_acc = [None] * depth
    for step in range(section_count):
        for layer in reversed(range(depth)):
            if layer == depth - 1 and step > 0:
                flowing, conv_term, out_term = backward_far(
                    flowing, stored[layer], conv_mat[layer], out_mat[layer], far_hops
                )
            elif layer == 0 and depth == 2 and 0 < step < section_count - 1:
                flowing, conv_term, out_term = backward_near_pieces(
                    flowing, stored[layer], conv_mat[layer], out_mat[layer]
                )
            else:
                if isinstance(flowing, tuple):
                    flowing = join_rows(flowing[0], flowing[1], NEAR)
                flowing, conv_term, out_term = backward_layer(
                    flowing, stored[layer], conv_mat[layer], out_mat[layer], layer, far_hops
                )
            conv_acc[layer] = conv_term if step == 0 else conv_acc[layer] + conv_term
            out_acc[layer] = out_term if step == 0 else out_acc[layer] + out_term
        low, inner, high = flowing
        flowing = jnp.concatenate([low, inner, high], axis=1)
        input_grads = flowing if step == 0 else input_grads + flowing
        if step + 1 < section_count:
            bf16 = jnp.bfloat16
            inner = shifted(inner.astype(bf16), "section", -1)
            edges = shifted(jnp.concatenate([low, high], axis=1).astype(bf16), "section", -1)
            flowing = (edges.astype(jnp.float32), inner.astype(jnp.float32))

    conv_rows = 3 * channels // seq_count
    out_rows = channels // seq_count
    conv_all = jnp.concatenate(
        [acc.reshape(seq_count, conv_rows, 2 * channels) for acc in conv_acc], axis=1
    )
    out_all = jnp.concatenate(
        [acc.reshape(seq_count, out_rows, channels) for acc in out_acc], axis=1
    ).reshape(seq_count, depth * out_rows * channels // (2 * channels), 2 * channels)
    (mine,) = halving_scatter([jnp.concatenate([conv_all, out_all], axis=1)], (0, 1, 3, 2, 4))
    conv_grads = mine[: depth * conv_rows].reshape(1, depth, conv_rows, 2 * channels) * grad_scale
    out_grads = mine[depth * conv_rows :].reshape(1, depth, out_rows, channels) * grad_scale
    return (input_grads[None], conv_grads, out_grads)


def solution(mesh):
    return jax.shard_map(
        shards,
        mesh=mesh,
        in_specs=(
            P("section", None, "seq", None),
            P(None, "seq", None),
            P("section", None, None, None, None),
            P("section", None, None, None),
        ),
        out_specs=(
            P("section", None, "seq", None),
            P("section", None, "seq", None),
            P("section", None, "seq", None),
        ),
        check_vma=False,
    )
```
